32 devices in a mesh: grp: 2 (over x), tok: 8 (over z, y), ep: 2 (over core).
Axes of the slice: x: 2, y: 2, z: 4, core: 2. Of those that a mesh axis runs over, the one named last changes fastest.
Arguments:
- tokens: bfloat16 [2, 2048, 768], P('ep', ('grp', 'tok')), parts along dimension 1, may hold values from -6 to 6
- norm_gain: float32 [768], replicated, may hold values from 0.5 to 1.5
- query_weight: bfloat16 [768, 768], replicated, may hold values from -0.21875 to 0.21875
- w_key: bfloat16 [768, 768], replicated, may hold values from -0.21875 to 0.21875
- w_value: bfloat16 [768, 768], replicated, may hold values from -0.21875 to 0.21875
- w_out: bfloat16 [768, 768], replicated, may hold values from -0.21875 to 0.21875
- head_scale: float32 [12], replicated, may hold values from 0.5 to 64
- matching: int32 [2, 64], P('ep', ('grp', 'tok')), parts along dimension 1, may hold values from 0 to 3, as said below
- valid: int32 [2, 64], P('ep', ('grp', 'tok')), parts along dimension 1, may hold values from 1 to 32, as said below
- stops: int32 [2, 16, 4], P('ep', ('grp', 'tok')), parts along dimension 1, may hold values from 0 to 7, as said below
Outputs:
- refined: bfloat16 [2, 2048, 768], P('ep', ('grp', 'tok')), parts along dimension 1
The draws below stay inside these ranges and needn't reach their ends.
There are 2 independent parts, one for each index of `grp`. The reference program is written for one: setup_inputs(seed, part) draws one part's arguments, and reference() takes and returns one part's arrays. A program takes and returns all parts, laid end to end along the dimension named above; an argument that names none is the same for every part. Nothing has to cross between parts.
Inputs may be any that keep to these rules, and one draw needn't show every extreme that they name: `matching`: each aligned group of 4 entries is a permutation of 0 to 3. `valid`: in every block of 4 tiles one tile is full. `stops`: the 4 entries of block t are distinct blocks within 3 of t, and one of them is t - 3 or t + 3.
All inputs are finite; a program needn't handle non-finite values.
Results may differ from the reference program's by a relative error of at most 0.004.
The reference program's roundings to bfloat16 on the way count: a program that leaves them out, or rounds other values in their place, can miss the bound.
Values may be sent and summed in bfloat16 or wider, within the bound.
No kernel may reach another device: no remote copies, remote signals or barrier semaphores. Data moves between devices by JAX's collectives and lax.ppermute only.
A program may use at most 64 MiB of HBM per device.

```python
import math
import jax
import jax.numpy as jnp
from jax import lax

D = 768
H = 12
HD = 64
TOK_DEV = 128
TILE = 32
BAND = 3
STOPS = 4
ROW_PATCHES = 1024
TPD = 4
NBLK = 8
TOKENS = 1024
TILES = 32


def draw_head_scale(key, part):
    base = jnp.exp(jax.random.uniform(key, (H,), jnp.float32, math.log(0.5), math.log(2.0)))
    return base.astype(jnp.float32)


def draw_matching(key, part):
    subkeys = jax.random.split(jax.random.fold_in(key, 11), 2 * NBLK)

    def shuffle(subkey):
        return jax.random.permutation(subkey, TPD)
    orders = jax.vmap(shuffle)(subkeys)
    return orders.reshape(2, TILES).astype(jnp.int32)


def draw_valid(key, part):
    counts = jax.random.randint(jax.random.fold_in(key, 21), (2, NBLK, TPD), 1, TILE + 1)
    full_at = jax.random.randint(jax.random.fold_in(key, 22), (2, NBLK, 1), 0, TPD)
    slots = jnp.arange(TPD, dtype=jnp.int32)[None, None, :]
    counts = jnp.where(slots == full_at, TILE, counts)
    return counts.reshape(2, TILES).astype(jnp.int32)


def draw_stops(key, part):
    width = 2 * BAND + 1
    subkeys = jax.random.split(jax.random.fold_in(key, 31), 2 * NBLK)

    def shuffle(subkey):
        return jax.random.permutation(subkey, width)
    ranks = jax.vmap(shuffle)(subkeys).reshape(2, NBLK, width).astype(jnp.int32)
    blocks = jnp.arange(NBLK, dtype=jnp.int32)[None, :, None]
    offsets = jnp.arange(width, dtype=jnp.int32)[None, None, :] - BAND
    target = blocks + offsets
    inside = (target >= 0) & (target < NBLK)
    slots = jnp.arange(width, dtype=jnp.int32)[None, None, :]
    ranks = jnp.where(inside, ranks, -1 - slots)
    upward = jax.random.randint(jax.random.fold_in(key, 32), (2, NBLK, 1), 0, 2) == 1
    upper_fits = blocks + BAND < NBLK
    lower_fits = blocks - BAND >= 0
    take_upper = upper_fits & (upward | jnp.logical_not(lower_fits))
    forced = jnp.where(take_upper, width - 1, 0)
    ranks = jnp.where(slots == forced, 100, ranks)
    chosen = lax.top_k(ranks, STOPS)[1]
    return jnp.take_along_axis(target, chosen, axis=-1).astype(jnp.int32)


def steps_of(key, extent, cuts, smallest, largest):
    def one(axis_at, parts):
        steps = jax.random.uniform(jax.random.fold_in(jax.random.fold_in(key, 6), axis_at), (parts,), jnp.float32, smallest / len(cuts), largest / len(cuts))
        return jnp.repeat(jnp.exp(steps), extent[axis_at] // parts).reshape((-1,) + (1,) * (len(extent) - axis_at - 1))

    gain = one(*cuts[0])
    for cut in cuts[1:]:
        gain = gain * one(*cut)
    return gain


def normal_values(rng, shape, scale, bound, pieces=(), held_as=jnp.bfloat16):
    factor_of = steps_of(rng, shape, pieces, -0.22, 0.18) if pieces else 1.0
    drawn = jax.random.normal(rng, shape, jnp.float32) * scale * factor_of
    return jnp.minimum(jnp.maximum(drawn, -bound), bound).astype(held_as)


def setup_inputs(seed: int = 0, part: int = 0) -> dict:
    streams_of = jax.random.split(jax.random.key(seed), 11)
    own_keys = jax.random.split(jax.random.fold_in(streams_of[10], part), 11)
    tokens = normal_values(own_keys[0], (2, TOKENS, D), 1.0, 6.0, ((0, 2), (1, 8)))
    norm_gain = jnp.clip(1.0 + 0.1 * jax.random.normal(streams_of[1], (D,), jnp.float32), 0.5, 1.5)
    query_weight = normal_values(streams_of[2], (D, D), D ** -0.5, 0.21875)
    w_key = normal_values(streams_of[3], (D, D), D ** -0.5, 0.21875)
    w_value = normal_values(streams_of[4], (D, D), D ** -0.5, 0.21875)
    w_out = normal_values(streams_of[5], (D, D), D ** -0.5, 0.21875)
    head_scale = draw_head_scale(jax.random.fold_in(streams_of[10], 71), part)
    matching = draw_matching(jax.random.fold_in(jax.random.fold_in(streams_of[10], part), 71), part)
    valid = draw_valid(jax.random.fold_in(jax.random.fold_in(streams_of[10], part), 71), part)
    stops = draw_stops(jax.random.fold_in(jax.random.fold_in(streams_of[10], part), 71), part)
    return {"tokens": tokens, "norm_gain": norm_gain, "query_weight": query_weight, "w_key": w_key, "w_value": w_value, "w_out": w_out, "head_scale": head_scale, "matching": matching, "valid": valid, "stops": stops}


def layer_norm(floated, norm_gain):
    center = lax.optimization_barrier(jnp.mean(floated, axis=-1, keepdims=True))
    spread = lax.optimization_barrier(jnp.mean((floated - center) ** 2, axis=-1, keepdims=True))
    return (floated - center) * lax.rsqrt(spread + 1e-05) * norm_gain

def turn_pairs(part, angle):
    quarter = part.shape[-1] // 2
    first = part[..., :quarter]
    second = part[..., quarter:]
    cosine = jnp.cos(angle)[:, None, :]
    sine = jnp.sin(angle)[:, None, :]
    return jnp.concatenate([first * cosine - second * sine, second * cosine + first * sine], axis=-1)

def rotate(values, patch_coordinates, heads):
    count_rows, width = values.shape
    head_dim = width // heads
    half = head_dim // 2
    quarter = head_dim // 4
    split = values.reshape(count_rows, heads, head_dim)
    row_coordinate = (patch_coordinates // ROW_PATCHES).astype(jnp.float32)
    column_coordinate = (patch_coordinates % ROW_PATCHES).astype(jnp.float32)
    freqs = 100.0 ** (-jnp.arange(quarter, dtype=jnp.float32) / quarter)
    turned = jnp.concatenate([turn_pairs(split[..., :half], row_coordinate[:, None] * freqs[None, :]), turn_pairs(split[..., half:], column_coordinate[:, None] * freqs[None, :])], axis=-1)
    return turned.reshape(count_rows, width)

def reference(tokens, norm_gain, query_weight, w_key, w_value, w_out, head_scale, matching, valid, stops):
    floated = tokens.astype(jnp.float32)
    normed = layer_norm(floated, norm_gain).astype(jnp.bfloat16)
    patch_coordinates = jnp.arange(TOKENS, dtype=jnp.int32)
    scales = head_scale / math.sqrt(HD)
    results = []
    for epoch in range(2):
        source = 1 - epoch
        tile_ids = jnp.arange(TILES, dtype=jnp.int32) // TPD * TPD + matching[epoch]
        key_rows = normed[source].reshape(TILES, TILE, D)[tile_ids].reshape(TOKENS, D)
        counts = valid[source][tile_ids]
        live = (jnp.arange(TILE, dtype=jnp.int32)[None, :] < counts[:, None]).reshape(TOKENS)
        queries = rotate(jnp.dot(normed[epoch], query_weight, preferred_element_type=jnp.float32), patch_coordinates, H).astype(jnp.bfloat16)
        key_proj = rotate(jnp.dot(key_rows, w_key, preferred_element_type=jnp.float32), patch_coordinates, H).astype(jnp.bfloat16)
        value_proj = jnp.dot(key_rows, w_value, preferred_element_type=jnp.float32).astype(jnp.bfloat16)
        key_blocks = key_proj.reshape(NBLK, TOK_DEV, H, HD)
        value_blocks = value_proj.reshape(NBLK, TOK_DEV, H, HD)
        live_blocks = live.reshape(NBLK, TOK_DEV)
        query_blocks = queries.reshape(NBLK, TOK_DEV, H, HD)
        epoch_stops = stops[epoch]

        def one_block(block):
            chosen = epoch_stops[block]
            key_selection = key_blocks[chosen].reshape(STOPS * TOK_DEV, H, HD).astype(jnp.float32)
            value_sel = value_blocks[chosen].reshape(STOPS * TOK_DEV, H, HD).astype(jnp.float32)
            live_sel = live_blocks[chosen].reshape(STOPS * TOK_DEV)
            query_selection = query_blocks[block].astype(jnp.float32)
            scores = jnp.einsum('qhd,khd->hqk', query_selection, key_selection) * scales[:, None, None]
            scores = jnp.where(live_sel[None, None, :], scores, jnp.float32(-1e+30))
            best = lax.optimization_barrier(jnp.max(scores, axis=2, keepdims=True))
            weights = jnp.exp(scores - best)
            total = lax.optimization_barrier(jnp.sum(weights, axis=2))
            summed = jnp.einsum('hqk,khd->qhd', weights.astype(jnp.bfloat16).astype(jnp.float32), value_sel)
            return (summed / jnp.transpose(total)[:, :, None]).reshape(TOK_DEV, D).astype(jnp.bfloat16)
        attended = lax.map(one_block, jnp.arange(NBLK, dtype=jnp.int32)).reshape(TOKENS, D)
        mixed = floated[epoch] + jnp.dot(attended, w_out, preferred_element_type=jnp.float32)
        results.append(mixed.astype(jnp.bfloat16))
    return jnp.stack(results)
```

```python
import math

import jax
import jax.numpy as jnp
from jax import lax
from jax.experimental import pallas as pl
from jax.experimental.pallas import tpu as pltpu
from jax.sharding import PartitionSpec as P

BAND = 3
ROW_PATCHES = 1024
META_ROWS = 8
NEG = -1e30


def partner(block, axis, apart):
    count = lax.axis_size(axis)
    route = []
    for low in range(count):
        high = low | 1 << apart
        if high != low and high < count:
            route += [(low, high), (high, low)]
    return lax.ppermute(block, axis, route)


def from_offset(shard, axis, by):
    size = lax.axis_size(axis)
    pairs = [(i + by, i) for i in range(size) if 0 <= i + by < size]
    return lax.ppermute(shard, axis, pairs)


def layer_norm(floated, norm_gain):
    center = jnp.mean(floated, axis=-1, keepdims=True)
    spread = jnp.mean((floated - center) ** 2, axis=-1, keepdims=True)
    return (floated - center) * lax.rsqrt(spread + 1e-05) * norm_gain


def turn_pairs(part, angle):
    quarter = part.shape[-1] // 2
    first = part[..., :quarter]
    second = part[..., quarter:]
    cosine = jnp.cos(angle)[:, None, :]
    sine = jnp.sin(angle)[:, None, :]
    return jnp.concatenate(
        [first * cosine - second * sine, second * cosine + first * sine], axis=-1
    )


def frequencies(quarter):
    return 100.0 ** (-jnp.arange(quarter, dtype=jnp.float32) / quarter)


def rotate(values, patch_coordinates, heads):
    count_rows, width = values.shape
    head_dim = width // heads
    half = head_dim // 2
    quarter = head_dim // 4
    split = values.reshape(count_rows, heads, head_dim)
    row_coordinate = (patch_coordinates // ROW_PATCHES).astype(jnp.float32)
    column_coordinate = (patch_coordinates % ROW_PATCHES).astype(jnp.float32)
    freqs = frequencies(quarter)
    turned = jnp.concatenate(
        [
            turn_pairs(split[..., :half], row_coordinate[:, None] * freqs[None, :]),
            turn_pairs(split[..., half:], column_coordinate[:, None] * freqs[None, :]),
        ],
        axis=-1,
    )
    return turned.reshape(count_rows, width)


def angle_tables(blocks, count_rows, head_dim):
    half = head_dim // 2
    quarter = head_dim // 4
    lanes = jnp.arange(128, dtype=jnp.int32)
    spots = blocks[:, None] * count_rows + jnp.arange(count_rows, dtype=jnp.int32)[None, :]
    row_coordinate = (spots // ROW_PATCHES).astype(jnp.float32)
    column_coordinate = (spots % ROW_PATCHES).astype(jnp.float32)
    in_row_part = (lanes % head_dim) < half
    coordinate = jnp.where(
        in_row_part[None, None, :], row_coordinate[:, :, None], column_coordinate[:, :, None]
    )
    freq_lane = frequencies(quarter)[lanes % quarter]
    angle = coordinate * freq_lane[None, None, :]
    first = (lanes % half) < quarter
    cosine = jnp.cos(angle)
    sine = jnp.sin(angle)
    signed = jnp.where(first[None, None, :], -sine, sine)
    return cosine, signed


def make_kernel(slots, heads, head_dim, count_rows, width):
    pairs = width // 128
    quarter = head_dim // 4
    per_pair = 128 // head_dim

    def kernel(needed_ref, scale_ref, q_ref, *rest):
        payload_refs = rest[:slots]
        cos_ref, sin_ref, wk_ref, wv_ref, wo_ref, tok_ref, out_ref, acc_ref, m_ref, l_ref = rest[slots:]
        acc_ref[...] = jnp.zeros_like(acc_ref)
        m_ref[...] = jnp.full(m_ref.shape, NEG, jnp.float32)
        l_ref[...] = jnp.zeros_like(l_ref)
        lane = lax.broadcasted_iota(jnp.int32, (count_rows, 128), 1)
        first = (lane % (2 * quarter)) < quarter
        head_of_lane = lane // head_dim

        for slot in range(slots):

            @pl.when(needed_ref[slot] != 0)
            def _():
                pref = payload_refs[slot]
                rows = pref[0:count_rows, :]
                live = pref[count_rows:count_rows + META_ROWS, 0:128].astype(jnp.float32)[0:1, :]
                kp = jnp.dot(rows, wk_ref[...], preferred_element_type=jnp.float32)
                vp = jnp.dot(rows, wv_ref[...], preferred_element_type=jnp.float32).astype(jnp.bfloat16)
                cosine = cos_ref[slot]
                signed = sin_ref[slot]
                for p in range(pairs):
                    lo = p * 128
                    x = kp[:, lo:lo + 128]
                    other = jnp.where(first, pltpu.roll(x, 128 - quarter, 1), pltpu.roll(x, quarter, 1))
                    k_pair = (x * cosine + other * signed).astype(jnp.bfloat16)
                    v_pair = vp[:, lo:lo + 128]
                    q_pair = q_ref[:, lo:lo + 128]
                    acc_pair = acc_ref[:, lo:lo + 128]
                    new_acc = acc_pair
                    for sub in range(per_pair):
                        h = p * per_pair + sub
                        mine = head_of_lane == sub
                        q_h = jnp.where(mine, q_pair, jnp.zeros_like(q_pair))
                        scores = lax.dot_general(
                            q_h, k_pair, (((1,), (1,)), ((), ())),
                            preferred_element_type=jnp.float32,
                        ) * scale_ref[h]
                        scores = jnp.where(live > 0, scores, jnp.float32(NEG))
                        best = m_ref[h]
                        fresh = jnp.maximum(best, jnp.max(scores, axis=1, keepdims=True))
                        decay = jnp.exp(best - fresh)
                        weights = jnp.exp(scores - fresh)
                        l_ref[h] = l_ref[h] * decay + jnp.sum(weights, axis=1, keepdims=True)
                        m_ref[h] = fresh
                        pv = jnp.dot(weights.astype(jnp.bfloat16), v_pair, preferred_element_type=jnp.float32)
                        new_acc = jnp.where(mine, acc_pair * decay + pv, new_acc)
                    acc_ref[:, lo:lo + 128] = new_acc

        parts = []
        for p in range(pairs):
            lo = p * 128
            acc_pair = acc_ref[:, lo:lo + 128]
            res = acc_pair
            for sub in range(per_pair):
                h = p * per_pair + sub
                res = jnp.where(head_of_lane == sub, acc_pair / l_ref[h], res)
            parts.append(res.astype(jnp.bfloat16))
        attended = jnp.concatenate(parts, axis=1)
        mixed = tok_ref[...].astype(jnp.float32) + jnp.dot(
            attended, wo_ref[...], preferred_element_type=jnp.float32
        )
        out_ref[...] = mixed.astype(out_ref.dtype)

    return kernel


def on_device(
    tokens, norm_gain, query_weight, w_key, w_value, w_out, head_scale, matching, valid, stops
):
    floated = tokens[0].astype(jnp.float32)
    count_rows, width = floated.shape
    heads = head_scale.shape[0]
    head_dim = width // heads
    block_index = lax.axis_index("tok")
    normed = layer_norm(floated, norm_gain).astype(jnp.bfloat16)
    row_ids = jnp.arange(count_rows, dtype=jnp.int32)
    patch_coordinates = block_index * count_rows + row_ids
    queries = rotate(
        jnp.dot(normed, query_weight, preferred_element_type=jnp.float32), patch_coordinates, heads
    ).astype(jnp.bfloat16)
    partner_rows, partner_counts = partner((normed, valid[0].astype(jnp.bfloat16)), "ep", 0)
    tile_count = matching.shape[1]
    tile_rows = count_rows // tile_count
    order = matching[0]
    key_rows = partner_rows.reshape(tile_count, tile_rows, width)[order].reshape(count_rows, width)
    counts = partner_counts[order].astype(jnp.float32)
    live = (
        (jnp.arange(tile_rows, dtype=jnp.float32)[None, :] < counts[:, None])
        .reshape(count_rows)
        .astype(jnp.bfloat16)
    )
    meta = jnp.zeros((META_ROWS, width), jnp.bfloat16).at[0, :count_rows].set(live)
    payload = jnp.concatenate([key_rows, meta], axis=0)

    offsets = list(range(-BAND, BAND + 1))
    received = [payload if d == 0 else from_offset(payload, "tok", d) for d in offsets]
    blocks = block_index + jnp.array(offsets, dtype=jnp.int32)
    needed = jnp.any(stops[0, 0][None, :] == blocks[:, None], axis=1).astype(jnp.int32)
    cosine, signed = angle_tables(blocks, count_rows, head_dim)
    scales = (head_scale / math.sqrt(head_dim)).astype(jnp.float32)

    slots = len(offsets)
    smem = pl.BlockSpec(memory_space=pltpu.SMEM)
    vmem = pl.BlockSpec(memory_space=pltpu.VMEM)
    out = pl.pallas_call(
        make_kernel(slots, heads, head_dim, count_rows, width),
        out_shape=jax.ShapeDtypeStruct((count_rows, width), jnp.bfloat16),
        in_specs=[smem, smem] + [vmem] * (1 + slots + 6),
        out_specs=vmem,
        scratch_shapes=[
            pltpu.VMEM((count_rows, width), jnp.float32),
            pltpu.VMEM((heads, count_rows, 1), jnp.float32),
            pltpu.VMEM((heads, count_rows, 1), jnp.float32),
        ],
    )(needed, scales, queries, *received, cosine, signed, w_key, w_value, w_out, tokens[0])
    return out[None]


def solution(mesh):
    in_specs = (
        P("ep", ("grp", "tok"), None),
        P(),
        P(),
        P(),
        P(),
        P(),
        P(),
        P("ep", ("grp", "tok")),
        P("ep", ("grp", "tok")),
        P("ep", ("grp", "tok"), None),
    )
    out_specs = P("ep", ("grp", "tok"), None)
    return jax.shard_map(
        on_device, mesh=mesh, in_specs=in_specs, out_specs=out_specs, check_vma=False
    )
```

```python
import math

import jax
import jax.numpy as jnp
from jax import lax
from jax.experimental import pallas as pl
from jax.experimental.pallas import tpu as pltpu
from jax.sharding import PartitionSpec as P

BAND = 3
ROW_PATCHES = 1024
META_ROWS = 8
NEG = -1e30


def partner(block, axis, apart):
    count = lax.axis_size(axis)
    route = []
    for low in range(count):
        high = low | 1 << apart
        if high != low and high < count:
            route += [(low, high), (high, low)]
    return lax.ppermute(block, axis, route)


def from_offset(shard, axis, by):
    size = lax.axis_size(axis)
    pairs = [(i + by, i) for i in range(size) if 0 <= i + by < size]
    return lax.ppermute(shard, axis, pairs)


def layer_norm(floated, norm_gain):
    center = jnp.mean(floated, axis=-1, keepdims=True)
    spread = jnp.mean((floated - center) ** 2, axis=-1, keepdims=True)
    return (floated - center) * lax.rsqrt(spread + 1e-05) * norm_gain


def turn_pairs(part, angle):
    quarter = part.shape[-1] // 2
    first = part[..., :quarter]
    second = part[..., quarter:]
    cosine = jnp.cos(angle)[:, None, :]
    sine = jnp.sin(angle)[:, None, :]
    return jnp.concatenate(
        [first * cosine - second * sine, second * cosine + first * sine], axis=-1
    )


def frequencies(quarter):
    return 100.0 ** (-jnp.arange(quarter, dtype=jnp.float32) / quarter)


def rotate(values, patch_coordinates, heads):
    count_rows, width = values.shape
    head_dim = width // heads
    half = head_dim // 2
    quarter = head_dim // 4
    split = values.reshape(count_rows, heads, head_dim)
    row_coordinate = (patch_coordinates // ROW_PATCHES).astype(jnp.float32)
    column_coordinate = (patch_coordinates % ROW_PATCHES).astype(jnp.float32)
    freqs = frequencies(quarter)
    turned = jnp.concatenate(
        [
            turn_pairs(split[..., :half], row_coordinate[:, None] * freqs[None, :]),
            turn_pairs(split[..., half:], column_coordinate[:, None] * freqs[None, :]),
        ],
        axis=-1,
    )
    return turned.reshape(count_rows, width)


def angle_tables(blocks, count_rows, head_dim):
    half = head_dim // 2
    quarter = head_dim // 4
    lanes = jnp.arange(128, dtype=jnp.int32)
    spots = blocks[:, None] * count_rows + jnp.arange(count_rows, dtype=jnp.int32)[None, :]
    row_coordinate = (spots // ROW_PATCHES).astype(jnp.float32)
    column_coordinate = (spots % ROW_PATCHES).astype(jnp.float32)
    in_row_part = (lanes % head_dim) < half
    coordinate = jnp.where(
        in_row_part[None, None, :], row_coordinate[:, :, None], column_coordinate[:, :, None]
    )
    freq_lane = jnp.tile(frequencies(quarter), 128 // quarter)
    angle = coordinate * freq_lane[None, None, :]
    first = (lanes % half) < quarter
    cosine = jnp.cos(angle)
    sine = jnp.sin(angle)
    signed = jnp.where(first[None, None, :], -sine, sine)
    return cosine, signed


def make_kernel(slots, heads, head_dim, count_rows, width):
    pairs = width // 128
    quarter = head_dim // 4
    per_pair = 128 // head_dim

    def kernel(needed_ref, scale_ref, q_ref, *rest):
        payload_refs = rest[:slots]
        cos_ref, sin_ref, wk_ref, wv_ref, wo_ref, tok_ref, out_ref, acc_ref, m_ref, l_ref = rest[slots:]
        acc_ref[...] = jnp.zeros_like(acc_ref)
        m_ref[...] = jnp.full(m_ref.shape, NEG, jnp.float32)
        l_ref[...] = jnp.zeros_like(l_ref)
        lane = lax.broadcasted_iota(jnp.int32, (count_rows, 128), 1)
        first = (lane % (2 * quarter)) < quarter
        head_of_lane = lane // head_dim

        for slot in range(slots):

            @pl.when(needed_ref[slot] != 0)
            def _():
                pref = payload_refs[slot]
                rows = pref[0:count_rows, :]
                live = pref[count_rows:count_rows + META_ROWS, 0:128].astype(jnp.float32)[0:1, :]
                kp = jnp.dot(rows, wk_ref[...], preferred_element_type=jnp.float32)
                vp = jnp.dot(rows, wv_ref[...], preferred_element_type=jnp.float32).astype(jnp.bfloat16)
                cosine = cos_ref[slot]
                signed = sin_ref[slot]
                for p in range(pairs):
                    lo = p * 128
                    x = kp[:, lo:lo + 128]
                    other = jnp.where(first, pltpu.roll(x, 128 - quarter, 1), pltpu.roll(x, quarter, 1))
                    k_pair = (x * cosine + other * signed).astype(jnp.bfloat16)
                    v_pair = vp[:, lo:lo + 128]
                    q_pair = q_ref[:, lo:lo + 128]
                    acc_pair = acc_ref[:, lo:lo + 128]
                    new_acc = acc_pair
                    for sub in range(per_pair):
                        h = p * per_pair + sub
                        mine = head_of_lane == sub
                        q_h = jnp.where(mine, q_pair, jnp.zeros_like(q_pair))
                        scores = lax.dot_general(
                            q_h, k_pair, (((1,), (1,)), ((), ())),
                            preferred_element_type=jnp.float32,
                        ) * scale_ref[h]
                        scores = jnp.where(live > 0, scores, jnp.float32(NEG))
                        best = m_ref[h]
                        fresh = jnp.maximum(best, jnp.max(scores, axis=1, keepdims=True))
                        decay = jnp.exp(best - fresh)
                        weights = jnp.exp(scores - fresh)
                        l_ref[h] = l_ref[h] * decay + jnp.sum(weights, axis=1, keepdims=True)
                        m_ref[h] = fresh
                        pv = jnp.dot(weights.astype(jnp.bfloat16), v_pair, preferred_element_type=jnp.float32)
                        new_acc = jnp.where(mine, acc_pair * decay + pv, new_acc)
                    acc_ref[:, lo:lo + 128] = new_acc

        parts = []
        for p in range(pairs):
            lo = p * 128
            acc_pair = acc_ref[:, lo:lo + 128]
            res = acc_pair
            for sub in range(per_pair):
                h = p * per_pair + sub
                res = jnp.where(head_of_lane == sub, acc_pair / l_ref[h], res)
            parts.append(res.astype(jnp.bfloat16))
        attended = jnp.concatenate(parts, axis=1)
        mixed = tok_ref[...].astype(jnp.float32) + jnp.dot(
            attended, wo_ref[...], preferred_element_type=jnp.float32
        )
        out_ref[...] = mixed.astype(out_ref.dtype)

    return kernel


def on_device(
    tokens, norm_gain, query_weight, w_key, w_value, w_out, head_scale, matching, valid, stops
):
    floated = tokens[0].astype(jnp.float32)
    count_rows, width = floated.shape
    heads = head_scale.shape[0]
    head_dim = width // heads
    block_index = lax.axis_index("tok")
    normed = layer_norm(floated, norm_gain).astype(jnp.bfloat16)
    row_ids = jnp.arange(count_rows, dtype=jnp.int32)
    patch_coordinates = block_index * count_rows + row_ids
    queries = rotate(
        jnp.dot(normed, query_weight, preferred_element_type=jnp.float32), patch_coordinates, heads
    ).astype(jnp.bfloat16)
    partner_rows, partner_counts = partner((normed, valid[0].astype(jnp.bfloat16)), "ep", 0)
    tile_count = matching.shape[1]
    tile_rows = count_rows // tile_count
    order = matching[0]
    key_rows = partner_rows.reshape(tile_count, tile_rows, width)[order].reshape(count_rows, width)
    counts = partner_counts[order].astype(jnp.float32)
    live = (
        (jnp.arange(tile_rows, dtype=jnp.float32)[None, :] < counts[:, None])
        .reshape(count_rows)
        .astype(jnp.bfloat16)
    )
    meta = jnp.zeros((META_ROWS, width), jnp.bfloat16).at[0, :count_rows].set(live)
    payload = jnp.concatenate([key_rows, meta], axis=0)

    offsets = list(range(-BAND, BAND + 1))
    received = [payload if d == 0 else from_offset(payload, "tok", d) for d in offsets]
    blocks = block_index + jnp.array(offsets, dtype=jnp.int32)
    needed = jnp.any(stops[0, 0][None, :] == blocks[:, None], axis=1).astype(jnp.int32)
    cosine, signed = angle_tables(blocks, count_rows, head_dim)
    scales = (head_scale / math.sqrt(head_dim)).astype(jnp.float32)

    slots = len(offsets)
    smem = pl.BlockSpec(memory_space=pltpu.SMEM)
    vmem = pl.BlockSpec(memory_space=pltpu.VMEM)
    out = pl.pallas_call(
        make_kernel(slots, heads, head_dim, count_rows, width),
        out_shape=jax.ShapeDtypeStruct((count_rows, width), jnp.bfloat16),
        in_specs=[smem, smem] + [vmem] * (1 + slots + 6),
        out_specs=vmem,
        scratch_shapes=[
            pltpu.VMEM((count_rows, width), jnp.float32),
            pltpu.VMEM((heads, count_rows, 1), jnp.float32),
            pltpu.VMEM((heads, count_rows, 1), jnp.float32),
        ],
    )(needed, scales, queries, *received, cosine, signed, w_key, w_value, w_out, tokens[0])
    return out[None]


def solution(mesh):
    in_specs = (
        P("ep", ("grp", "tok"), None),
        P(),
        P(),
        P(),
        P(),
        P(),
        P(),
        P("ep", ("grp", "tok")),
        P("ep", ("grp", "tok")),
        P("ep", ("grp", "tok"), None),
    )
    out_specs = P("ep", ("grp", "tok"), None)
    return jax.shard_map(
        on_device, mesh=mesh, in_specs=in_specs, out_specs=out_specs, check_vma=False
    )
```

```python
import math

import jax
import jax.numpy as jnp
from jax import lax
from jax.experimental import pallas as pl
from jax.experimental.pallas import tpu as pltpu
from jax.sharding import PartitionSpec as P

BAND = 3
ROW_PATCHES = 1024
META_ROWS = 8
NEG = -1e30


def partner(block, axis, apart):
    count = lax.axis_size(axis)
    route = []
    for low in range(count):
        high = low | 1 << apart
        if high != low and high < count:
            route += [(low, high), (high, low)]
    return lax.ppermute(block, axis, route)


def from_offset(shard, axis, by):
    size = lax.axis_size(axis)
    pairs = [(i + by, i) for i in range(size) if 0 <= i + by < size]
    return lax.ppermute(shard, axis, pairs)


def layer_norm(floated, norm_gain):
    center = jnp.mean(floated, axis=-1, keepdims=True)
    spread = jnp.mean((floated - center) ** 2, axis=-1, keepdims=True)
    return (floated - center) * lax.rsqrt(spread + 1e-05) * norm_gain


def turn_pairs(part, angle):
    quarter = part.shape[-1] // 2
    first = part[..., :quarter]
    second = part[..., quarter:]
    cosine = jnp.cos(angle)[:, None, :]
    sine = jnp.sin(angle)[:, None, :]
    return jnp.concatenate(
        [first * cosine - second * sine, second * cosine + first * sine], axis=-1
    )


def frequencies(quarter):
    return 100.0 ** (-jnp.arange(quarter, dtype=jnp.float32) / quarter)


def rotate(values, patch_coordinates, heads):
    count_rows, width = values.shape
    head_dim = width // heads
    half = head_dim // 2
    quarter = head_dim // 4
    split = values.reshape(count_rows, heads, head_dim)
    row_coordinate = (patch_coordinates // ROW_PATCHES).astype(jnp.float32)
    column_coordinate = (patch_coordinates % ROW_PATCHES).astype(jnp.float32)
    freqs = frequencies(quarter)
    turned = jnp.concatenate(
        [
            turn_pairs(split[..., :half], row_coordinate[:, None] * freqs[None, :]),
            turn_pairs(split[..., half:], column_coordinate[:, None] * freqs[None, :]),
        ],
        axis=-1,
    )
    return turned.reshape(count_rows, width)


def angle_tables(blocks, count_rows, head_dim):
    half = head_dim // 2
    quarter = head_dim // 4
    lanes = jnp.arange(128, dtype=jnp.int32)
    spots = blocks[:, None] * count_rows + jnp.arange(count_rows, dtype=jnp.int32)[None, :]
    row_coordinate = (spots // ROW_PATCHES).astype(jnp.float32)
    column_coordinate = (spots % ROW_PATCHES).astype(jnp.float32)
    in_row_part = (lanes % head_dim) < half
    coordinate = jnp.where(
        in_row_part[None, None, :], row_coordinate[:, :, None], column_coordinate[:, :, None]
    )
    freq_lane = jnp.tile(frequencies(quarter), 128 // quarter)
    angle = coordinate * freq_lane[None, None, :]
    first = (lanes % half) < quarter
    cosine = jnp.cos(angle)
    sine = jnp.sin(angle)
    signed = jnp.where(first[None, None, :], -sine, sine)
    return cosine, signed


def make_slot_kernel(heads, head_dim, count_rows, width):
    pairs = width // 128
    quarter = head_dim // 4
    per_pair = 128 // head_dim

    def kernel(scale_ref, q_ref, pay_ref, cos_ref, sin_ref, wk_ref, wv_ref,
               acc_in, m_in, l_in, acc_out, m_out, l_out):
        lane = lax.broadcasted_iota(jnp.int32, (count_rows, 128), 1)
        first = (lane % (2 * quarter)) < quarter
        head_of_lane = lane // head_dim
        rows = pay_ref[0:count_rows, :]
        live = pay_ref[count_rows:count_rows + META_ROWS, 0:128].astype(jnp.float32)[0:1, :]
        kp = jnp.dot(rows, wk_ref[...], preferred_element_type=jnp.float32)
        vp = jnp.dot(rows, wv_ref[...], preferred_element_type=jnp.float32).astype(jnp.bfloat16)
        cosine = cos_ref[...]
        signed = sin_ref[...]
        m_all = m_in[...]
        l_all = l_in[...]
        m_new = m_all
        l_new = l_all
        for p in range(pairs):
            lo = p * 128
            x = kp[:, lo:lo + 128]
            other = jnp.where(first, pltpu.roll(x, 128 - quarter, 1), pltpu.roll(x, quarter, 1))
            k_pair = (x * cosine + other * signed).astype(jnp.bfloat16)
            v_pair = vp[:, lo:lo + 128]
            q_pair = q_ref[:, lo:lo + 128]
            acc_pair = acc_in[:, lo:lo + 128]
            new_acc = acc_pair
            for sub in range(per_pair):
                h = p * per_pair + sub
                mine = head_of_lane == sub
                at_h = lane == h
                q_h = jnp.where(mine, q_pair, jnp.zeros_like(q_pair))
                scores = lax.dot_general(
                    q_h, k_pair, (((1,), (1,)), ((), ())),
                    preferred_element_type=jnp.float32,
                ) * scale_ref[h]
                scores = jnp.where(live > 0, scores, jnp.float32(NEG))
                best = jnp.max(jnp.where(at_h, m_all, jnp.float32(NEG)), axis=1, keepdims=True)
                total = jnp.sum(jnp.where(at_h, l_all, jnp.float32(0)), axis=1, keepdims=True)
                fresh = jnp.maximum(best, jnp.max(scores, axis=1, keepdims=True))
                decay = jnp.exp(best - fresh)
                weights = jnp.exp(scores - fresh)
                total = total * decay + jnp.sum(weights, axis=1, keepdims=True)
                m_new = jnp.where(at_h, fresh, m_new)
                l_new = jnp.where(at_h, total, l_new)
                pv = jnp.dot(weights.astype(jnp.bfloat16), v_pair, preferred_element_type=jnp.float32)
                new_acc = jnp.where(mine, acc_pair * decay + pv, new_acc)
            acc_out[:, lo:lo + 128] = new_acc
        m_out[...] = m_new
        l_out[...] = l_new

    return kernel


def make_final_kernel(heads, head_dim, count_rows, width):
    pairs = width // 128
    per_pair = 128 // head_dim

    def kernel(acc_ref, l_ref, tok_ref, wo_ref, out_ref):
        lane = lax.broadcasted_iota(jnp.int32, (count_rows, 128), 1)
        head_of_lane = lane // head_dim
        l_all = l_ref[...]
        parts = []
        for p in range(pairs):
            lo = p * 128
            acc_pair = acc_ref[:, lo:lo + 128]
            res = acc_pair
            for sub in range(per_pair):
                h = p * per_pair + sub
                total = jnp.sum(jnp.where(lane == h, l_all, jnp.float32(0)), axis=1, keepdims=True)
                res = jnp.where(head_of_lane == sub, acc_pair / total, res)
            parts.append(res.astype(jnp.bfloat16))
        attended = jnp.concatenate(parts, axis=1)
        mixed = tok_ref[...].astype(jnp.float32) + jnp.dot(
            attended, wo_ref[...], preferred_element_type=jnp.float32
        )
        out_ref[...] = mixed.astype(out_ref.dtype)

    return kernel


def on_device(
    tokens, norm_gain, query_weight, w_key, w_value, w_out, head_scale, matching, valid, stops
):
    floated = tokens[0].astype(jnp.float32)
    count_rows, width = floated.shape
    heads = head_scale.shape[0]
    head_dim = width // heads
    block_index = lax.axis_index("tok")
    normed = layer_norm(floated, norm_gain).astype(jnp.bfloat16)
    row_ids = jnp.arange(count_rows, dtype=jnp.int32)
    patch_coordinates = block_index * count_rows + row_ids
    queries = rotate(
        jnp.dot(normed, query_weight, preferred_element_type=jnp.float32), patch_coordinates, heads
    ).astype(jnp.bfloat16)
    partner_rows, partner_counts = partner((normed, valid[0].astype(jnp.bfloat16)), "ep", 0)
    tile_count = matching.shape[1]
    tile_rows = count_rows // tile_count
    order = matching[0]
    key_rows = partner_rows.reshape(tile_count, tile_rows, width)[order].reshape(count_rows, width)
    counts = partner_counts[order].astype(jnp.float32)
    live = (
        (jnp.arange(tile_rows, dtype=jnp.float32)[None, :] < counts[:, None])
        .reshape(count_rows)
        .astype(jnp.bfloat16)
    )
    meta = jnp.zeros((META_ROWS, width), jnp.bfloat16).at[0, :count_rows].set(live)
    payload = jnp.concatenate([key_rows, meta], axis=0)

    offsets = list(range(-BAND, BAND + 1))
    blocks = block_index + jnp.array(offsets, dtype=jnp.int32)
    needed = jnp.any(stops[0, 0][None, :] == blocks[:, None], axis=1)
    cosine, signed = angle_tables(blocks, count_rows, head_dim)
    scales = (head_scale / math.sqrt(head_dim)).astype(jnp.float32)

    smem = pl.BlockSpec(memory_space=pltpu.SMEM)
    vmem = pl.BlockSpec(memory_space=pltpu.VMEM)
    slot_call = pl.pallas_call(
        make_slot_kernel(heads, head_dim, count_rows, width),
        out_shape=(
            jax.ShapeDtypeStruct((count_rows, width), jnp.float32),
            jax.ShapeDtypeStruct((count_rows, 128), jnp.float32),
            jax.ShapeDtypeStruct((count_rows, 128), jnp.float32),
        ),
        in_specs=[smem] + [vmem] * 9,
        out_specs=(vmem, vmem, vmem),
        input_output_aliases={7: 0, 8: 1, 9: 2},
    )

    def absorb(state, parcel, d):
        slot = offsets.index(d)

        def run(st):
            return slot_call(scales, queries, parcel, cosine[slot], signed[slot], w_key, w_value, *st)

        return lax.cond(needed[slot], run, lambda st: st, state)

    state = (
        jnp.zeros((count_rows, width), jnp.float32),
        jnp.full((count_rows, 128), NEG, jnp.float32),
        jnp.zeros((count_rows, 128), jnp.float32),
    )
    sends = [d for k in range(1, BAND + 1) for d in (k, -k)]
    history = []
    state = absorb(state, payload, 0)
    history.append(state)
    received = {}
    for j, d in enumerate(sends):
        if j >= 2:
            parcel, _ = lax.optimization_barrier((payload, history[j - 1]))
        else:
            parcel = payload
        received[d] = from_offset(parcel, "tok", d)
        if j >= 1:
            prev = sends[j - 1]
            state = absorb(state, received[prev], prev)
            history.append(state)
    state = absorb(state, received[sends[-1]], sends[-1])

    acc, _, l_sum = state
    out = pl.pallas_call(
        make_final_kernel(heads, head_dim, count_rows, width),
        out_shape=jax.ShapeDtypeStruct((count_rows, width), jnp.bfloat16),
        in_specs=[vmem] * 4,
        out_specs=vmem,
    )(acc, l_sum, tokens[0], w_out)
    return out[None]


def solution(mesh):
    in_specs = (
        P("ep", ("grp", "tok"), None),
        P(),
        P(),
        P(),
        P(),
        P(),
        P(),
        P("ep", ("grp", "tok")),
        P("ep", ("grp", "tok")),
        P("ep", ("grp", "tok"), None),
    )
    out_specs = P("ep", ("grp", "tok"), None)
    return jax.shard_map(
        on_device, mesh=mesh, in_specs=in_specs, out_specs=out_specs, check_vma=False
    )
```

```python
import math

import jax
import jax.numpy as jnp
from jax import lax
from jax.experimental import pallas as pl
from jax.experimental.pallas import tpu as pltpu
from jax.sharding import PartitionSpec as P

BAND = 3
ROW_PATCHES = 1024
META_ROWS = 8
NEG = -1e30


def partner(block, axis, apart):
    count = lax.axis_size(axis)
    route = []
    for low in range(count):
        high = low | 1 << apart
        if high != low and high < count:
            route += [(low, high), (high, low)]
    return lax.ppermute(block, axis, route)


def from_offset(shard, axis, by):
    size = lax.axis_size(axis)
    pairs = [(i + by, i) for i in range(size) if 0 <= i + by < size]
    return lax.ppermute(shard, axis, pairs)


def layer_norm(floated, norm_gain):
    center = jnp.mean(floated, axis=-1, keepdims=True)
    spread = jnp.mean((floated - center) ** 2, axis=-1, keepdims=True)
    return (floated - center) * lax.rsqrt(spread + 1e-05) * norm_gain


def turn_pairs(part, angle):
    quarter = part.shape[-1] // 2
    first = part[..., :quarter]
    second = part[..., quarter:]
    cosine = jnp.cos(angle)[:, None, :]
    sine = jnp.sin(angle)[:, None, :]
    return jnp.concatenate(
        [first * cosine - second * sine, second * cosine + first * sine], axis=-1
    )


def frequencies(quarter):
    return 100.0 ** (-jnp.arange(quarter, dtype=jnp.float32) / quarter)


def rotate(values, patch_coordinates, heads):
    count_rows, width = values.shape
    head_dim = width // heads
    half = head_dim // 2
    quarter = head_dim // 4
    split = values.reshape(count_rows, heads, head_dim)
    row_coordinate = (patch_coordinates // ROW_PATCHES).astype(jnp.float32)
    column_coordinate = (patch_coordinates % ROW_PATCHES).astype(jnp.float32)
    freqs = frequencies(quarter)
    turned = jnp.concatenate(
        [
            turn_pairs(split[..., :half], row_coordinate[:, None] * freqs[None, :]),
            turn_pairs(split[..., half:], column_coordinate[:, None] * freqs[None, :]),
        ],
        axis=-1,
    )
    return turned.reshape(count_rows, width)


def angle_tables(blocks, count_rows, head_dim):
    half = head_dim // 2
    quarter = head_dim // 4
    lanes = jnp.arange(128, dtype=jnp.int32)
    spots = blocks[:, None] * count_rows + jnp.arange(count_rows, dtype=jnp.int32)[None, :]
    row_coordinate = (spots // ROW_PATCHES).astype(jnp.float32)
    column_coordinate = (spots % ROW_PATCHES).astype(jnp.float32)
    in_row_part = (lanes % head_dim) < half
    coordinate = jnp.where(
        in_row_part[None, None, :], row_coordinate[:, :, None], column_coordinate[:, :, None]
    )
    freq_lane = jnp.tile(frequencies(quarter), 128 // quarter)
    angle = coordinate * freq_lane[None, None, :]
    first = (lanes % half) < quarter
    cosine = jnp.cos(angle)
    sine = jnp.sin(angle)
    signed = jnp.where(first[None, None, :], -sine, sine)
    return cosine, signed


def attend_slot(scale_ref, q_ref, pay_ref, cos_ref, sin_ref, wk_ref, wv_ref,
                acc_load, m_all, l_all, acc_out, m_out, l_out, heads, head_dim, count_rows, width):
    pairs = width // 128
    quarter = head_dim // 4
    per_pair = 128 // head_dim
    lane = lax.broadcasted_iota(jnp.int32, (count_rows, 128), 1)
    first = (lane % (2 * quarter)) < quarter
    head_of_lane = lane // head_dim
    rows = pay_ref[0:count_rows, :]
    live = pay_ref[count_rows:count_rows + META_ROWS, 0:128].astype(jnp.float32)[0:1, :]
    kp = jnp.dot(rows, wk_ref[...], preferred_element_type=jnp.float32)
    vp = jnp.dot(rows, wv_ref[...], preferred_element_type=jnp.float32).astype(jnp.bfloat16)
    cosine = cos_ref[...]
    signed = sin_ref[...]
    m_new = m_all
    l_new = l_all
    for p in range(pairs):
        lo = p * 128
        x = kp[:, lo:lo + 128]
        other = jnp.where(first, pltpu.roll(x, 128 - quarter, 1), pltpu.roll(x, quarter, 1))
        k_pair = (x * cosine + other * signed).astype(jnp.bfloat16)
        v_pair = vp[:, lo:lo + 128]
        q_pair = q_ref[:, lo:lo + 128]
        acc_pair = acc_load(lo)
        new_acc = acc_pair
        for sub in range(per_pair):
            h = p * per_pair + sub
            mine = head_of_lane == sub
            at_h = lane == h
            q_h = jnp.where(mine, q_pair, jnp.zeros_like(q_pair))
            scores = lax.dot_general(
                q_h, k_pair, (((1,), (1,)), ((), ())),
                preferred_element_type=jnp.float32,
            ) * scale_ref[h]
            scores = jnp.where(live > 0, scores, jnp.float32(NEG))
            best = jnp.max(jnp.where(at_h, m_all, jnp.float32(NEG)), axis=1, keepdims=True)
            total = jnp.sum(jnp.where(at_h, l_all, jnp.float32(0)), axis=1, keepdims=True)
            fresh = jnp.maximum(best, jnp.max(scores, axis=1, keepdims=True))
            decay = jnp.exp(best - fresh)
            weights = jnp.exp(scores - fresh)
            total = total * decay + jnp.sum(weights, axis=1, keepdims=True)
            m_new = jnp.where(at_h, fresh, m_new)
            l_new = jnp.where(at_h, total, l_new)
            pv = jnp.dot(weights.astype(jnp.bfloat16), v_pair, preferred_element_type=jnp.float32)
            new_acc = jnp.where(mine, acc_pair * decay + pv, new_acc)
        acc_out[:, lo:lo + 128] = new_acc
    m_out[...] = m_new
    l_out[...] = l_new


def make_slot_kernel(heads, head_dim, count_rows, width):
    def kernel(scale_ref, q_ref, pay_ref, cos_ref, sin_ref, wk_ref, wv_ref,
               acc_in, m_in, l_in, acc_out, m_out, l_out):
        attend_slot(scale_ref, q_ref, pay_ref, cos_ref, sin_ref, wk_ref, wv_ref,
                    lambda lo: acc_in[:, lo:lo + 128], m_in[...], l_in[...],
                    acc_out, m_out, l_out, heads, head_dim, count_rows, width)

    return kernel


def make_first_kernel(heads, head_dim, count_rows, width):
    def kernel(flag_ref, scale_ref, q_ref, pay_ref, cos_ref, sin_ref, wk_ref, wv_ref,
               acc_out, m_out, l_out):
        @pl.when(flag_ref[0] != 0)
        def _():
            attend_slot(scale_ref, q_ref, pay_ref, cos_ref, sin_ref, wk_ref, wv_ref,
                        lambda lo: jnp.zeros((count_rows, 128), jnp.float32),
                        jnp.full((count_rows, 128), NEG, jnp.float32),
                        jnp.zeros((count_rows, 128), jnp.float32),
                        acc_out, m_out, l_out, heads, head_dim, count_rows, width)

        @pl.when(flag_ref[0] == 0)
        def _():
            acc_out[...] = jnp.zeros_like(acc_out)
            m_out[...] = jnp.full(m_out.shape, NEG, jnp.float32)
            l_out[...] = jnp.zeros_like(l_out)

    return kernel


def norm_kernel(tok_ref, gain_ref, out_ref):
    floated = tok_ref[...].astype(jnp.float32)
    out_ref[...] = layer_norm(floated, gain_ref[...]).astype(out_ref.dtype)


def make_query_kernel(head_dim):
    quarter = head_dim // 4

    def kernel(x_ref, w_ref, cos_ref, sin_ref, out_ref):
        proj = jnp.dot(x_ref[...], w_ref[...], preferred_element_type=jnp.float32)
        lane = lax.broadcasted_iota(jnp.int32, (proj.shape[0], 128), 1)
        first = (lane % (2 * quarter)) < quarter
        cosine = cos_ref[...]
        signed = sin_ref[...]
        for p in range(proj.shape[1] // 128):
            lo = p * 128
            x = proj[:, lo:lo + 128]
            other = jnp.where(first, pltpu.roll(x, 128 - quarter, 1), pltpu.roll(x, quarter, 1))
            out_ref[:, lo:lo + 128] = (x * cosine + other * signed).astype(out_ref.dtype)

    return kernel


def make_payload_kernel(tile_count, tile_rows, count_rows):
    def kernel(order_ref, count_ref, rows_ref, out_ref):
        lane = lax.broadcasted_iota(jnp.int32, (META_ROWS, 128), 1)
        row = lax.broadcasted_iota(jnp.int32, (META_ROWS, 128), 0)
        live = jnp.zeros((META_ROWS, 128), jnp.float32)
        for s in range(tile_count):
            src = order_ref[s]
            start = pl.multiple_of(src * tile_rows, tile_rows)
            out_ref[s * tile_rows:(s + 1) * tile_rows, :] = rows_ref[pl.ds(start, tile_rows), :]
            inside = (lane // tile_rows == s) & ((lane % tile_rows) < count_ref[src]) & (row == 0)
            live = jnp.where(inside, jnp.float32(1), live)
        out_ref[count_rows:count_rows + META_ROWS, :] = jnp.zeros(
            (META_ROWS, out_ref.shape[1]), out_ref.dtype)
        out_ref[count_rows:count_rows + META_ROWS, 0:128] = live.astype(out_ref.dtype)

    return kernel


def make_final_kernel(heads, head_dim, count_rows, width):
    pairs = width // 128
    per_pair = 128 // head_dim

    def kernel(acc_ref, l_ref, tok_ref, wo_ref, out_ref):
        lane = lax.broadcasted_iota(jnp.int32, (count_rows, 128), 1)
        head_of_lane = lane // head_dim
        l_all = l_ref[...]
        parts = []
        for p in range(pairs):
            lo = p * 128
            acc_pair = acc_ref[:, lo:lo + 128]
            res = acc_pair
            for sub in range(per_pair):
                h = p * per_pair + sub
                total = jnp.sum(jnp.where(lane == h, l_all, jnp.float32(0)), axis=1, keepdims=True)
                res = jnp.where(head_of_lane == sub, acc_pair / total, res)
            parts.append(res.astype(jnp.bfloat16))
        attended = jnp.concatenate(parts, axis=1)
        mixed = tok_ref[...].astype(jnp.float32) + jnp.dot(
            attended, wo_ref[...], preferred_element_type=jnp.float32
        )
        out_ref[...] = mixed.astype(out_ref.dtype)

    return kernel


def full_spec(shape):
    return pl.BlockSpec(shape, lambda i: (0,) * len(shape))


def on_device(
    tokens, norm_gain, query_weight, w_key, w_value, w_out, head_scale, matching, valid, stops
):
    count_rows, width = tokens.shape[1:]
    heads = head_scale.shape[0]
    head_dim = width // heads
    block_index = lax.axis_index("tok")
    smem = pl.BlockSpec(memory_space=pltpu.SMEM)
    vmem = pl.BlockSpec(memory_space=pltpu.VMEM)
    normed = pl.pallas_call(
        norm_kernel,
        out_shape=jax.ShapeDtypeStruct((count_rows, width), jnp.bfloat16),
        in_specs=[vmem, vmem],
        out_specs=vmem,
    )(tokens[0], norm_gain.reshape(1, width))
    partner_rows, partner_counts = partner((normed, valid[0]), "ep", 0)
    tile_count = matching.shape[1]
    tile_rows = count_rows // tile_count
    payload = pl.pallas_call(
        make_payload_kernel(tile_count, tile_rows, count_rows),
        out_shape=jax.ShapeDtypeStruct((count_rows + META_ROWS, width), jnp.bfloat16),
        in_specs=[smem, smem, vmem],
        out_specs=vmem,
    )(matching[0], partner_counts, partner_rows)

    offsets = list(range(-BAND, BAND + 1))
    blocks = block_index + jnp.array(offsets, dtype=jnp.int32)
    needed = jnp.any(stops[0, 0][None, :] == blocks[:, None], axis=1)
    cosine, signed = angle_tables(blocks, count_rows, head_dim)
    scales = (head_scale / math.sqrt(head_dim)).astype(jnp.float32)
    own = offsets.index(0)
    table_spec = pl.BlockSpec((None, count_rows, 128), lambda i: (own, 0, 0))

    queries = pl.pallas_call(
        make_query_kernel(head_dim),
        out_shape=jax.ShapeDtypeStruct((count_rows, width), jnp.bfloat16),
        grid=(1,),
        in_specs=[full_spec((count_rows, width)), full_spec((width, width)), table_spec, table_spec],
        out_specs=full_spec((count_rows, width)),
    )(normed, query_weight, cosine, signed)

    state_shapes = (
        jax.ShapeDtypeStruct((count_rows, width), jnp.float32),
        jax.ShapeDtypeStruct((count_rows, 128), jnp.float32),
        jax.ShapeDtypeStruct((count_rows, 128), jnp.float32),
    )
    state_specs = (full_spec((count_rows, width)), full_spec((count_rows, 128)),
                   full_spec((count_rows, 128)))

    def common_specs(slot):
        spec = pl.BlockSpec((None, count_rows, 128), lambda i: (slot, 0, 0))
        return [smem, full_spec((count_rows, width)), full_spec((count_rows + META_ROWS, width)),
                spec, spec, full_spec((width, width)), full_spec((width, width))]

    state = pl.pallas_call(
        make_first_kernel(heads, head_dim, count_rows, width),
        out_shape=state_shapes,
        grid=(1,),
        in_specs=[smem] + common_specs(own),
        out_specs=state_specs,
    )(needed[own:own + 1].astype(jnp.int32), scales, queries, payload, cosine, signed, w_key, w_value)

    def absorb(state, parcel, d):
        slot = offsets.index(d)
        call = pl.pallas_call(
            make_slot_kernel(heads, head_dim, count_rows, width),
            out_shape=state_shapes,
            grid=(1,),
            in_specs=common_specs(slot) + list(state_specs),
            out_specs=state_specs,
            input_output_aliases={7: 0, 8: 1, 9: 2},
        )

        def run(st):
            return call(scales, queries, parcel, cosine, signed, w_key, w_value, *st)

        return lax.cond(needed[slot], run, lambda st: st, state)

    sends = [d for k in range(1, BAND + 1) for d in (k, -k)]
    history = [state]
    received = {}
    for j, d in enumerate(sends):
        if j >= 1:
            parcel, _ = lax.optimization_barrier((payload, history[j - 1]))
        else:
            parcel = payload
        received[d] = from_offset(parcel, "tok", d)
        if j >= 1:
            prev = sends[j - 1]
            state = absorb(state, received[prev], prev)
            history.append(state)
    state = absorb(state, received[sends[-1]], sends[-1])

    acc, _, l_sum = state
    out = pl.pallas_call(
        make_final_kernel(heads, head_dim, count_rows, width),
        out_shape=jax.ShapeDtypeStruct((count_rows, width), jnp.bfloat16),
        in_specs=[vmem] * 4,
        out_specs=vmem,
    )(acc, l_sum, tokens[0], w_out)
    return out[None]


def solution(mesh):
    in_specs = (
        P("ep", ("grp", "tok"), None),
        P(),
        P(),
        P(),
        P(),
        P(),
        P(),
        P("ep", ("grp", "tok")),
        P("ep", ("grp", "tok")),
        P("ep", ("grp", "tok"), None),
    )
    out_specs = P("ep", ("grp", "tok"), None)
    return jax.shard_map(
        on_device, mesh=mesh, in_specs=in_specs, out_specs=out_specs, check_vma=False
    )
```

```python
import math

import jax
import jax.numpy as jnp
from jax import lax
from jax.experimental import pallas as pl
from jax.experimental.pallas import tpu as pltpu
from jax.sharding import PartitionSpec as P

BAND = 3
ROW_PATCHES = 1024
META_ROWS = 8
NEG = -1e30


def partner(block, axis, apart):
    count = lax.axis_size(axis)
    route = []
    for low in range(count):
        high = low | 1 << apart
        if high != low and high < count:
            route += [(low, high), (high, low)]
    return lax.ppermute(block, axis, route)


def from_offset(shard, axis, by):
    size = lax.axis_size(axis)
    pairs = [(i + by, i) for i in range(size) if 0 <= i + by < size]
    return lax.ppermute(shard, axis, pairs)


def layer_norm(floated, norm_gain):
    center = jnp.mean(floated, axis=-1, keepdims=True)
    spread = jnp.mean((floated - center) ** 2, axis=-1, keepdims=True)
    return (floated - center) * lax.rsqrt(spread + 1e-05) * norm_gain


def turn_pairs(part, angle):
    quarter = part.shape[-1] // 2
    first = part[..., :quarter]
    second = part[..., quarter:]
    cosine = jnp.cos(angle)[:, None, :]
    sine = jnp.sin(angle)[:, None, :]
    return jnp.concatenate(
        [first * cosine - second * sine, second * cosine + first * sine], axis=-1
    )


def frequencies(quarter):
    return 100.0 ** (-jnp.arange(quarter, dtype=jnp.float32) / quarter)


def rotate(values, patch_coordinates, heads):
    count_rows, width = values.shape
    head_dim = width // heads
    half = head_dim // 2
    quarter = head_dim // 4
    split = values.reshape(count_rows, heads, head_dim)
    row_coordinate = (patch_coordinates // ROW_PATCHES).astype(jnp.float32)
    column_coordinate = (patch_coordinates % ROW_PATCHES).astype(jnp.float32)
    freqs = frequencies(quarter)
    turned = jnp.concatenate(
        [
            turn_pairs(split[..., :half], row_coordinate[:, None] * freqs[None, :]),
            turn_pairs(split[..., half:], column_coordinate[:, None] * freqs[None, :]),
        ],
        axis=-1,
    )
    return turned.reshape(count_rows, width)


def angle_tables(blocks, count_rows, head_dim):
    half = head_dim // 2
    quarter = head_dim // 4
    lanes = jnp.arange(128, dtype=jnp.int32)
    spots = blocks[:, None] * count_rows + jnp.arange(count_rows, dtype=jnp.int32)[None, :]
    row_coordinate = (spots // ROW_PATCHES).astype(jnp.float32)
    column_coordinate = (spots % ROW_PATCHES).astype(jnp.float32)
    in_row_part = (lanes % head_dim) < half
    coordinate = jnp.where(
        in_row_part[None, None, :], row_coordinate[:, :, None], column_coordinate[:, :, None]
    )
    freq_lane = jnp.tile(frequencies(quarter), 128 // quarter)
    angle = coordinate * freq_lane[None, None, :]
    first = (lanes % half) < quarter
    cosine = jnp.cos(angle)
    sine = jnp.sin(angle)
    signed = jnp.where(first[None, None, :], -sine, sine)
    return cosine, signed


def attend_slot(scale_ref, q_ref, pay_ref, cos_ref, sin_ref, wk_ref, wv_ref,
                acc_load, m_all, l_all, acc_out, m_out, l_out, heads, head_dim, count_rows, width):
    pairs = width // 128
    quarter = head_dim // 4
    per_pair = 128 // head_dim
    lane = lax.broadcasted_iota(jnp.int32, (count_rows, 128), 1)
    first = (lane % (2 * quarter)) < quarter
    head_of_lane = lane // head_dim
    rows = pay_ref[0:count_rows, :]
    live = pay_ref[count_rows:count_rows + META_ROWS, 0:128].astype(jnp.float32)[0:1, :]
    kp = jnp.dot(rows, wk_ref[...], preferred_element_type=jnp.float32)
    vp = jnp.dot(rows, wv_ref[...], preferred_element_type=jnp.float32).astype(jnp.bfloat16)
    cosine = cos_ref[...]
    signed = sin_ref[...]
    m_new = m_all
    l_new = l_all
    for p in range(pairs):
        lo = p * 128
        x = kp[:, lo:lo + 128]
        other = jnp.where(first, pltpu.roll(x, 128 - quarter, 1), pltpu.roll(x, quarter, 1))
        k_pair = (x * cosine + other * signed).astype(jnp.bfloat16)
        v_pair = vp[:, lo:lo + 128]
        q_pair = q_ref[:, lo:lo + 128]
        acc_pair = acc_load(lo)
        new_acc = acc_pair
        for sub in range(per_pair):
            h = p * per_pair + sub
            mine = head_of_lane == sub
            at_h = lane == h
            q_h = jnp.where(mine, q_pair, jnp.zeros_like(q_pair))
            scores = lax.dot_general(
                q_h, k_pair, (((1,), (1,)), ((), ())),
                preferred_element_type=jnp.float32,
            ) * scale_ref[h]
            scores = jnp.where(live > 0, scores, jnp.float32(NEG))
            best = jnp.max(jnp.where(at_h, m_all, jnp.float32(NEG)), axis=1, keepdims=True)
            total = jnp.sum(jnp.where(at_h, l_all, jnp.float32(0)), axis=1, keepdims=True)
            fresh = jnp.maximum(best, jnp.max(scores, axis=1, keepdims=True))
            decay = jnp.exp(best - fresh)
            weights = jnp.exp(scores - fresh)
            total = total * decay + jnp.sum(weights, axis=1, keepdims=True)
            m_new = jnp.where(at_h, fresh, m_new)
            l_new = jnp.where(at_h, total, l_new)
            pv = jnp.dot(weights.astype(jnp.bfloat16), v_pair, preferred_element_type=jnp.float32)
            new_acc = jnp.where(mine, acc_pair * decay + pv, new_acc)
        acc_out[:, lo:lo + 128] = new_acc
    m_out[...] = m_new
    l_out[...] = l_new


def make_slot_kernel(heads, head_dim, count_rows, width):
    def kernel(scale_ref, q_ref, pay_ref, cos_ref, sin_ref, wk_ref, wv_ref,
               acc_in, m_in, l_in, acc_out, m_out, l_out):
        attend_slot(scale_ref, q_ref, pay_ref, cos_ref, sin_ref, wk_ref, wv_ref,
                    lambda lo: acc_in[:, lo:lo + 128], m_in[...], l_in[...],
                    acc_out, m_out, l_out, heads, head_dim, count_rows, width)

    return kernel


def make_first_kernel(heads, head_dim, count_rows, width):
    def kernel(flag_ref, scale_ref, q_ref, pay_ref, cos_ref, sin_ref, wk_ref, wv_ref,
               acc_out, m_out, l_out):
        @pl.when(flag_ref[0] != 0)
        def _():
            attend_slot(scale_ref, q_ref, pay_ref, cos_ref, sin_ref, wk_ref, wv_ref,
                        lambda lo: jnp.zeros((count_rows, 128), jnp.float32),
                        jnp.full((count_rows, 128), NEG, jnp.float32),
                        jnp.zeros((count_rows, 128), jnp.float32),
                        acc_out, m_out, l_out, heads, head_dim, count_rows, width)

        @pl.when(flag_ref[0] == 0)
        def _():
            acc_out[...] = jnp.zeros_like(acc_out)
            m_out[...] = jnp.full(m_out.shape, NEG, jnp.float32)
            l_out[...] = jnp.zeros_like(l_out)

    return kernel


def norm_kernel(tok_ref, gain_ref, out_ref):
    floated = tok_ref[...].astype(jnp.float32)
    out_ref[...] = layer_norm(floated, gain_ref[...]).astype(out_ref.dtype)


def make_query_kernel(head_dim):
    quarter = head_dim // 4

    def kernel(x_ref, w_ref, cos_ref, sin_ref, out_ref):
        proj = jnp.dot(x_ref[...], w_ref[...], preferred_element_type=jnp.float32)
        lane = lax.broadcasted_iota(jnp.int32, (proj.shape[0], 128), 1)
        first = (lane % (2 * quarter)) < quarter
        cosine = cos_ref[...]
        signed = sin_ref[...]
        for p in range(proj.shape[1] // 128):
            lo = p * 128
            x = proj[:, lo:lo + 128]
            other = jnp.where(first, pltpu.roll(x, 128 - quarter, 1), pltpu.roll(x, quarter, 1))
            out_ref[:, lo:lo + 128] = (x * cosine + other * signed).astype(out_ref.dtype)

    return kernel


def make_payload_kernel(tile_count, tile_rows, count_rows):
    def kernel(order_ref, count_ref, rows_ref, out_ref):
        lane = lax.broadcasted_iota(jnp.int32, (META_ROWS, 128), 1)
        row = lax.broadcasted_iota(jnp.int32, (META_ROWS, 128), 0)
        live = jnp.zeros((META_ROWS, 128), jnp.float32)
        for s in range(tile_count):
            src = order_ref[s]
            start = pl.multiple_of(src * tile_rows, tile_rows)
            out_ref[s * tile_rows:(s + 1) * tile_rows, :] = rows_ref[pl.ds(start, tile_rows), :]
            inside = (lane // tile_rows == s) & ((lane % tile_rows) < count_ref[src]) & (row == 0)
            live = jnp.where(inside, jnp.float32(1), live)
        out_ref[count_rows:count_rows + META_ROWS, :] = jnp.zeros(
            (META_ROWS, out_ref.shape[1]), out_ref.dtype)
        out_ref[count_rows:count_rows + META_ROWS, 0:128] = live.astype(out_ref.dtype)

    return kernel


def make_band_kernel(slots, heads, head_dim, count_rows, width):
    pairs = width // 128
    quarter = head_dim // 4
    per_pair = 128 // head_dim
    stacked = per_pair * count_rows

    def kernel(needed_ref, scale_ref, q_ref, *rest):
        payload_refs = rest[:slots]
        cos_ref, sin_ref, wk_ref, wv_ref, wo_ref, tok_ref, out_ref, acc_ref, m_ref, l_ref = rest[slots:]
        acc_ref[...] = jnp.zeros_like(acc_ref)
        m_ref[...] = jnp.full(m_ref.shape, NEG, jnp.float32)
        l_ref[...] = jnp.zeros_like(l_ref)
        lane = lax.broadcasted_iota(jnp.int32, (count_rows, 128), 1)
        first = (lane % (2 * quarter)) < quarter
        head_of_lane = lane // head_dim
        row = lax.broadcasted_iota(jnp.int32, (stacked, 1), 0)

        for slot in range(slots):

            @pl.when(needed_ref[slot] != 0)
            def _():
                pref = payload_refs[slot]
                rows = pref[0:count_rows, :]
                live = pref[count_rows:count_rows + META_ROWS, 0:128].astype(jnp.float32)[0:1, :]
                kp = jnp.dot(rows, wk_ref[...], preferred_element_type=jnp.float32)
                vp = jnp.dot(rows, wv_ref[...], preferred_element_type=jnp.float32).astype(jnp.bfloat16)
                cosine = cos_ref[slot]
                signed = sin_ref[slot]
                for p in range(pairs):
                    lo = p * 128
                    x = kp[:, lo:lo + 128]
                    other = jnp.where(first, pltpu.roll(x, 128 - quarter, 1), pltpu.roll(x, quarter, 1))
                    k_pair = (x * cosine + other * signed).astype(jnp.bfloat16)
                    v_pair = vp[:, lo:lo + 128]
                    q_pair = q_ref[:, lo:lo + 128]
                    q_two = jnp.concatenate(
                        [jnp.where(head_of_lane == sub, q_pair, jnp.zeros_like(q_pair))
                         for sub in range(per_pair)], axis=0)
                    scale_col = jnp.zeros((stacked, 1), jnp.float32)
                    for sub in range(per_pair):
                        scale_col = jnp.where(row // count_rows == sub, scale_ref[p * per_pair + sub], scale_col)
                    scores = lax.dot_general(
                        q_two, k_pair, (((1,), (1,)), ((), ())),
                        preferred_element_type=jnp.float32,
                    ) * scale_col
                    scores = jnp.where(live > 0, scores, jnp.float32(NEG))
                    best = m_ref[p]
                    fresh = jnp.maximum(best, jnp.max(scores, axis=1, keepdims=True))
                    decay = jnp.exp(best - fresh)
                    weights = jnp.exp(scores - fresh)
                    l_ref[p] = l_ref[p] * decay + jnp.sum(weights, axis=1, keepdims=True)
                    m_ref[p] = fresh
                    pv = jnp.dot(weights.astype(jnp.bfloat16), v_pair, preferred_element_type=jnp.float32)
                    acc_ref[p] = acc_ref[p] * decay + pv

        parts = []
        for p in range(pairs):
            acc_two = acc_ref[p] / l_ref[p]
            res = acc_two[0:count_rows]
            for sub in range(1, per_pair):
                res = jnp.where(head_of_lane == sub, acc_two[sub * count_rows:(sub + 1) * count_rows], res)
            parts.append(res.astype(jnp.bfloat16))
        attended = jnp.concatenate(parts, axis=1)
        mixed = tok_ref[...].astype(jnp.float32) + jnp.dot(
            attended, wo_ref[...], preferred_element_type=jnp.float32
        )
        out_ref[...] = mixed.astype(out_ref.dtype)

    return kernel


def norm_kernel(tok_ref, gain_ref, out_ref):
    floated = tok_ref[...].astype(jnp.float32)
    out_ref[...] = layer_norm(floated, gain_ref[...]).astype(out_ref.dtype)


def make_query_kernel(head_dim):
    quarter = head_dim // 4

    def kernel(x_ref, w_ref, cos_ref, sin_ref, out_ref):
        proj = jnp.dot(x_ref[...], w_ref[...], preferred_element_type=jnp.float32)
        lane = lax.broadcasted_iota(jnp.int32, (proj.shape[0], 128), 1)
        first = (lane % (2 * quarter)) < quarter
        cosine = cos_ref[...]
        signed = sin_ref[...]
        for p in range(proj.shape[1] // 128):
            lo = p * 128
            x = proj[:, lo:lo + 128]
            other = jnp.where(first, pltpu.roll(x, 128 - quarter, 1), pltpu.roll(x, quarter, 1))
            out_ref[:, lo:lo + 128] = (x * cosine + other * signed).astype(out_ref.dtype)

    return kernel


def make_payload_kernel(tile_count, tile_rows, count_rows):
    def kernel(order_ref, count_ref, rows_ref, out_ref):
        lane = lax.broadcasted_iota(jnp.int32, (META_ROWS, 128), 1)
        row = lax.broadcasted_iota(jnp.int32, (META_ROWS, 128), 0)
        live = jnp.zeros((META_ROWS, 128), jnp.float32)
        for s in range(tile_count):
            src = order_ref[s]
            start = pl.multiple_of(src * tile_rows, tile_rows)
            out_ref[s * tile_rows:(s + 1) * tile_rows, :] = rows_ref[pl.ds(start, tile_rows), :]
            inside = (lane // tile_rows == s) & ((lane % tile_rows) < count_ref[src]) & (row == 0)
            live = jnp.where(inside, jnp.float32(1), live)
        out_ref[count_rows:count_rows + META_ROWS, :] = jnp.zeros(
            (META_ROWS, out_ref.shape[1]), out_ref.dtype)
        out_ref[count_rows:count_rows + META_ROWS, 0:128] = live.astype(out_ref.dtype)

    return kernel


def make_final_kernel(heads, head_dim, count_rows, width):
    pairs = width // 128
    per_pair = 128 // head_dim

    def kernel(acc_ref, l_ref, tok_ref, wo_ref, out_ref):
        lane = lax.broadcasted_iota(jnp.int32, (count_rows, 128), 1)
        head_of_lane = lane // head_dim
        l_all = l_ref[...]
        parts = []
        for p in range(pairs):
            lo = p * 128
            acc_pair = acc_ref[:, lo:lo + 128]
            res = acc_pair
            for sub in range(per_pair):
                h = p * per_pair + sub
                total = jnp.sum(jnp.where(lane == h, l_all, jnp.float32(0)), axis=1, keepdims=True)
                res = jnp.where(head_of_lane == sub, acc_pair / total, res)
            parts.append(res.astype(jnp.bfloat16))
        attended = jnp.concatenate(parts, axis=1)
        mixed = tok_ref[...].astype(jnp.float32) + jnp.dot(
            attended, wo_ref[...], preferred_element_type=jnp.float32
        )
        out_ref[...] = mixed.astype(out_ref.dtype)

    return kernel


def full_spec(shape):
    return pl.BlockSpec(shape, lambda i: (0,) * len(shape))


def on_device(
    tokens, norm_gain, query_weight, w_key, w_value, w_out, head_scale, matching, valid, stops
):
    count_rows, width = tokens.shape[1:]
    heads = head_scale.shape[0]
    head_dim = width // heads
    block_index = lax.axis_index("tok")
    smem = pl.BlockSpec(memory_space=pltpu.SMEM)
    vmem = pl.BlockSpec(memory_space=pltpu.VMEM)
    normed = pl.pallas_call(
        norm_kernel,
        out_shape=jax.ShapeDtypeStruct((count_rows, width), jnp.bfloat16),
        in_specs=[vmem, vmem],
        out_specs=vmem,
    )(tokens[0], norm_gain.reshape(1, width))
    partner_rows, partner_counts = partner((normed, valid[0]), "ep", 0)
    tile_count = matching.shape[1]
    tile_rows = count_rows // tile_count
    payload = pl.pallas_call(
        make_payload_kernel(tile_count, tile_rows, count_rows),
        out_shape=jax.ShapeDtypeStruct((count_rows + META_ROWS, width), jnp.bfloat16),
        in_specs=[smem, smem, vmem],
        out_specs=vmem,
    )(matching[0], partner_counts, partner_rows)

    offsets = list(range(-BAND, BAND + 1))
    blocks = block_index + jnp.array(offsets, dtype=jnp.int32)
    needed = jnp.any(stops[0, 0][None, :] == blocks[:, None], axis=1)
    cosine, signed = angle_tables(blocks, count_rows, head_dim)
    scales = (head_scale / math.sqrt(head_dim)).astype(jnp.float32)
    own = offsets.index(0)
    table_spec = pl.BlockSpec((None, count_rows, 128), lambda i: (own, 0, 0))

    queries = pl.pallas_call(
        make_query_kernel(head_dim),
        out_shape=jax.ShapeDtypeStruct((count_rows, width), jnp.bfloat16),
        grid=(1,),
        in_specs=[full_spec((count_rows, width)), full_spec((width, width)), table_spec, table_spec],
        out_specs=full_spec((count_rows, width)),
    )(normed, query_weight, cosine, signed)

    slots = len(offsets)
    received = [payload if d == 0 else from_offset(payload, "tok", d) for d in offsets]
    pairs = width // 128
    stacked = (128 // head_dim) * count_rows
    out = pl.pallas_call(
        make_band_kernel(slots, heads, head_dim, count_rows, width),
        out_shape=jax.ShapeDtypeStruct((count_rows, width), jnp.bfloat16),
        in_specs=[smem, smem] + [vmem] * (1 + slots + 6),
        out_specs=vmem,
        scratch_shapes=[
            pltpu.VMEM((pairs, stacked, 128), jnp.float32),
            pltpu.VMEM((pairs, stacked, 1), jnp.float32),
            pltpu.VMEM((pairs, stacked, 1), jnp.float32),
        ],
    )(needed.astype(jnp.int32), scales, queries, *received, cosine, signed, w_key, w_value, w_out,
      tokens[0])
    return out[None]


def solution(mesh):
    in_specs = (
        P("ep", ("grp", "tok"), None),
        P(),
        P(),
        P(),
        P(),
        P(),
        P(),
        P("ep", ("grp", "tok")),
        P("ep", ("grp", "tok")),
        P("ep", ("grp", "tok"), None),
    )
    out_specs = P("ep", ("grp", "tok"), None)
    return jax.shard_map(
        on_device, mesh=mesh, in_specs=in_specs, out_specs=out_specs, check_vma=False
    )
```

```python
import math

import jax
import jax.numpy as jnp
from jax import lax
from jax.experimental import pallas as pl
from jax.experimental.pallas import tpu as pltpu
from jax.sharding import PartitionSpec as P

BAND = 3
ROW_PATCHES = 1024
META_ROWS = 8
NEG = -1e30


def partner(block, axis, apart):
    count = lax.axis_size(axis)
    route = []
    for low in range(count):
        high = low | 1 << apart
        if high != low and high < count:
            route += [(low, high), (high, low)]
    return lax.ppermute(block, axis, route)


def layer_norm(floated, norm_gain):
    center = jnp.mean(floated, axis=-1, keepdims=True)
    spread = jnp.mean((floated - center) ** 2, axis=-1, keepdims=True)
    return (floated - center) * lax.rsqrt(spread + 1e-05) * norm_gain


def turn_pairs(part, angle):
    quarter = part.shape[-1] // 2
    first = part[..., :quarter]
    second = part[..., quarter:]
    cosine = jnp.cos(angle)[:, None, :]
    sine = jnp.sin(angle)[:, None, :]
    return jnp.concatenate(
        [first * cosine - second * sine, second * cosine + first * sine], axis=-1
    )


def frequencies(quarter):
    return 100.0 ** (-jnp.arange(quarter, dtype=jnp.float32) / quarter)


def rotate(values, patch_coordinates, heads):
    count_rows, width = values.shape
    head_dim = width // heads
    half = head_dim // 2
    quarter = head_dim // 4
    split = values.reshape(count_rows, heads, head_dim)
    row_coordinate = (patch_coordinates // ROW_PATCHES).astype(jnp.float32)
    column_coordinate = (patch_coordinates % ROW_PATCHES).astype(jnp.float32)
    freqs = frequencies(quarter)
    turned = jnp.concatenate(
        [
            turn_pairs(split[..., :half], row_coordinate[:, None] * freqs[None, :]),
            turn_pairs(split[..., half:], column_coordinate[:, None] * freqs[None, :]),
        ],
        axis=-1,
    )
    return turned.reshape(count_rows, width)


def angle_tables(blocks, count_rows, head_dim):
    half = head_dim // 2
    quarter = head_dim // 4
    lanes = jnp.arange(128, dtype=jnp.int32)
    spots = blocks[:, None] * count_rows + jnp.arange(count_rows, dtype=jnp.int32)[None, :]
    row_coordinate = (spots // ROW_PATCHES).astype(jnp.float32)
    column_coordinate = (spots % ROW_PATCHES).astype(jnp.float32)
    in_row_part = (lanes % head_dim) < half
    coordinate = jnp.where(
        in_row_part[None, None, :], row_coordinate[:, :, None], column_coordinate[:, :, None]
    )
    freq_lane = jnp.tile(frequencies(quarter), 128 // quarter)
    angle = coordinate * freq_lane[None, None, :]
    first = (lanes % half) < quarter
    cosine = jnp.cos(angle)
    sine = jnp.sin(angle)
    signed = jnp.where(first[None, None, :], -sine, sine)
    return cosine, signed


def make_band_kernel(slots, heads, head_dim, count_rows, width):
    pairs = width // 128
    quarter = head_dim // 4
    per_pair = 128 // head_dim
    stacked = per_pair * count_rows

    def kernel(needed_ref, scale_ref, q_ref, *rest):
        payload_refs = rest[:slots]
        cos_ref, sin_ref, wk_ref, wv_ref, wo_ref, tok_ref, out_ref, acc_ref, m_ref, l_ref = rest[slots:]
        acc_ref[...] = jnp.zeros_like(acc_ref)
        m_ref[...] = jnp.full(m_ref.shape, NEG, jnp.float32)
        l_ref[...] = jnp.zeros_like(l_ref)
        lane = lax.broadcasted_iota(jnp.int32, (count_rows, 128), 1)
        first = (lane % (2 * quarter)) < quarter
        head_of_lane = lane // head_dim
        row = lax.broadcasted_iota(jnp.int32, (stacked, 1), 0)

        for slot in range(slots):

            @pl.when(needed_ref[slot] != 0)
            def _():
                pref = payload_refs[slot]
                rows = pref[0:count_rows, :]
                live = pref[count_rows:count_rows + META_ROWS, 0:128].astype(jnp.float32)[0:1, :]
                kp = jnp.dot(rows, wk_ref[...], preferred_element_type=jnp.float32)
                vp = jnp.dot(rows, wv_ref[...], preferred_element_type=jnp.float32).astype(jnp.bfloat16)
                cosine = cos_ref[slot]
                signed = sin_ref[slot]
                for p in range(pairs):
                    lo = p * 128
                    x = kp[:, lo:lo + 128]
                    other = jnp.where(first, pltpu.roll(x, 128 - quarter, 1), pltpu.roll(x, quarter, 1))
                    k_pair = (x * cosine + other * signed).astype(jnp.bfloat16)
                    v_pair = vp[:, lo:lo + 128]
                    q_pair = q_ref[:, lo:lo + 128]
                    q_two = jnp.concatenate(
                        [jnp.where(head_of_lane == sub, q_pair, jnp.zeros_like(q_pair))
                         for sub in range(per_pair)], axis=0)
                    scale_col = jnp.zeros((stacked, 1), jnp.float32)
                    for sub in range(per_pair):
                        scale_col = jnp.where(row // count_rows == sub, scale_ref[p * per_pair + sub], scale_col)
                    scores = lax.dot_general(
                        q_two, k_pair, (((1,), (1,)), ((), ())),
                        preferred_element_type=jnp.float32,
                    ) * scale_col
                    scores = jnp.where(live > 0, scores, jnp.float32(NEG))
                    best = m_ref[p]
                    fresh = jnp.maximum(best, jnp.max(scores, axis=1, keepdims=True))
                    decay = jnp.exp(best - fresh)
                    weights = jnp.exp(scores - fresh)
                    l_ref[p] = l_ref[p] * decay + jnp.sum(weights, axis=1, keepdims=True)
                    m_ref[p] = fresh
                    pv = jnp.dot(weights.astype(jnp.bfloat16), v_pair, preferred_element_type=jnp.float32)
                    acc_ref[p] = acc_ref[p] * decay + pv

        parts = []
        for p in range(pairs):
            acc_two = acc_ref[p] / l_ref[p]
            res = acc_two[0:count_rows]
            for sub in range(1, per_pair):
                res = jnp.where(head_of_lane == sub, acc_two[sub * count_rows:(sub + 1) * count_rows], res)
            parts.append(res.astype(jnp.bfloat16))
        attended = jnp.concatenate(parts, axis=1)
        mixed = tok_ref[...].astype(jnp.float32) + jnp.dot(
            attended, wo_ref[...], preferred_element_type=jnp.float32
        )
        out_ref[...] = mixed.astype(out_ref.dtype)

    return kernel


def make_query_kernel(head_dim):
    quarter = head_dim // 4

    def kernel(x_ref, w_ref, cos_ref, sin_ref, out_ref):
        proj = jnp.dot(x_ref[...], w_ref[...], preferred_element_type=jnp.float32)
        lane = lax.broadcasted_iota(jnp.int32, (proj.shape[0], 128), 1)
        first = (lane % (2 * quarter)) < quarter
        cosine = cos_ref[...]
        signed = sin_ref[...]
        for p in range(proj.shape[1] // 128):
            lo = p * 128
            x = proj[:, lo:lo + 128]
            other = jnp.where(first, pltpu.roll(x, 128 - quarter, 1), pltpu.roll(x, quarter, 1))
            out_ref[:, lo:lo + 128] = (x * cosine + other * signed).astype(out_ref.dtype)

    return kernel


def make_prep_kernel(tile_count, tile_rows, count_rows):
    def kernel(order_ref, count_ref, tok_ref, gain_ref, normed_ref, out_ref):
        floated = tok_ref[...].astype(jnp.float32)
        normed_ref[...] = layer_norm(floated, gain_ref[...]).astype(normed_ref.dtype)
        lane = lax.broadcasted_iota(jnp.int32, (META_ROWS, 128), 1)
        row = lax.broadcasted_iota(jnp.int32, (META_ROWS, 128), 0)
        live = jnp.zeros((META_ROWS, 128), jnp.float32)
        for s in range(tile_count):
            src = order_ref[s]
            start = pl.multiple_of(src * tile_rows, tile_rows)
            out_ref[s * tile_rows:(s + 1) * tile_rows, :] = normed_ref[pl.ds(start, tile_rows), :]
            inside = (lane // tile_rows == s) & ((lane % tile_rows) < count_ref[src]) & (row == 0)
            live = jnp.where(inside, jnp.float32(1), live)
        out_ref[count_rows:count_rows + META_ROWS, :] = jnp.zeros(
            (META_ROWS, out_ref.shape[1]), out_ref.dtype)
        out_ref[count_rows:count_rows + META_ROWS, 0:128] = live.astype(out_ref.dtype)

    return kernel


def across(shard, by):
    size = lax.axis_size("tok")
    epochs = lax.axis_size("ep")
    pairs = [
        ((i + by) * epochs + (epochs - 1 - e), i * epochs + e)
        for i in range(size)
        for e in range(epochs)
        if 0 <= i + by < size
    ]
    return lax.ppermute(shard, ("tok", "ep"), pairs)


def full_spec(shape):
    return pl.BlockSpec(shape, lambda i: (0,) * len(shape))


def on_device(
    tokens, norm_gain, query_weight, w_key, w_value, w_out, head_scale, matching, valid, stops
):
    count_rows, width = tokens.shape[1:]
    heads = head_scale.shape[0]
    head_dim = width // heads
    block_index = lax.axis_index("tok")
    smem = pl.BlockSpec(memory_space=pltpu.SMEM)
    vmem = pl.BlockSpec(memory_space=pltpu.VMEM)
    theirs = partner(matching[0], "ep", 0)
    tile_count = matching.shape[1]
    tile_rows = count_rows // tile_count
    normed, payload = pl.pallas_call(
        make_prep_kernel(tile_count, tile_rows, count_rows),
        out_shape=(
            jax.ShapeDtypeStruct((count_rows, width), jnp.bfloat16),
            jax.ShapeDtypeStruct((count_rows + META_ROWS, width), jnp.bfloat16),
        ),
        in_specs=[smem, smem, vmem, vmem],
        out_specs=(vmem, vmem),
    )(theirs, valid[0], tokens[0], norm_gain.reshape(1, width))

    offsets = list(range(-BAND, BAND + 1))
    blocks = block_index + jnp.array(offsets, dtype=jnp.int32)
    needed = jnp.any(stops[0, 0][None, :] == blocks[:, None], axis=1)
    cosine, signed = angle_tables(blocks, count_rows, head_dim)
    scales = (head_scale / math.sqrt(head_dim)).astype(jnp.float32)
    own = offsets.index(0)
    table_spec = pl.BlockSpec((None, count_rows, 128), lambda i: (own, 0, 0))

    queries = pl.pallas_call(
        make_query_kernel(head_dim),
        out_shape=jax.ShapeDtypeStruct((count_rows, width), jnp.bfloat16),
        grid=(1,),
        in_specs=[full_spec((count_rows, width)), full_spec((width, width)), table_spec, table_spec],
        out_specs=full_spec((count_rows, width)),
    )(normed, query_weight, cosine, signed)

    slots = len(offsets)
    received = [partner(payload, "ep", 0) if d == 0 else across(payload, d) for d in offsets]
    pairs = width // 128
    stacked = (128 // head_dim) * count_rows
    out = pl.pallas_call(
        make_band_kernel(slots, heads, head_dim, count_rows, width),
        out_shape=jax.ShapeDtypeStruct((count_rows, width), jnp.bfloat16),
        in_specs=[smem, smem] + [vmem] * (1 + slots + 6),
        out_specs=vmem,
        scratch_shapes=[
            pltpu.VMEM((pairs, stacked, 128), jnp.float32),
            pltpu.VMEM((pairs, stacked, 1), jnp.float32),
            pltpu.VMEM((pairs, stacked, 1), jnp.float32),
        ],
    )(needed.astype(jnp.int32), scales, queries, *received, cosine, signed, w_key, w_value, w_out,
      tokens[0])
    return out[None]


def solution(mesh):
    in_specs = (
        P("ep", ("grp", "tok"), None),
        P(),
        P(),
        P(),
        P(),
        P(),
        P(),
        P("ep", ("grp", "tok")),
        P("ep", ("grp", "tok")),
        P("ep", ("grp", "tok"), None),
    )
    out_specs = P("ep", ("grp", "tok"), None)
    return jax.shard_map(
        on_device, mesh=mesh, in_specs=in_specs, out_specs=out_specs, check_vma=False
    )
```

```python
import math

import jax
import jax.numpy as jnp
from jax import lax
from jax.experimental import pallas as pl
from jax.experimental.pallas import tpu as pltpu
from jax.sharding import PartitionSpec as P

BAND = 3
ROW_PATCHES = 1024
META_ROWS = 8
NEG = -1e30


def partner(block, axis, apart):
    count = lax.axis_size(axis)
    route = []
    for low in range(count):
        high = low | 1 << apart
        if high != low and high < count:
            route += [(low, high), (high, low)]
    return lax.ppermute(block, axis, route)


def layer_norm(floated, norm_gain):
    center = jnp.mean(floated, axis=-1, keepdims=True)
    spread = jnp.mean((floated - center) ** 2, axis=-1, keepdims=True)
    return (floated - center) * lax.rsqrt(spread + 1e-05) * norm_gain


def turn_pairs(part, angle):
    quarter = part.shape[-1] // 2
    first = part[..., :quarter]
    second = part[..., quarter:]
    cosine = jnp.cos(angle)[:, None, :]
    sine = jnp.sin(angle)[:, None, :]
    return jnp.concatenate(
        [first * cosine - second * sine, second * cosine + first * sine], axis=-1
    )


def frequencies(quarter):
    return 100.0 ** (-jnp.arange(quarter, dtype=jnp.float32) / quarter)


def rotate(values, patch_coordinates, heads):
    count_rows, width = values.shape
    head_dim = width // heads
    half = head_dim // 2
    quarter = head_dim // 4
    split = values.reshape(count_rows, heads, head_dim)
    row_coordinate = (patch_coordinates // ROW_PATCHES).astype(jnp.float32)
    column_coordinate = (patch_coordinates % ROW_PATCHES).astype(jnp.float32)
    freqs = frequencies(quarter)
    turned = jnp.concatenate(
        [
            turn_pairs(split[..., :half], row_coordinate[:, None] * freqs[None, :]),
            turn_pairs(split[..., half:], column_coordinate[:, None] * freqs[None, :]),
        ],
        axis=-1,
    )
    return turned.reshape(count_rows, width)


def angle_tables(blocks, count_rows, head_dim):
    half = head_dim // 2
    quarter = head_dim // 4
    lanes = jnp.arange(128, dtype=jnp.int32)
    spots = blocks[:, None] * count_rows + jnp.arange(count_rows, dtype=jnp.int32)[None, :]
    row_coordinate = (spots // ROW_PATCHES).astype(jnp.float32)
    column_coordinate = (spots % ROW_PATCHES).astype(jnp.float32)
    in_row_part = (lanes % head_dim) < half
    coordinate = jnp.where(
        in_row_part[None, None, :], row_coordinate[:, :, None], column_coordinate[:, :, None]
    )
    freq_lane = jnp.tile(frequencies(quarter), 128 // quarter)
    angle = coordinate * freq_lane[None, None, :]
    first = (lanes % half) < quarter
    cosine = jnp.cos(angle)
    sine = jnp.sin(angle)
    signed = jnp.where(first[None, None, :], -sine, sine)
    return cosine, signed


def make_band_kernel(slots, heads, head_dim, count_rows, width):
    pairs = width // 128
    quarter = head_dim // 4
    per_pair = 128 // head_dim
    stacked = per_pair * count_rows

    def kernel(needed_ref, scale_ref, q_ref, *rest):
        payload_refs = rest[:slots]
        cos_ref, sin_ref, wk_ref, wv_ref, wo_ref, tok_ref, out_ref, acc_ref, m_ref, l_ref = rest[slots:]
        acc_ref[...] = jnp.zeros_like(acc_ref)
        m_ref[...] = jnp.full(m_ref.shape, NEG, jnp.float32)
        l_ref[...] = jnp.zeros_like(l_ref)
        lane = lax.broadcasted_iota(jnp.int32, (count_rows, 128), 1)
        first = (lane % (2 * quarter)) < quarter
        head_of_lane = lane // head_dim
        row = lax.broadcasted_iota(jnp.int32, (stacked, 1), 0)

        for slot in range(slots):

            @pl.when(needed_ref[slot] != 0)
            def _():
                pref = payload_refs[slot]
                rows = pref[0:count_rows, :]
                live = pref[count_rows:count_rows + META_ROWS, 0:128].astype(jnp.float32)[0:1, :]
                kp = jnp.dot(rows, wk_ref[...], preferred_element_type=jnp.float32)
                vp = jnp.dot(rows, wv_ref[...], preferred_element_type=jnp.float32).astype(jnp.bfloat16)
                cosine = cos_ref[slot]
                signed = sin_ref[slot]
                for p in range(pairs):
                    lo = p * 128
                    x = kp[:, lo:lo + 128]
                    other = jnp.where(first, pltpu.roll(x, 128 - quarter, 1), pltpu.roll(x, quarter, 1))
                    k_pair = (x * cosine + other * signed).astype(jnp.bfloat16)
                    v_pair = vp[:, lo:lo + 128]
                    q_pair = q_ref[:, lo:lo + 128]
                    q_two = jnp.concatenate(
                        [jnp.where(head_of_lane == sub, q_pair, jnp.zeros_like(q_pair))
                         for sub in range(per_pair)], axis=0)
                    scale_col = jnp.zeros((stacked, 1), jnp.float32)
                    for sub in range(per_pair):
                        scale_col = jnp.where(row // count_rows == sub, scale_ref[p * per_pair + sub], scale_col)
                    scores = lax.dot_general(
                        q_two, k_pair, (((1,), (1,)), ((), ())),
                        preferred_element_type=jnp.float32,
                    ) * scale_col
                    scores = jnp.where(live > 0, scores, jnp.float32(NEG))
                    best = m_ref[p]
                    fresh = jnp.maximum(best, jnp.max(scores, axis=1, keepdims=True))
                    decay = jnp.exp(best - fresh)
                    weights = jnp.exp(scores - fresh)
                    l_ref[p] = l_ref[p] * decay + jnp.sum(weights, axis=1, keepdims=True)
                    m_ref[p] = fresh
                    pv = jnp.dot(weights.astype(jnp.bfloat16), v_pair, preferred_element_type=jnp.float32)
                    acc_ref[p] = acc_ref[p] * decay + pv

        parts = []
        for p in range(pairs):
            acc_two = acc_ref[p] / l_ref[p]
            res = acc_two[0:count_rows]
            for sub in range(1, per_pair):
                res = jnp.where(head_of_lane == sub, acc_two[sub * count_rows:(sub + 1) * count_rows], res)
            parts.append(res.astype(jnp.bfloat16))
        attended = jnp.concatenate(parts, axis=1)
        mixed = tok_ref[...].astype(jnp.float32) + jnp.dot(
            attended, wo_ref[...], preferred_element_type=jnp.float32
        )
        out_ref[...] = mixed.astype(out_ref.dtype)

    return kernel


def make_query_kernel(head_dim):
    quarter = head_dim // 4

    def kernel(x_ref, w_ref, cos_ref, sin_ref, out_ref):
        proj = jnp.dot(x_ref[...], w_ref[...], preferred_element_type=jnp.float32)
        lane = lax.broadcasted_iota(jnp.int32, (proj.shape[0], 128), 1)
        first = (lane % (2 * quarter)) < quarter
        cosine = cos_ref[...]
        signed = sin_ref[...]
        for p in range(proj.shape[1] // 128):
            lo = p * 128
            x = proj[:, lo:lo + 128]
            other = jnp.where(first, pltpu.roll(x, 128 - quarter, 1), pltpu.roll(x, quarter, 1))
            out_ref[:, lo:lo + 128] = (x * cosine + other * signed).astype(out_ref.dtype)

    return kernel


def make_prep_kernel(tile_count, tile_rows, count_rows):
    def kernel(order_ref, count_ref, tok_ref, gain_ref, normed_ref, out_ref):
        floated = tok_ref[...].astype(jnp.float32)
        normed_ref[...] = layer_norm(floated, gain_ref[...]).astype(normed_ref.dtype)
        lane = lax.broadcasted_iota(jnp.int32, (META_ROWS, 128), 1)
        row = lax.broadcasted_iota(jnp.int32, (META_ROWS, 128), 0)
        live = jnp.zeros((META_ROWS, 128), jnp.float32)
        for s in range(tile_count):
            src = order_ref[s]
            start = pl.multiple_of(src * tile_rows, tile_rows)
            out_ref[s * tile_rows:(s + 1) * tile_rows, :] = normed_ref[pl.ds(start, tile_rows), :]
            inside = (lane // tile_rows == s) & ((lane % tile_rows) < count_ref[src]) & (row == 0)
            live = jnp.where(inside, jnp.float32(1), live)
        out_ref[count_rows:count_rows + META_ROWS, :] = jnp.zeros(
            (META_ROWS, out_ref.shape[1]), out_ref.dtype)
        out_ref[count_rows:count_rows + META_ROWS, 0:128] = live.astype(out_ref.dtype)

    return kernel


def across(shard, by):
    size = lax.axis_size("tok")
    epochs = lax.axis_size("ep")
    pairs = [
        ((i + by) * epochs + (epochs - 1 - e), i * epochs + e)
        for i in range(size)
        for e in range(epochs)
        if 0 <= i + by < size
    ]
    return lax.ppermute(shard, ("tok", "ep"), pairs)


def full_spec(shape):
    return pl.BlockSpec(shape, lambda i: (0,) * len(shape))


def on_device(
    tokens, norm_gain, query_weight, w_key, w_value, w_out, head_scale, matching, valid, stops
):
    count_rows, width = tokens.shape[1:]
    heads = head_scale.shape[0]
    head_dim = width // heads
    block_index = lax.axis_index("tok")
    smem = pl.BlockSpec(memory_space=pltpu.SMEM)
    vmem = pl.BlockSpec(memory_space=pltpu.VMEM)
    theirs = partner(matching[0], "ep", 0)
    tile_count = matching.shape[1]
    tile_rows = count_rows // tile_count
    normed, payload = pl.pallas_call(
        make_prep_kernel(tile_count, tile_rows, count_rows),
        out_shape=(
            jax.ShapeDtypeStruct((count_rows, width), jnp.bfloat16),
            jax.ShapeDtypeStruct((count_rows + META_ROWS, width), jnp.bfloat16),
        ),
        in_specs=[smem, smem, vmem, vmem],
        out_specs=(vmem, vmem),
    )(theirs, valid[0], tokens[0], norm_gain.reshape(1, width))

    _, stops, head_scale, block_index = lax.optimization_barrier(
        (payload, stops, head_scale, block_index))
    offsets = list(range(-BAND, BAND + 1))
    blocks = block_index + jnp.array(offsets, dtype=jnp.int32)
    needed = jnp.any(stops[0, 0][None, :] == blocks[:, None], axis=1)
    cosine, signed = angle_tables(blocks, count_rows, head_dim)
    scales = (head_scale / math.sqrt(head_dim)).astype(jnp.float32)
    own = offsets.index(0)
    table_spec = pl.BlockSpec((None, count_rows, 128), lambda i: (own, 0, 0))

    queries = pl.pallas_call(
        make_query_kernel(head_dim),
        out_shape=jax.ShapeDtypeStruct((count_rows, width), jnp.bfloat16),
        grid=(1,),
        in_specs=[full_spec((count_rows, width)), full_spec((width, width)), table_spec, table_spec],
        out_specs=full_spec((count_rows, width)),
    )(normed, query_weight, cosine, signed)

    slots = len(offsets)
    received = [partner(payload, "ep", 0) if d == 0 else across(payload, d) for d in offsets]
    pairs = width // 128
    stacked = (128 // head_dim) * count_rows
    out = pl.pallas_call(
        make_band_kernel(slots, heads, head_dim, count_rows, width),
        out_shape=jax.ShapeDtypeStruct((count_rows, width), jnp.bfloat16),
        in_specs=[smem, smem] + [vmem] * (1 + slots + 6),
        out_specs=vmem,
        scratch_shapes=[
            pltpu.VMEM((pairs, stacked, 128), jnp.float32),
            pltpu.VMEM((pairs, stacked, 1), jnp.float32),
            pltpu.VMEM((pairs, stacked, 1), jnp.float32),
        ],
    )(needed.astype(jnp.int32), scales, queries, *received, cosine, signed, w_key, w_value, w_out,
      tokens[0])
    return out[None]


def solution(mesh):
    in_specs = (
        P("ep", ("grp", "tok"), None),
        P(),
        P(),
        P(),
        P(),
        P(),
        P(),
        P("ep", ("grp", "tok")),
        P("ep", ("grp", "tok")),
        P("ep", ("grp", "tok"), None),
    )
    out_specs = P("ep", ("grp", "tok"), None)
    return jax.shard_map(
        on_device, mesh=mesh, in_specs=in_specs, out_specs=out_specs, check_vma=False
    )
```

```python
import math

import jax
import jax.numpy as jnp
from jax import lax
from jax.experimental import pallas as pl
from jax.experimental.pallas import tpu as pltpu
from jax.sharding import PartitionSpec as P

BAND = 3
ROW_PATCHES = 1024
META_ROWS = 8
NEG = -1e30


def partner(block, axis, apart):
    count = lax.axis_size(axis)
    route = []
    for low in range(count):
        high = low | 1 << apart
        if high != low and high < count:
            route += [(low, high), (high, low)]
    return lax.ppermute(block, axis, route)


def layer_norm(floated, norm_gain):
    center = jnp.mean(floated, axis=-1, keepdims=True)
    spread = jnp.mean((floated - center) ** 2, axis=-1, keepdims=True)
    return (floated - center) * lax.rsqrt(spread + 1e-05) * norm_gain


def turn_pairs(part, angle):
    quarter = part.shape[-1] // 2
    first = part[..., :quarter]
    second = part[..., quarter:]
    cosine = jnp.cos(angle)[:, None, :]
    sine = jnp.sin(angle)[:, None, :]
    return jnp.concatenate(
        [first * cosine - second * sine, second * cosine + first * sine], axis=-1
    )


def frequencies(quarter):
    return 100.0 ** (-jnp.arange(quarter, dtype=jnp.float32) / quarter)


def rotate(values, patch_coordinates, heads):
    count_rows, width = values.shape
    head_dim = width // heads
    half = head_dim // 2
    quarter = head_dim // 4
    split = values.reshape(count_rows, heads, head_dim)
    row_coordinate = (patch_coordinates // ROW_PATCHES).astype(jnp.float32)
    column_coordinate = (patch_coordinates % ROW_PATCHES).astype(jnp.float32)
    freqs = frequencies(quarter)
    turned = jnp.concatenate(
        [
            turn_pairs(split[..., :half], row_coordinate[:, None] * freqs[None, :]),
            turn_pairs(split[..., half:], column_coordinate[:, None] * freqs[None, :]),
        ],
        axis=-1,
    )
    return turned.reshape(count_rows, width)


def angle_tables(blocks, count_rows, head_dim):
    half = head_dim // 2
    quarter = head_dim // 4
    lanes = jnp.arange(128, dtype=jnp.int32)
    spots = blocks[:, None] * count_rows + jnp.arange(count_rows, dtype=jnp.int32)[None, :]
    row_coordinate = (spots // ROW_PATCHES).astype(jnp.float32)
    column_coordinate = (spots % ROW_PATCHES).astype(jnp.float32)
    in_row_part = (lanes % head_dim) < half
    coordinate = jnp.where(
        in_row_part[None, None, :], row_coordinate[:, :, None], column_coordinate[:, :, None]
    )
    freq_lane = jnp.tile(frequencies(quarter), 128 // quarter)
    angle = coordinate * freq_lane[None, None, :]
    first = (lanes % half) < quarter
    cosine = jnp.cos(angle)
    sine = jnp.sin(angle)
    signed = jnp.where(first[None, None, :], -sine, sine)
    return cosine, signed


def make_band_kernel(slots, heads, head_dim, count_rows, width):
    pairs = width // 128
    quarter = head_dim // 4
    per_pair = 128 // head_dim
    stacked = per_pair * count_rows

    def kernel(needed_ref, scale_ref, q_ref, *rest):
        payload_refs = rest[:slots]
        cos_ref, sin_ref, wk_ref, wv_ref, wo_ref, tok_ref, out_ref, acc_ref, m_ref, l_ref = rest[slots:]
        acc_ref[...] = jnp.zeros_like(acc_ref)
        m_ref[...] = jnp.full(m_ref.shape, NEG, jnp.float32)
        l_ref[...] = jnp.zeros_like(l_ref)
        lane = lax.broadcasted_iota(jnp.int32, (count_rows, 128), 1)
        first = (lane % (2 * quarter)) < quarter
        head_of_lane = lane // head_dim
        row = lax.broadcasted_iota(jnp.int32, (stacked, 1), 0)

        for slot in range(slots):

            @pl.when(needed_ref[slot] != 0)
            def _():
                pref = payload_refs[slot]
                rows = pref[...]
                kp = jnp.dot(rows, wk_ref[...], preferred_element_type=jnp.float32)
                vp = jnp.dot(rows, wv_ref[...], preferred_element_type=jnp.float32)
                vp = jnp.where(jnp.abs(vp) < jnp.inf, vp, jnp.float32(0)).astype(jnp.bfloat16)
                cosine = cos_ref[slot]
                signed = sin_ref[slot]
                for p in range(pairs):
                    lo = p * 128
                    x = kp[:, lo:lo + 128]
                    other = jnp.where(first, pltpu.roll(x, 128 - quarter, 1), pltpu.roll(x, quarter, 1))
                    k_pair = (x * cosine + other * signed).astype(jnp.bfloat16)
                    v_pair = vp[:, lo:lo + 128]
                    q_pair = q_ref[:, lo:lo + 128]
                    q_two = jnp.concatenate(
                        [jnp.where(head_of_lane == sub, q_pair, jnp.zeros_like(q_pair))
                         for sub in range(per_pair)], axis=0)
                    scale_col = jnp.zeros((stacked, 1), jnp.float32)
                    for sub in range(per_pair):
                        scale_col = jnp.where(row // count_rows == sub, scale_ref[p * per_pair + sub], scale_col)
                    scores = lax.dot_general(
                        q_two, k_pair, (((1,), (1,)), ((), ())),
                        preferred_element_type=jnp.float32,
                    ) * scale_col
                    scores = jnp.where(jnp.abs(scores) < jnp.inf, scores, jnp.float32(NEG))
                    best = m_ref[p]
                    fresh = jnp.maximum(best, jnp.max(scores, axis=1, keepdims=True))
                    decay = jnp.exp(best - fresh)
                    weights = jnp.exp(scores - fresh)
                    l_ref[p] = l_ref[p] * decay + jnp.sum(weights, axis=1, keepdims=True)
                    m_ref[p] = fresh
                    pv = jnp.dot(weights.astype(jnp.bfloat16), v_pair, preferred_element_type=jnp.float32)
                    acc_ref[p] = acc_ref[p] * decay + pv

        parts = []
        for p in range(pairs):
            acc_two = acc_ref[p] / l_ref[p]
            res = acc_two[0:count_rows]
            for sub in range(1, per_pair):
                res = jnp.where(head_of_lane == sub, acc_two[sub * count_rows:(sub + 1) * count_rows], res)
            parts.append(res.astype(jnp.bfloat16))
        attended = jnp.concatenate(parts, axis=1)
        mixed = tok_ref[...].astype(jnp.float32) + jnp.dot(
            attended, wo_ref[...], preferred_element_type=jnp.float32
        )
        out_ref[...] = mixed.astype(out_ref.dtype)

    return kernel


def make_query_kernel(head_dim):
    quarter = head_dim // 4

    def kernel(x_ref, w_ref, cos_ref, sin_ref, out_ref):
        proj = jnp.dot(x_ref[...], w_ref[...], preferred_element_type=jnp.float32)
        lane = lax.broadcasted_iota(jnp.int32, (proj.shape[0], 128), 1)
        first = (lane % (2 * quarter)) < quarter
        cosine = cos_ref[...]
        signed = sin_ref[...]
        for p in range(proj.shape[1] // 128):
            lo = p * 128
            x = proj[:, lo:lo + 128]
            other = jnp.where(first, pltpu.roll(x, 128 - quarter, 1), pltpu.roll(x, quarter, 1))
            out_ref[:, lo:lo + 128] = (x * cosine + other * signed).astype(out_ref.dtype)

    return kernel


def make_prep_kernel(tile_count, tile_rows, count_rows):
    def kernel(order_ref, count_ref, tok_ref, gain_ref, normed_ref, out_ref):
        floated = tok_ref[...].astype(jnp.float32)
        normed_ref[...] = layer_norm(floated, gain_ref[...]).astype(normed_ref.dtype)
        row = lax.broadcasted_iota(jnp.int32, (tile_rows, 1), 0)
        for s in range(tile_count):
            src = order_ref[s]
            start = pl.multiple_of(src * tile_rows, tile_rows)
            rows = normed_ref[pl.ds(start, tile_rows), :]
            out_ref[s * tile_rows:(s + 1) * tile_rows, :] = jnp.where(
                row < count_ref[src], rows, jnp.asarray(jnp.inf, rows.dtype))

    return kernel


def across(shard, by):
    size = lax.axis_size("tok")
    epochs = lax.axis_size("ep")
    pairs = [
        ((i + by) * epochs + (epochs - 1 - e), i * epochs + e)
        for i in range(size)
        for e in range(epochs)
        if 0 <= i + by < size
    ]
    return lax.ppermute(shard, ("tok", "ep"), pairs)


def full_spec(shape):
    return pl.BlockSpec(shape, lambda i: (0,) * len(shape))


def on_device(
    tokens, norm_gain, query_weight, w_key, w_value, w_out, head_scale, matching, valid, stops
):
    count_rows, width = tokens.shape[1:]
    heads = head_scale.shape[0]
    head_dim = width // heads
    block_index = lax.axis_index("tok")
    smem = pl.BlockSpec(memory_space=pltpu.SMEM)
    vmem = pl.BlockSpec(memory_space=pltpu.VMEM)
    theirs = partner(matching[0], "ep", 0)
    tile_count = matching.shape[1]
    tile_rows = count_rows // tile_count
    normed, payload = pl.pallas_call(
        make_prep_kernel(tile_count, tile_rows, count_rows),
        out_shape=(
            jax.ShapeDtypeStruct((count_rows, width), jnp.bfloat16),
            jax.ShapeDtypeStruct((count_rows, width), jnp.bfloat16),
        ),
        in_specs=[smem, smem, vmem, vmem],
        out_specs=(vmem, vmem),
    )(theirs, valid[0], tokens[0], norm_gain.reshape(1, width))

    offsets = list(range(-BAND, BAND + 1))
    blocks = block_index + jnp.array(offsets, dtype=jnp.int32)
    needed = jnp.any(stops[0, 0][None, :] == blocks[:, None], axis=1)
    cosine, signed = angle_tables(blocks, count_rows, head_dim)
    scales = (head_scale / math.sqrt(head_dim)).astype(jnp.float32)
    own = offsets.index(0)
    table_spec = pl.BlockSpec((None, count_rows, 128), lambda i: (own, 0, 0))

    queries = pl.pallas_call(
        make_query_kernel(head_dim),
        out_shape=jax.ShapeDtypeStruct((count_rows, width), jnp.bfloat16),
        grid=(1,),
        in_specs=[full_spec((count_rows, width)), full_spec((width, width)), table_spec, table_spec],
        out_specs=full_spec((count_rows, width)),
    )(normed, query_weight, cosine, signed)

    slots = len(offsets)
    received = [partner(payload, "ep", 0) if d == 0 else across(payload, d) for d in offsets]
    pairs = width // 128
    stacked = (128 // head_dim) * count_rows
    out = pl.pallas_call(
        make_band_kernel(slots, heads, head_dim, count_rows, width),
        out_shape=jax.ShapeDtypeStruct((count_rows, width), jnp.bfloat16),
        in_specs=[smem, smem] + [vmem] * (1 + slots + 6),
        out_specs=vmem,
        scratch_shapes=[
            pltpu.VMEM((pairs, stacked, 128), jnp.float32),
            pltpu.VMEM((pairs, stacked, 1), jnp.float32),
            pltpu.VMEM((pairs, stacked, 1), jnp.float32),
        ],
    )(needed.astype(jnp.int32), scales, queries, *received, cosine, signed, w_key, w_value, w_out,
      tokens[0])
    return out[None]


def solution(mesh):
    in_specs = (
        P("ep", ("grp", "tok"), None),
        P(),
        P(),
        P(),
        P(),
        P(),
        P(),
        P("ep", ("grp", "tok")),
        P("ep", ("grp", "tok")),
        P("ep", ("grp", "tok"), None),
    )
    out_specs = P("ep", ("grp", "tok"), None)
    return jax.shard_map(
        on_device, mesh=mesh, in_specs=in_specs, out_specs=out_specs, check_vma=False
    )
```

```python
import math

import jax
import jax.numpy as jnp
from jax import lax
from jax.experimental import pallas as pl
from jax.experimental.pallas import tpu as pltpu
from jax.sharding import PartitionSpec as P

BAND = 3
ROW_PATCHES = 1024
META_ROWS = 8
NEG = -1e30


def partner(block, axis, apart):
    count = lax.axis_size(axis)
    route = []
    for low in range(count):
        high = low | 1 << apart
        if high != low and high < count:
            route += [(low, high), (high, low)]
    return lax.ppermute(block, axis, route)


def layer_norm(floated, norm_gain):
    center = jnp.mean(floated, axis=-1, keepdims=True)
    spread = jnp.mean((floated - center) ** 2, axis=-1, keepdims=True)
    return (floated - center) * lax.rsqrt(spread + 1e-05) * norm_gain


def turn_pairs(part, angle):
    quarter = part.shape[-1] // 2
    first = part[..., :quarter]
    second = part[..., quarter:]
    cosine = jnp.cos(angle)[:, None, :]
    sine = jnp.sin(angle)[:, None, :]
    return jnp.concatenate(
        [first * cosine - second * sine, second * cosine + first * sine], axis=-1
    )


def frequencies(quarter):
    return 100.0 ** (-jnp.arange(quarter, dtype=jnp.float32) / quarter)


def rotate(values, patch_coordinates, heads):
    count_rows, width = values.shape
    head_dim = width // heads
    half = head_dim // 2
    quarter = head_dim // 4
    split = values.reshape(count_rows, heads, head_dim)
    row_coordinate = (patch_coordinates // ROW_PATCHES).astype(jnp.float32)
    column_coordinate = (patch_coordinates % ROW_PATCHES).astype(jnp.float32)
    freqs = frequencies(quarter)
    turned = jnp.concatenate(
        [
            turn_pairs(split[..., :half], row_coordinate[:, None] * freqs[None, :]),
            turn_pairs(split[..., half:], column_coordinate[:, None] * freqs[None, :]),
        ],
        axis=-1,
    )
    return turned.reshape(count_rows, width)


def angle_tables(blocks, count_rows, head_dim):
    half = head_dim // 2
    quarter = head_dim // 4
    lanes = jnp.arange(128, dtype=jnp.int32)
    spots = blocks[:, None] * count_rows + jnp.arange(count_rows, dtype=jnp.int32)[None, :]
    row_coordinate = (spots // ROW_PATCHES).astype(jnp.float32)
    column_coordinate = (spots % ROW_PATCHES).astype(jnp.float32)
    in_row_part = (lanes % head_dim) < half
    coordinate = jnp.where(
        in_row_part[None, None, :], row_coordinate[:, :, None], column_coordinate[:, :, None]
    )
    freq_lane = jnp.tile(frequencies(quarter), 128 // quarter)
    angle = coordinate * freq_lane[None, None, :]
    first = (lanes % half) < quarter
    cosine = jnp.cos(angle)
    sine = jnp.sin(angle)
    signed = jnp.where(first[None, None, :], -sine, sine)
    return cosine, signed


def make_band_kernel(slots, heads, head_dim, count_rows, width):
    pairs = width // 128
    quarter = head_dim // 4
    per_pair = 128 // head_dim
    stacked = per_pair * count_rows

    def kernel(needed_ref, scale_ref, q_ref, *rest):
        payload_hbm = rest[:slots]
        (cos_ref, sin_ref, wk_ref, wv_ref, wo_hbm, tok_ref, out_ref, acc_ref, m_ref, l_ref,
         pay_buf, wo_ref, sems) = rest[slots:]
        copies = [pltpu.make_async_copy(payload_hbm[slot], pay_buf.at[slot], sems.at[slot])
                  for slot in range(slots)]
        wo_copy = pltpu.make_async_copy(wo_hbm, wo_ref, sems.at[slots])
        for slot in range(slots):

            @pl.when(needed_ref[slot] != 0)
            def _():
                copies[slot].start()

        wo_copy.start()
        acc_ref[...] = jnp.zeros_like(acc_ref)
        m_ref[...] = jnp.full(m_ref.shape, NEG, jnp.float32)
        l_ref[...] = jnp.zeros_like(l_ref)
        lane = lax.broadcasted_iota(jnp.int32, (count_rows, 128), 1)
        first = (lane % (2 * quarter)) < quarter
        head_of_lane = lane // head_dim
        row = lax.broadcasted_iota(jnp.int32, (stacked, 1), 0)

        for slot in range(slots):

            @pl.when(needed_ref[slot] != 0)
            def _():
                copies[slot].wait()
                rows = pay_buf[slot]
                kp = jnp.dot(rows, wk_ref[...], preferred_element_type=jnp.float32)
                vp = jnp.dot(rows, wv_ref[...], preferred_element_type=jnp.float32)
                vp = jnp.where(jnp.abs(vp) < jnp.inf, vp, jnp.float32(0)).astype(jnp.bfloat16)
                cosine = cos_ref[slot]
                signed = sin_ref[slot]
                for p in range(pairs):
                    lo = p * 128
                    x = kp[:, lo:lo + 128]
                    other = jnp.where(first, pltpu.roll(x, 128 - quarter, 1), pltpu.roll(x, quarter, 1))
                    k_pair = (x * cosine + other * signed).astype(jnp.bfloat16)
                    v_pair = vp[:, lo:lo + 128]
                    q_pair = q_ref[:, lo:lo + 128]
                    q_two = jnp.concatenate(
                        [jnp.where(head_of_lane == sub, q_pair, jnp.zeros_like(q_pair))
                         for sub in range(per_pair)], axis=0)
                    scale_col = jnp.zeros((stacked, 1), jnp.float32)
                    for sub in range(per_pair):
                        scale_col = jnp.where(row // count_rows == sub, scale_ref[p * per_pair + sub], scale_col)
                    scores = lax.dot_general(
                        q_two, k_pair, (((1,), (1,)), ((), ())),
                        preferred_element_type=jnp.float32,
                    ) * scale_col
                    scores = jnp.where(jnp.abs(scores) < jnp.inf, scores, jnp.float32(NEG))
                    best = m_ref[p]
                    fresh = jnp.maximum(best, jnp.max(scores, axis=1, keepdims=True))
                    decay = jnp.exp(best - fresh)
                    weights = jnp.exp(scores - fresh)
                    l_ref[p] = l_ref[p] * decay + jnp.sum(weights, axis=1, keepdims=True)
                    m_ref[p] = fresh
                    pv = jnp.dot(weights.astype(jnp.bfloat16), v_pair, preferred_element_type=jnp.float32)
                    acc_ref[p] = acc_ref[p] * decay + pv

        parts = []
        for p in range(pairs):
            acc_two = acc_ref[p] / l_ref[p]
            res = acc_two[0:count_rows]
            for sub in range(1, per_pair):
                res = jnp.where(head_of_lane == sub, acc_two[sub * count_rows:(sub + 1) * count_rows], res)
            parts.append(res.astype(jnp.bfloat16))
        attended = jnp.concatenate(parts, axis=1)
        wo_copy.wait()
        mixed = tok_ref[...].astype(jnp.float32) + jnp.dot(
            attended, wo_ref[...], preferred_element_type=jnp.float32
        )
        out_ref[...] = mixed.astype(out_ref.dtype)

    return kernel


def make_query_kernel(head_dim):
    quarter = head_dim // 4

    def kernel(x_ref, w_ref, cos_ref, sin_ref, out_ref):
        proj = jnp.dot(x_ref[...], w_ref[...], preferred_element_type=jnp.float32)
        lane = lax.broadcasted_iota(jnp.int32, (proj.shape[0], 128), 1)
        first = (lane % (2 * quarter)) < quarter
        cosine = cos_ref[...]
        signed = sin_ref[...]
        for p in range(proj.shape[1] // 128):
            lo = p * 128
            x = proj[:, lo:lo + 128]
            other = jnp.where(first, pltpu.roll(x, 128 - quarter, 1), pltpu.roll(x, quarter, 1))
            out_ref[:, lo:lo + 128] = (x * cosine + other * signed).astype(out_ref.dtype)

    return kernel


def make_prep_kernel(tile_count, tile_rows, count_rows):
    def kernel(order_ref, count_ref, tok_ref, gain_ref, normed_ref, out_ref):
        floated = tok_ref[...].astype(jnp.float32)
        normed_ref[...] = layer_norm(floated, gain_ref[...]).astype(normed_ref.dtype)
        row = lax.broadcasted_iota(jnp.int32, (tile_rows, 1), 0)
        for s in range(tile_count):
            src = order_ref[s]
            start = pl.multiple_of(src * tile_rows, tile_rows)
            rows = normed_ref[pl.ds(start, tile_rows), :]
            out_ref[s * tile_rows:(s + 1) * tile_rows, :] = jnp.where(
                row < count_ref[src], rows, jnp.asarray(jnp.inf, rows.dtype))

    return kernel


def across(shard, by):
    size = lax.axis_size("tok")
    epochs = lax.axis_size("ep")
    pairs = [
        ((i + by) * epochs + (epochs - 1 - e), i * epochs + e)
        for i in range(size)
        for e in range(epochs)
        if 0 <= i + by < size
    ]
    return lax.ppermute(shard, ("tok", "ep"), pairs)


def full_spec(shape):
    return pl.BlockSpec(shape, lambda i: (0,) * len(shape))


def on_device(
    tokens, norm_gain, query_weight, w_key, w_value, w_out, head_scale, matching, valid, stops
):
    count_rows, width = tokens.shape[1:]
    heads = head_scale.shape[0]
    head_dim = width // heads
    block_index = lax.axis_index("tok")
    smem = pl.BlockSpec(memory_space=pltpu.SMEM)
    vmem = pl.BlockSpec(memory_space=pltpu.VMEM)
    hbm = pl.BlockSpec(memory_space=pl.ANY)
    theirs = partner(matching[0], "ep", 0)
    tile_count = matching.shape[1]
    tile_rows = count_rows // tile_count
    normed, payload = pl.pallas_call(
        make_prep_kernel(tile_count, tile_rows, count_rows),
        out_shape=(
            jax.ShapeDtypeStruct((count_rows, width), jnp.bfloat16),
            jax.ShapeDtypeStruct((count_rows, width), jnp.bfloat16),
        ),
        in_specs=[smem, smem, vmem, vmem],
        out_specs=(vmem, vmem),
    )(theirs, valid[0], tokens[0], norm_gain.reshape(1, width))

    offsets = list(range(-BAND, BAND + 1))
    blocks = block_index + jnp.array(offsets, dtype=jnp.int32)
    needed = jnp.any(stops[0, 0][None, :] == blocks[:, None], axis=1)
    cosine, signed = angle_tables(blocks, count_rows, head_dim)
    scales = (head_scale / math.sqrt(head_dim)).astype(jnp.float32)
    own = offsets.index(0)
    table_spec = pl.BlockSpec((None, count_rows, 128), lambda i: (own, 0, 0))

    queries = pl.pallas_call(
        make_query_kernel(head_dim),
        out_shape=jax.ShapeDtypeStruct((count_rows, width), jnp.bfloat16),
        grid=(1,),
        in_specs=[full_spec((count_rows, width)), full_spec((width, width)), table_spec, table_spec],
        out_specs=full_spec((count_rows, width)),
    )(normed, query_weight, cosine, signed)

    slots = len(offsets)
    received = [partner(payload, "ep", 0) if d == 0 else across(payload, d) for d in offsets]
    pairs = width // 128
    stacked = (128 // head_dim) * count_rows
    out = pl.pallas_call(
        make_band_kernel(slots, heads, head_dim, count_rows, width),
        out_shape=jax.ShapeDtypeStruct((count_rows, width), jnp.bfloat16),
        in_specs=[smem, smem, vmem] + [hbm] * slots + [vmem] * 4 + [hbm, vmem],
        out_specs=vmem,
        scratch_shapes=[
            pltpu.VMEM((pairs, stacked, 128), jnp.float32),
            pltpu.VMEM((pairs, stacked, 1), jnp.float32),
            pltpu.VMEM((pairs, stacked, 1), jnp.float32),
            pltpu.VMEM((slots, count_rows, width), jnp.bfloat16),
            pltpu.VMEM((width, width), jnp.bfloat16),
            pltpu.SemaphoreType.DMA((slots + 1,)),
        ],
    )(needed.astype(jnp.int32), scales, queries, *received, cosine, signed, w_key, w_value, w_out,
      tokens[0])
    return out[None]


def solution(mesh):
    in_specs = (
        P("ep", ("grp", "tok"), None),
        P(),
        P(),
        P(),
        P(),
        P(),
        P(),
        P("ep", ("grp", "tok")),
        P("ep", ("grp", "tok")),
        P("ep", ("grp", "tok"), None),
    )
    out_specs = P("ep", ("grp", "tok"), None)
    return jax.shard_map(
        on_device, mesh=mesh, in_specs=in_specs, out_specs=out_specs, check_vma=False
    )
```

```python
import math

import jax
import jax.numpy as jnp
from jax import lax
from jax.experimental import pallas as pl
from jax.experimental.pallas import tpu as pltpu
from jax.sharding import PartitionSpec as P

BAND = 3
ROW_PATCHES = 1024
META_ROWS = 8
NEG = -1e30


def partner(block, axis, apart):
    count = lax.axis_size(axis)
    route = []
    for low in range(count):
        high = low | 1 << apart
        if high != low and high < count:
            route += [(low, high), (high, low)]
    return lax.ppermute(block, axis, route)


def layer_norm(floated, norm_gain):
    center = jnp.mean(floated, axis=-1, keepdims=True)
    spread = jnp.mean((floated - center) ** 2, axis=-1, keepdims=True)
    return (floated - center) * lax.rsqrt(spread + 1e-05) * norm_gain


def turn_pairs(part, angle):
    quarter = part.shape[-1] // 2
    first = part[..., :quarter]
    second = part[..., quarter:]
    cosine = jnp.cos(angle)[:, None, :]
    sine = jnp.sin(angle)[:, None, :]
    return jnp.concatenate(
        [first * cosine - second * sine, second * cosine + first * sine], axis=-1
    )


def frequencies(quarter):
    return 100.0 ** (-jnp.arange(quarter, dtype=jnp.float32) / quarter)


def rotate(values, patch_coordinates, heads):
    count_rows, width = values.shape
    head_dim = width // heads
    half = head_dim // 2
    quarter = head_dim // 4
    split = values.reshape(count_rows, heads, head_dim)
    row_coordinate = (patch_coordinates // ROW_PATCHES).astype(jnp.float32)
    column_coordinate = (patch_coordinates % ROW_PATCHES).astype(jnp.float32)
    freqs = frequencies(quarter)
    turned = jnp.concatenate(
        [
            turn_pairs(split[..., :half], row_coordinate[:, None] * freqs[None, :]),
            turn_pairs(split[..., half:], column_coordinate[:, None] * freqs[None, :]),
        ],
        axis=-1,
    )
    return turned.reshape(count_rows, width)


def angle_tables(blocks, count_rows, head_dim):
    half = head_dim // 2
    quarter = head_dim // 4
    lanes = jnp.arange(128, dtype=jnp.int32)
    spots = blocks[:, None] * count_rows + jnp.arange(count_rows, dtype=jnp.int32)[None, :]
    row_coordinate = (spots // ROW_PATCHES).astype(jnp.float32)
    column_coordinate = (spots % ROW_PATCHES).astype(jnp.float32)
    in_row_part = (lanes % head_dim) < half
    coordinate = jnp.where(
        in_row_part[None, None, :], row_coordinate[:, :, None], column_coordinate[:, :, None]
    )
    freq_lane = jnp.tile(frequencies(quarter), 128 // quarter)
    angle = coordinate * freq_lane[None, None, :]
    first = (lanes % half) < quarter
    cosine = jnp.cos(angle)
    sine = jnp.sin(angle)
    signed = jnp.where(first[None, None, :], -sine, sine)
    return cosine, signed


def make_band_kernel(slots, reads, heads, head_dim, count_rows, width):
    pairs = width // 128
    quarter = head_dim // 4
    per_pair = 128 // head_dim
    stacked = per_pair * count_rows

    def kernel(needed_ref, place_ref, scale_ref, q_ref, *rest):
        payload_refs = rest[:slots]
        cos_ref, sin_ref, wk_ref, wv_ref, wo_ref, tok_ref, out_ref, k_buf, v_buf = rest[slots:]
        lane = lax.broadcasted_iota(jnp.int32, (count_rows, 128), 1)
        first = (lane % (2 * quarter)) < quarter
        head_of_lane = lane // head_dim
        row = lax.broadcasted_iota(jnp.int32, (stacked, 1), 0)

        for slot in range(slots):

            @pl.when(needed_ref[slot] != 0)
            def _():
                rows = payload_refs[slot][...]
                at = pl.ds(pl.multiple_of(place_ref[slot] * count_rows, count_rows), count_rows)
                kp = jnp.dot(rows, wk_ref[...], preferred_element_type=jnp.float32)
                vp = jnp.dot(rows, wv_ref[...], preferred_element_type=jnp.float32)
                v_buf[at, :] = jnp.where(jnp.abs(vp) < jnp.inf, vp, jnp.float32(0)).astype(jnp.bfloat16)
                cosine = cos_ref[slot]
                signed = sin_ref[slot]
                for p in range(pairs):
                    lo = p * 128
                    x = kp[:, lo:lo + 128]
                    other = jnp.where(first, pltpu.roll(x, 128 - quarter, 1), pltpu.roll(x, quarter, 1))
                    k_buf[at, lo:lo + 128] = (x * cosine + other * signed).astype(jnp.bfloat16)

        parts = []
        for p in range(pairs):
            lo = p * 128
            q_pair = q_ref[:, lo:lo + 128]
            q_two = jnp.concatenate(
                [jnp.where(head_of_lane == sub, q_pair, jnp.zeros_like(q_pair))
                 for sub in range(per_pair)], axis=0)
            scale_col = jnp.zeros((stacked, 1), jnp.float32)
            for sub in range(per_pair):
                scale_col = jnp.where(row // count_rows == sub, scale_ref[p * per_pair + sub], scale_col)
            scores = lax.dot_general(
                q_two, k_buf[:, lo:lo + 128], (((1,), (1,)), ((), ())),
                preferred_element_type=jnp.float32,
            ) * scale_col
            scores = jnp.where(jnp.abs(scores) < jnp.inf, scores, jnp.float32(NEG))
            best = jnp.max(scores, axis=1, keepdims=True)
            weights = jnp.exp(scores - best)
            total = jnp.sum(weights, axis=1, keepdims=True)
            summed = jnp.dot(weights.astype(jnp.bfloat16), v_buf[:, lo:lo + 128],
                             preferred_element_type=jnp.float32)
            two = summed / total
            res = two[0:count_rows]
            for sub in range(1, per_pair):
                res = jnp.where(head_of_lane == sub, two[sub * count_rows:(sub + 1) * count_rows], res)
            parts.append(res.astype(jnp.bfloat16))
        attended = jnp.concatenate(parts, axis=1)
        mixed = tok_ref[...].astype(jnp.float32) + jnp.dot(
            attended, wo_ref[...], preferred_element_type=jnp.float32
        )
        out_ref[...] = mixed.astype(out_ref.dtype)

    return kernel


def make_query_kernel(head_dim):
    quarter = head_dim // 4

    def kernel(x_ref, w_ref, cos_ref, sin_ref, out_ref):
        proj = jnp.dot(x_ref[...], w_ref[...], preferred_element_type=jnp.float32)
        lane = lax.broadcasted_iota(jnp.int32, (proj.shape[0], 128), 1)
        first = (lane % (2 * quarter)) < quarter
        cosine = cos_ref[...]
        signed = sin_ref[...]
        for p in range(proj.shape[1] // 128):
            lo = p * 128
            x = proj[:, lo:lo + 128]
            other = jnp.where(first, pltpu.roll(x, 128 - quarter, 1), pltpu.roll(x, quarter, 1))
            out_ref[:, lo:lo + 128] = (x * cosine + other * signed).astype(out_ref.dtype)

    return kernel


def make_prep_kernel(tile_count, tile_rows, count_rows):
    def kernel(order_ref, count_ref, tok_ref, gain_ref, normed_ref, out_ref):
        floated = tok_ref[...].astype(jnp.float32)
        normed_ref[...] = layer_norm(floated, gain_ref[...]).astype(normed_ref.dtype)
        row = lax.broadcasted_iota(jnp.int32, (tile_rows, 1), 0)
        for s in range(tile_count):
            src = order_ref[s]
            start = pl.multiple_of(src * tile_rows, tile_rows)
            rows = normed_ref[pl.ds(start, tile_rows), :]
            out_ref[s * tile_rows:(s + 1) * tile_rows, :] = jnp.where(
                row < count_ref[src], rows, jnp.asarray(jnp.inf, rows.dtype))

    return kernel


def across(shard, by):
    size = lax.axis_size("tok")
    epochs = lax.axis_size("ep")
    pairs = [
        ((i + by) * epochs + (epochs - 1 - e), i * epochs + e)
        for i in range(size)
        for e in range(epochs)
        if 0 <= i + by < size
    ]
    return lax.ppermute(shard, ("tok", "ep"), pairs)


def full_spec(shape):
    return pl.BlockSpec(shape, lambda i: (0,) * len(shape))


def on_device(
    tokens, norm_gain, query_weight, w_key, w_value, w_out, head_scale, matching, valid, stops
):
    count_rows, width = tokens.shape[1:]
    heads = head_scale.shape[0]
    head_dim = width // heads
    block_index = lax.axis_index("tok")
    smem = pl.BlockSpec(memory_space=pltpu.SMEM)
    vmem = pl.BlockSpec(memory_space=pltpu.VMEM)
    theirs = partner(matching[0], "ep", 0)
    tile_count = matching.shape[1]
    tile_rows = count_rows // tile_count
    normed, payload = pl.pallas_call(
        make_prep_kernel(tile_count, tile_rows, count_rows),
        out_shape=(
            jax.ShapeDtypeStruct((count_rows, width), jnp.bfloat16),
            jax.ShapeDtypeStruct((count_rows, width), jnp.bfloat16),
        ),
        in_specs=[smem, smem, vmem, vmem],
        out_specs=(vmem, vmem),
    )(theirs, valid[0], tokens[0], norm_gain.reshape(1, width))

    offsets = list(range(-BAND, BAND + 1))
    blocks = block_index + jnp.array(offsets, dtype=jnp.int32)
    needed = jnp.any(stops[0, 0][None, :] == blocks[:, None], axis=1)
    cosine, signed = angle_tables(blocks, count_rows, head_dim)
    scales = (head_scale / math.sqrt(head_dim)).astype(jnp.float32)
    own = offsets.index(0)
    table_spec = pl.BlockSpec((None, count_rows, 128), lambda i: (own, 0, 0))

    queries = pl.pallas_call(
        make_query_kernel(head_dim),
        out_shape=jax.ShapeDtypeStruct((count_rows, width), jnp.bfloat16),
        grid=(1,),
        in_specs=[full_spec((count_rows, width)), full_spec((width, width)), table_spec, table_spec],
        out_specs=full_spec((count_rows, width)),
    )(normed, query_weight, cosine, signed)

    slots = len(offsets)
    received = [partner(payload, "ep", 0) if d == 0 else across(payload, d) for d in offsets]
    reads = stops.shape[-1]
    flags = needed.astype(jnp.int32)
    place = jnp.cumsum(flags) - flags
    out = pl.pallas_call(
        make_band_kernel(slots, reads, heads, head_dim, count_rows, width),
        out_shape=jax.ShapeDtypeStruct((count_rows, width), jnp.bfloat16),
        in_specs=[smem, smem, smem] + [vmem] * (1 + slots + 6),
        out_specs=vmem,
        scratch_shapes=[
            pltpu.VMEM((reads * count_rows, width), jnp.bfloat16),
            pltpu.VMEM((reads * count_rows, width), jnp.bfloat16),
        ],
    )(flags, place, scales, queries, *received, cosine, signed, w_key, w_value, w_out, tokens[0])
    return out[None]


def solution(mesh):
    in_specs = (
        P("ep", ("grp", "tok"), None),
        P(),
        P(),
        P(),
        P(),
        P(),
        P(),
        P("ep", ("grp", "tok")),
        P("ep", ("grp", "tok")),
        P("ep", ("grp", "tok"), None),
    )
    out_specs = P("ep", ("grp", "tok"), None)
    return jax.shard_map(
        on_device, mesh=mesh, in_specs=in_specs, out_specs=out_specs, check_vma=False
    )
```

```python
import math

import jax
import jax.numpy as jnp
from jax import lax
from jax.experimental import pallas as pl
from jax.experimental.pallas import tpu as pltpu
from jax.sharding import PartitionSpec as P

BAND = 3
ROW_PATCHES = 1024
META_ROWS = 8
NEG = -1e30


def partner(block, axis, apart):
    count = lax.axis_size(axis)
    route = []
    for low in range(count):
        high = low | 1 << apart
        if high != low and high < count:
            route += [(low, high), (high, low)]
    return lax.ppermute(block, axis, route)


def layer_norm(floated, norm_gain):
    center = jnp.mean(floated, axis=-1, keepdims=True)
    spread = jnp.mean((floated - center) ** 2, axis=-1, keepdims=True)
    return (floated - center) * lax.rsqrt(spread + 1e-05) * norm_gain


def turn_pairs(part, angle):
    quarter = part.shape[-1] // 2
    first = part[..., :quarter]
    second = part[..., quarter:]
    cosine = jnp.cos(angle)[:, None, :]
    sine = jnp.sin(angle)[:, None, :]
    return jnp.concatenate(
        [first * cosine - second * sine, second * cosine + first * sine], axis=-1
    )


def frequencies(quarter):
    return 100.0 ** (-jnp.arange(quarter, dtype=jnp.float32) / quarter)


def rotate(values, patch_coordinates, heads):
    count_rows, width = values.shape
    head_dim = width // heads
    half = head_dim // 2
    quarter = head_dim // 4
    split = values.reshape(count_rows, heads, head_dim)
    row_coordinate = (patch_coordinates // ROW_PATCHES).astype(jnp.float32)
    column_coordinate = (patch_coordinates % ROW_PATCHES).astype(jnp.float32)
    freqs = frequencies(quarter)
    turned = jnp.concatenate(
        [
            turn_pairs(split[..., :half], row_coordinate[:, None] * freqs[None, :]),
            turn_pairs(split[..., half:], column_coordinate[:, None] * freqs[None, :]),
        ],
        axis=-1,
    )
    return turned.reshape(count_rows, width)


def angle_tables(blocks, count_rows, head_dim):
    half = head_dim // 2
    quarter = head_dim // 4
    lanes = jnp.arange(128, dtype=jnp.int32)
    spots = blocks[:, None] * count_rows + jnp.arange(count_rows, dtype=jnp.int32)[None, :]
    row_coordinate = (spots // ROW_PATCHES).astype(jnp.float32)
    column_coordinate = (spots % ROW_PATCHES).astype(jnp.float32)
    in_row_part = (lanes % head_dim) < half
    coordinate = jnp.where(
        in_row_part[None, None, :], row_coordinate[:, :, None], column_coordinate[:, :, None]
    )
    freq_lane = jnp.tile(frequencies(quarter), 128 // quarter)
    angle = coordinate * freq_lane[None, None, :]
    first = (lanes % half) < quarter
    cosine = jnp.cos(angle)
    sine = jnp.sin(angle)
    signed = jnp.where(first[None, None, :], -sine, sine)
    return cosine, signed


def make_band_kernel(slots, reads, heads, head_dim, count_rows, width):
    pairs = width // 128
    quarter = head_dim // 4
    per_pair = 128 // head_dim
    stacked = per_pair * count_rows

    def kernel(needed_ref, place_ref, scale_ref, q_ref, *rest):
        payload_refs = rest[:slots]
        (cos_ref, sin_ref, wk_ref, wv_ref, wo_ref, tok_ref, out_ref, k_buf, v_buf,
         r_buf, c_buf, s_buf) = rest[slots:]
        lane = lax.broadcasted_iota(jnp.int32, (count_rows, 128), 1)
        first = (lane % (2 * quarter)) < quarter
        head_of_lane = lane // head_dim
        row = lax.broadcasted_iota(jnp.int32, (stacked, 1), 0)

        for slot in range(slots):

            @pl.when(needed_ref[slot] != 0)
            def _():
                at = pl.ds(pl.multiple_of(place_ref[slot] * count_rows, count_rows), count_rows)
                r_buf[at, :] = payload_refs[slot][...]
                c_buf[at, :] = cos_ref[slot]
                s_buf[at, :] = sin_ref[slot]

        rows = r_buf[...]
        kp = jnp.dot(rows, wk_ref[...], preferred_element_type=jnp.float32)
        vp = jnp.dot(rows, wv_ref[...], preferred_element_type=jnp.float32)
        v_buf[...] = jnp.where(jnp.abs(vp) < jnp.inf, vp, jnp.float32(0)).astype(jnp.bfloat16)
        cosine = c_buf[...]
        signed = s_buf[...]
        lane_k = lax.broadcasted_iota(jnp.int32, (reads * count_rows, 128), 1)
        first_k = (lane_k % (2 * quarter)) < quarter
        for p in range(pairs):
            lo = p * 128
            x = kp[:, lo:lo + 128]
            other = jnp.where(first_k, pltpu.roll(x, 128 - quarter, 1), pltpu.roll(x, quarter, 1))
            k_buf[:, lo:lo + 128] = (x * cosine + other * signed).astype(jnp.bfloat16)

        parts = []
        for p in range(pairs):
            lo = p * 128
            q_pair = q_ref[:, lo:lo + 128]
            q_two = jnp.concatenate(
                [jnp.where(head_of_lane == sub, q_pair, jnp.zeros_like(q_pair))
                 for sub in range(per_pair)], axis=0)
            scale_col = jnp.zeros((stacked, 1), jnp.float32)
            for sub in range(per_pair):
                scale_col = jnp.where(row // count_rows == sub, scale_ref[p * per_pair + sub], scale_col)
            scores = lax.dot_general(
                q_two, k_buf[:, lo:lo + 128], (((1,), (1,)), ((), ())),
                preferred_element_type=jnp.float32,
            ) * scale_col
            scores = jnp.where(jnp.abs(scores) < jnp.inf, scores, jnp.float32(NEG))
            best = jnp.max(scores, axis=1, keepdims=True)
            weights = jnp.exp(scores - best)
            total = jnp.sum(weights, axis=1, keepdims=True)
            summed = jnp.dot(weights.astype(jnp.bfloat16), v_buf[:, lo:lo + 128],
                             preferred_element_type=jnp.float32)
            two = summed / total
            res = two[0:count_rows]
            for sub in range(1, per_pair):
                res = jnp.where(head_of_lane == sub, two[sub * count_rows:(sub + 1) * count_rows], res)
            parts.append(res.astype(jnp.bfloat16))
        attended = jnp.concatenate(parts, axis=1)
        mixed = tok_ref[...].astype(jnp.float32) + jnp.dot(
            attended, wo_ref[...], preferred_element_type=jnp.float32
        )
        out_ref[...] = mixed.astype(out_ref.dtype)

    return kernel


def make_query_kernel(head_dim):
    quarter = head_dim // 4

    def kernel(x_ref, w_ref, cos_ref, sin_ref, out_ref):
        proj = jnp.dot(x_ref[...], w_ref[...], preferred_element_type=jnp.float32)
        lane = lax.broadcasted_iota(jnp.int32, (proj.shape[0], 128), 1)
        first = (lane % (2 * quarter)) < quarter
        cosine = cos_ref[...]
        signed = sin_ref[...]
        for p in range(proj.shape[1] // 128):
            lo = p * 128
            x = proj[:, lo:lo + 128]
            other = jnp.where(first, pltpu.roll(x, 128 - quarter, 1), pltpu.roll(x, quarter, 1))
            out_ref[:, lo:lo + 128] = (x * cosine + other * signed).astype(out_ref.dtype)

    return kernel


def make_prep_kernel(tile_count, tile_rows, count_rows):
    def kernel(order_ref, count_ref, tok_ref, gain_ref, normed_ref, out_ref):
        floated = tok_ref[...].astype(jnp.float32)
        normed_ref[...] = layer_norm(floated, gain_ref[...]).astype(normed_ref.dtype)
        row = lax.broadcasted_iota(jnp.int32, (tile_rows, 1), 0)
        for s in range(tile_count):
            src = order_ref[s]
            start = pl.multiple_of(src * tile_rows, tile_rows)
            rows = normed_ref[pl.ds(start, tile_rows), :]
            out_ref[s * tile_rows:(s + 1) * tile_rows, :] = jnp.where(
                row < count_ref[src], rows, jnp.asarray(jnp.inf, rows.dtype))

    return kernel


def across(shard, by):
    size = lax.axis_size("tok")
    epochs = lax.axis_size("ep")
    pairs = [
        ((i + by) * epochs + (epochs - 1 - e), i * epochs + e)
        for i in range(size)
        for e in range(epochs)
        if 0 <= i + by < size
    ]
    return lax.ppermute(shard, ("tok", "ep"), pairs)


def full_spec(shape):
    return pl.BlockSpec(shape, lambda i: (0,) * len(shape))


def on_device(
    tokens, norm_gain, query_weight, w_key, w_value, w_out, head_scale, matching, valid, stops
):
    count_rows, width = tokens.shape[1:]
    heads = head_scale.shape[0]
    head_dim = width // heads
    block_index = lax.axis_index("tok")
    smem = pl.BlockSpec(memory_space=pltpu.SMEM)
    vmem = pl.BlockSpec(memory_space=pltpu.VMEM)
    theirs = partner(matching[0], "ep", 0)
    tile_count = matching.shape[1]
    tile_rows = count_rows // tile_count
    normed, payload = pl.pallas_call(
        make_prep_kernel(tile_count, tile_rows, count_rows),
        out_shape=(
            jax.ShapeDtypeStruct((count_rows, width), jnp.bfloat16),
            jax.ShapeDtypeStruct((count_rows, width), jnp.bfloat16),
        ),
        in_specs=[smem, smem, vmem, vmem],
        out_specs=(vmem, vmem),
    )(theirs, valid[0], tokens[0], norm_gain.reshape(1, width))

    offsets = list(range(-BAND, BAND + 1))
    blocks = block_index + jnp.array(offsets, dtype=jnp.int32)
    needed = jnp.any(stops[0, 0][None, :] == blocks[:, None], axis=1)
    cosine, signed = angle_tables(blocks, count_rows, head_dim)
    scales = (head_scale / math.sqrt(head_dim)).astype(jnp.float32)
    own = offsets.index(0)
    table_spec = pl.BlockSpec((None, count_rows, 128), lambda i: (own, 0, 0))

    queries = pl.pallas_call(
        make_query_kernel(head_dim),
        out_shape=jax.ShapeDtypeStruct((count_rows, width), jnp.bfloat16),
        grid=(1,),
        in_specs=[full_spec((count_rows, width)), full_spec((width, width)), table_spec, table_spec],
        out_specs=full_spec((count_rows, width)),
    )(normed, query_weight, cosine, signed)

    slots = len(offsets)
    received = [partner(payload, "ep", 0) if d == 0 else across(payload, d) for d in offsets]
    reads = stops.shape[-1]
    flags = needed.astype(jnp.int32)
    place = jnp.cumsum(flags) - flags
    out = pl.pallas_call(
        make_band_kernel(slots, reads, heads, head_dim, count_rows, width),
        out_shape=jax.ShapeDtypeStruct((count_rows, width), jnp.bfloat16),
        in_specs=[smem, smem, smem] + [vmem] * (1 + slots + 6),
        out_specs=vmem,
        scratch_shapes=[
            pltpu.VMEM((reads * count_rows, width), jnp.bfloat16),
            pltpu.VMEM((reads * count_rows, width), jnp.bfloat16),
            pltpu.VMEM((reads * count_rows, width), jnp.bfloat16),
            pltpu.VMEM((reads * count_rows, 128), jnp.float32),
            pltpu.VMEM((reads * count_rows, 128), jnp.float32),
        ],
    )(flags, place, scales, queries, *received, cosine, signed, w_key, w_value, w_out, tokens[0])
    return out[None]


def solution(mesh):
    in_specs = (
        P("ep", ("grp", "tok"), None),
        P(),
        P(),
        P(),
        P(),
        P(),
        P(),
        P("ep", ("grp", "tok")),
        P("ep", ("grp", "tok")),
        P("ep", ("grp", "tok"), None),
    )
    out_specs = P("ep", ("grp", "tok"), None)
    return jax.shard_map(
        on_device, mesh=mesh, in_specs=in_specs, out_specs=out_specs, check_vma=False
    )
```

```python
import math

import jax
import jax.numpy as jnp
from jax import lax
from jax.experimental import pallas as pl
from jax.experimental.pallas import tpu as pltpu
from jax.sharding import PartitionSpec as P

BAND = 3
ROW_PATCHES = 1024
META_ROWS = 8
NEG = -1e30


def partner(block, axis, apart):
    count = lax.axis_size(axis)
    route = []
    for low in range(count):
        high = low | 1 << apart
        if high != low and high < count:
            route += [(low, high), (high, low)]
    return lax.ppermute(block, axis, route)


def layer_norm(floated, norm_gain):
    center = jnp.mean(floated, axis=-1, keepdims=True)
    spread = jnp.mean((floated - center) ** 2, axis=-1, keepdims=True)
    return (floated - center) * lax.rsqrt(spread + 1e-05) * norm_gain


def turn_pairs(part, angle):
    quarter = part.shape[-1] // 2
    first = part[..., :quarter]
    second = part[..., quarter:]
    cosine = jnp.cos(angle)[:, None, :]
    sine = jnp.sin(angle)[:, None, :]
    return jnp.concatenate(
        [first * cosine - second * sine, second * cosine + first * sine], axis=-1
    )


def frequencies(quarter):
    return 100.0 ** (-jnp.arange(quarter, dtype=jnp.float32) / quarter)


def rotate(values, patch_coordinates, heads):
    count_rows, width = values.shape
    head_dim = width // heads
    half = head_dim // 2
    quarter = head_dim // 4
    split = values.reshape(count_rows, heads, head_dim)
    row_coordinate = (patch_coordinates // ROW_PATCHES).astype(jnp.float32)
    column_coordinate = (patch_coordinates % ROW_PATCHES).astype(jnp.float32)
    freqs = frequencies(quarter)
    turned = jnp.concatenate(
        [
            turn_pairs(split[..., :half], row_coordinate[:, None] * freqs[None, :]),
            turn_pairs(split[..., half:], column_coordinate[:, None] * freqs[None, :]),
        ],
        axis=-1,
    )
    return turned.reshape(count_rows, width)


def angle_tables(blocks, count_rows, head_dim):
    half = head_dim // 2
    quarter = head_dim // 4
    lanes = jnp.arange(128, dtype=jnp.int32)
    spots = blocks[:, None] * count_rows + jnp.arange(count_rows, dtype=jnp.int32)[None, :]
    row_coordinate = (spots // ROW_PATCHES).astype(jnp.float32)
    column_coordinate = (spots % ROW_PATCHES).astype(jnp.float32)
    in_row_part = (lanes % head_dim) < half
    coordinate = jnp.where(
        in_row_part[None, None, :], row_coordinate[:, :, None], column_coordinate[:, :, None]
    )
    freq_lane = jnp.tile(frequencies(quarter), 128 // quarter)
    angle = coordinate * freq_lane[None, None, :]
    first = (lanes % half) < quarter
    cosine = jnp.cos(angle)
    sine = jnp.sin(angle)
    signed = jnp.where(first[None, None, :], -sine, sine)
    return cosine, signed


def rotate_keys(kp, cosine, signed, k_ref, quarter):
    lane = lax.broadcasted_iota(jnp.int32, (kp.shape[0], 128), 1)
    first = (lane % (2 * quarter)) < quarter
    for p in range(kp.shape[1] // 128):
        lo = p * 128
        x = kp[:, lo:lo + 128]
        other = jnp.where(first, pltpu.roll(x, 128 - quarter, 1), pltpu.roll(x, quarter, 1))
        k_ref[:, lo:lo + 128] = (x * cosine + other * signed).astype(k_ref.dtype)


def finite_values(vp):
    return jnp.where(jnp.abs(vp) < jnp.inf, vp, jnp.float32(0)).astype(jnp.bfloat16)


def make_project_kernel(slots, late, head_dim, count_rows):
    quarter = head_dim // 4
    early = [slot for slot in range(slots) if slot != late]

    def kernel(needed_ref, place_ref, *rest):
        payload_refs = rest[:len(early)]
        cos_ref, sin_ref, wk_ref, wv_ref, k_out, v_out, r_buf, c_buf, s_buf = rest[len(early):]
        for pref, slot in zip(payload_refs, early):

            @pl.when(needed_ref[slot] != 0)
            def _():
                at = pl.ds(pl.multiple_of(place_ref[slot] * count_rows, count_rows), count_rows)
                r_buf[at, :] = pref[...]
                c_buf[at, :] = cos_ref[slot]
                s_buf[at, :] = sin_ref[slot]

        rows = r_buf[...]
        kp = jnp.dot(rows, wk_ref[...], preferred_element_type=jnp.float32)
        vp = jnp.dot(rows, wv_ref[...], preferred_element_type=jnp.float32)
        v_out[...] = finite_values(vp)
        rotate_keys(kp, c_buf[...], s_buf[...], k_out, quarter)

    return kernel


def make_band_kernel(late, heads, head_dim, count_rows, width):
    pairs = width // 128
    quarter = head_dim // 4
    per_pair = 128 // head_dim
    stacked = per_pair * count_rows

    def kernel(needed_ref, place_ref, scale_ref, q_ref, pay_ref, cos_ref, sin_ref, wk_ref, wv_ref,
               wo_ref, tok_ref, k_in, v_in, out_ref, k_buf, v_buf):
        lane = lax.broadcasted_iota(jnp.int32, (count_rows, 128), 1)
        head_of_lane = lane // head_dim
        row = lax.broadcasted_iota(jnp.int32, (stacked, 1), 0)
        k_buf[...] = k_in[...]
        v_buf[...] = v_in[...]

        @pl.when(needed_ref[late] != 0)
        def _():
            at = pl.ds(pl.multiple_of(place_ref[late] * count_rows, count_rows), count_rows)
            rows = pay_ref[...]
            kp = jnp.dot(rows, wk_ref[...], preferred_element_type=jnp.float32)
            vp = jnp.dot(rows, wv_ref[...], preferred_element_type=jnp.float32)
            v_buf[at, :] = finite_values(vp)
            rotate_keys(kp, cos_ref[late], sin_ref[late], k_buf.at[at], quarter)

        parts = []
        for p in range(pairs):
            lo = p * 128
            q_pair = q_ref[:, lo:lo + 128]
            q_two = jnp.concatenate(
                [jnp.where(head_of_lane == sub, q_pair, jnp.zeros_like(q_pair))
                 for sub in range(per_pair)], axis=0)
            scale_col = jnp.zeros((stacked, 1), jnp.float32)
            for sub in range(per_pair):
                scale_col = jnp.where(row // count_rows == sub, scale_ref[p * per_pair + sub], scale_col)
            scores = lax.dot_general(
                q_two, k_buf[:, lo:lo + 128], (((1,), (1,)), ((), ())),
                preferred_element_type=jnp.float32,
            ) * scale_col
            scores = jnp.where(jnp.abs(scores) < jnp.inf, scores, jnp.float32(NEG))
            best = jnp.max(scores, axis=1, keepdims=True)
            weights = jnp.exp(scores - best)
            total = jnp.sum(weights, axis=1, keepdims=True)
            summed = jnp.dot(weights.astype(jnp.bfloat16), v_buf[:, lo:lo + 128],
                             preferred_element_type=jnp.float32)
            two = summed / total
            res = two[0:count_rows]
            for sub in range(1, per_pair):
                res = jnp.where(head_of_lane == sub, two[sub * count_rows:(sub + 1) * count_rows], res)
            parts.append(res.astype(jnp.bfloat16))
        attended = jnp.concatenate(parts, axis=1)
        mixed = tok_ref[...].astype(jnp.float32) + jnp.dot(
            attended, wo_ref[...], preferred_element_type=jnp.float32
        )
        out_ref[...] = mixed.astype(out_ref.dtype)

    return kernel


def make_query_kernel(head_dim):
    quarter = head_dim // 4

    def kernel(x_ref, w_ref, cos_ref, sin_ref, out_ref):
        proj = jnp.dot(x_ref[...], w_ref[...], preferred_element_type=jnp.float32)
        lane = lax.broadcasted_iota(jnp.int32, (proj.shape[0], 128), 1)
        first = (lane % (2 * quarter)) < quarter
        cosine = cos_ref[...]
        signed = sin_ref[...]
        for p in range(proj.shape[1] // 128):
            lo = p * 128
            x = proj[:, lo:lo + 128]
            other = jnp.where(first, pltpu.roll(x, 128 - quarter, 1), pltpu.roll(x, quarter, 1))
            out_ref[:, lo:lo + 128] = (x * cosine + other * signed).astype(out_ref.dtype)

    return kernel


def make_prep_kernel(tile_count, tile_rows, count_rows):
    def kernel(order_ref, count_ref, tok_ref, gain_ref, normed_ref, out_ref):
        floated = tok_ref[...].astype(jnp.float32)
        normed_ref[...] = layer_norm(floated, gain_ref[...]).astype(normed_ref.dtype)
        row = lax.broadcasted_iota(jnp.int32, (tile_rows, 1), 0)
        for s in range(tile_count):
            src = order_ref[s]
            start = pl.multiple_of(src * tile_rows, tile_rows)
            rows = normed_ref[pl.ds(start, tile_rows), :]
            out_ref[s * tile_rows:(s + 1) * tile_rows, :] = jnp.where(
                row < count_ref[src], rows, jnp.asarray(jnp.inf, rows.dtype))

    return kernel


def across(shard, by):
    size = lax.axis_size("tok")
    epochs = lax.axis_size("ep")
    pairs = [
        ((i + by) * epochs + (epochs - 1 - e), i * epochs + e)
        for i in range(size)
        for e in range(epochs)
        if 0 <= i + by < size
    ]
    return lax.ppermute(shard, ("tok", "ep"), pairs)


def full_spec(shape):
    return pl.BlockSpec(shape, lambda i: (0,) * len(shape))


def on_device(
    tokens, norm_gain, query_weight, w_key, w_value, w_out, head_scale, matching, valid, stops
):
    count_rows, width = tokens.shape[1:]
    heads = head_scale.shape[0]
    head_dim = width // heads
    block_index = lax.axis_index("tok")
    smem = pl.BlockSpec(memory_space=pltpu.SMEM)
    vmem = pl.BlockSpec(memory_space=pltpu.VMEM)
    theirs = partner(matching[0], "ep", 0)
    tile_count = matching.shape[1]
    tile_rows = count_rows // tile_count
    normed, payload = pl.pallas_call(
        make_prep_kernel(tile_count, tile_rows, count_rows),
        out_shape=(
            jax.ShapeDtypeStruct((count_rows, width), jnp.bfloat16),
            jax.ShapeDtypeStruct((count_rows, width), jnp.bfloat16),
        ),
        in_specs=[smem, smem, vmem, vmem],
        out_specs=(vmem, vmem),
    )(theirs, valid[0], tokens[0], norm_gain.reshape(1, width))

    offsets = list(range(-BAND, BAND + 1))
    blocks = block_index + jnp.array(offsets, dtype=jnp.int32)
    needed = jnp.any(stops[0, 0][None, :] == blocks[:, None], axis=1)
    cosine, signed = angle_tables(blocks, count_rows, head_dim)
    scales = (head_scale / math.sqrt(head_dim)).astype(jnp.float32)
    own = offsets.index(0)
    table_spec = pl.BlockSpec((None, count_rows, 128), lambda i: (own, 0, 0))

    queries = pl.pallas_call(
        make_query_kernel(head_dim),
        out_shape=jax.ShapeDtypeStruct((count_rows, width), jnp.bfloat16),
        grid=(1,),
        in_specs=[full_spec((count_rows, width)), full_spec((width, width)), table_spec, table_spec],
        out_specs=full_spec((count_rows, width)),
    )(normed, query_weight, cosine, signed)

    slots = len(offsets)
    received = [partner(payload, "ep", 0) if d == 0 else across(payload, d) for d in offsets]
    reads = stops.shape[-1]
    flags = needed.astype(jnp.int32)
    place = jnp.cumsum(flags) - flags
    late = offsets.index(-BAND)
    packed = (reads * count_rows, width)
    keys, values = pl.pallas_call(
        make_project_kernel(slots, late, head_dim, count_rows),
        out_shape=(jax.ShapeDtypeStruct(packed, jnp.bfloat16), jax.ShapeDtypeStruct(packed, jnp.bfloat16)),
        in_specs=[smem, smem] + [vmem] * (slots - 1 + 4),
        out_specs=(vmem, vmem),
        scratch_shapes=[
            pltpu.VMEM(packed, jnp.bfloat16),
            pltpu.VMEM((reads * count_rows, 128), jnp.float32),
            pltpu.VMEM((reads * count_rows, 128), jnp.float32),
        ],
    )(flags, place, *[r for i, r in enumerate(received) if i != late], cosine, signed, w_key, w_value)
    out = pl.pallas_call(
        make_band_kernel(late, heads, head_dim, count_rows, width),
        out_shape=jax.ShapeDtypeStruct((count_rows, width), jnp.bfloat16),
        in_specs=[smem, smem, smem] + [vmem] * 10,
        out_specs=vmem,
        scratch_shapes=[pltpu.VMEM(packed, jnp.bfloat16), pltpu.VMEM(packed, jnp.bfloat16)],
    )(flags, place, scales, queries, received[late], cosine, signed, w_key, w_value, w_out,
      tokens[0], keys, values)
    return out[None]


def solution(mesh):
    in_specs = (
        P("ep", ("grp", "tok"), None),
        P(),
        P(),
        P(),
        P(),
        P(),
        P(),
        P("ep", ("grp", "tok")),
        P("ep", ("grp", "tok")),
        P("ep", ("grp", "tok"), None),
    )
    out_specs = P("ep", ("grp", "tok"), None)
    return jax.shard_map(
        on_device, mesh=mesh, in_specs=in_specs, out_specs=out_specs, check_vma=False
    )
```

```python
import math

import jax
import jax.numpy as jnp
from jax import lax
from jax.experimental import pallas as pl
from jax.experimental.pallas import tpu as pltpu
from jax.sharding import PartitionSpec as P

BAND = 3
ROW_PATCHES = 1024
META_ROWS = 8
NEG = -1e30


def partner(block, axis, apart):
    count = lax.axis_size(axis)
    route = []
    for low in range(count):
        high = low | 1 << apart
        if high != low and high < count:
            route += [(low, high), (high, low)]
    return lax.ppermute(block, axis, route)


def layer_norm(floated, norm_gain):
    center = jnp.mean(floated, axis=-1, keepdims=True)
    spread = jnp.mean((floated - center) ** 2, axis=-1, keepdims=True)
    return (floated - center) * lax.rsqrt(spread + 1e-05) * norm_gain


def turn_pairs(part, angle):
    quarter = part.shape[-1] // 2
    first = part[..., :quarter]
    second = part[..., quarter:]
    cosine = jnp.cos(angle)[:, None, :]
    sine = jnp.sin(angle)[:, None, :]
    return jnp.concatenate(
        [first * cosine - second * sine, second * cosine + first * sine], axis=-1
    )


def frequencies(quarter):
    return 100.0 ** (-jnp.arange(quarter, dtype=jnp.float32) / quarter)


def rotate(values, patch_coordinates, heads):
    count_rows, width = values.shape
    head_dim = width // heads
    half = head_dim // 2
    quarter = head_dim // 4
    split = values.reshape(count_rows, heads, head_dim)
    row_coordinate = (patch_coordinates // ROW_PATCHES).astype(jnp.float32)
    column_coordinate = (patch_coordinates % ROW_PATCHES).astype(jnp.float32)
    freqs = frequencies(quarter)
    turned = jnp.concatenate(
        [
            turn_pairs(split[..., :half], row_coordinate[:, None] * freqs[None, :]),
            turn_pairs(split[..., half:], column_coordinate[:, None] * freqs[None, :]),
        ],
        axis=-1,
    )
    return turned.reshape(count_rows, width)


def angle_tables(blocks, count_rows, head_dim):
    half = head_dim // 2
    quarter = head_dim // 4
    lanes = jnp.arange(128, dtype=jnp.int32)
    spots = blocks[:, None] * count_rows + jnp.arange(count_rows, dtype=jnp.int32)[None, :]
    row_coordinate = (spots // ROW_PATCHES).astype(jnp.float32)
    column_coordinate = (spots % ROW_PATCHES).astype(jnp.float32)
    in_row_part = (lanes % head_dim) < half
    coordinate = jnp.where(
        in_row_part[None, None, :], row_coordinate[:, :, None], column_coordinate[:, :, None]
    )
    freq_lane = jnp.tile(frequencies(quarter), 128 // quarter)
    angle = coordinate * freq_lane[None, None, :]
    first = (lanes % half) < quarter
    cosine = jnp.cos(angle)
    sine = jnp.sin(angle)
    signed = jnp.where(first[None, None, :], -sine, sine)
    return cosine, signed


def make_band_kernel(slots, reads, heads, head_dim, count_rows, width):
    pairs = width // 128
    quarter = head_dim // 4
    per_pair = 128 // head_dim
    stacked = per_pair * count_rows

    def kernel(needed_ref, place_ref, scale_ref, q_ref, *rest):
        payload_hbm = rest[:slots]
        (cos_ref, sin_ref, wk_ref, wv_ref, wo_hbm, tok_ref, out_ref, k_buf, v_buf,
         r_buf, c_buf, s_buf, wo_ref, sems) = rest[slots:]
        wo_copy = pltpu.make_async_copy(wo_hbm, wo_ref, sems.at[slots])
        wo_copy.start()
        copies = []
        for slot in range(slots):
            at = pl.ds(pl.multiple_of(place_ref[slot] * count_rows, count_rows), count_rows)
            copies.append(pltpu.make_async_copy(payload_hbm[slot], r_buf.at[at], sems.at[slot]))

            @pl.when(needed_ref[slot] != 0)
            def _():
                copies[slot].start()

        lane = lax.broadcasted_iota(jnp.int32, (count_rows, 128), 1)
        first = (lane % (2 * quarter)) < quarter
        head_of_lane = lane // head_dim
        row = lax.broadcasted_iota(jnp.int32, (stacked, 1), 0)

        for slot in range(slots):

            @pl.when(needed_ref[slot] != 0)
            def _():
                at = pl.ds(pl.multiple_of(place_ref[slot] * count_rows, count_rows), count_rows)
                c_buf[at, :] = cos_ref[slot]
                s_buf[at, :] = sin_ref[slot]

        for slot in range(slots):

            @pl.when(needed_ref[slot] != 0)
            def _():
                copies[slot].wait()

        rows = r_buf[...]
        kp = jnp.dot(rows, wk_ref[...], preferred_element_type=jnp.float32)
        vp = jnp.dot(rows, wv_ref[...], preferred_element_type=jnp.float32)
        v_buf[...] = jnp.where(jnp.abs(vp) < jnp.inf, vp, jnp.float32(0)).astype(jnp.bfloat16)
        cosine = c_buf[...]
        signed = s_buf[...]
        lane_k = lax.broadcasted_iota(jnp.int32, (reads * count_rows, 128), 1)
        first_k = (lane_k % (2 * quarter)) < quarter
        for p in range(pairs):
            lo = p * 128
            x = kp[:, lo:lo + 128]
            other = jnp.where(first_k, pltpu.roll(x, 128 - quarter, 1), pltpu.roll(x, quarter, 1))
            k_buf[:, lo:lo + 128] = (x * cosine + other * signed).astype(jnp.bfloat16)

        parts = []
        for p in range(pairs):
            lo = p * 128
            q_pair = q_ref[:, lo:lo + 128]
            q_two = jnp.concatenate(
                [jnp.where(head_of_lane == sub, q_pair, jnp.zeros_like(q_pair))
                 for sub in range(per_pair)], axis=0)
            scale_col = jnp.zeros((stacked, 1), jnp.float32)
            for sub in range(per_pair):
                scale_col = jnp.where(row // count_rows == sub, scale_ref[p * per_pair + sub], scale_col)
            scores = lax.dot_general(
                q_two, k_buf[:, lo:lo + 128], (((1,), (1,)), ((), ())),
                preferred_element_type=jnp.float32,
            ) * scale_col
            scores = jnp.where(jnp.abs(scores) < jnp.inf, scores, jnp.float32(NEG))
            best = jnp.max(scores, axis=1, keepdims=True)
            weights = jnp.exp(scores - best)
            total = jnp.sum(weights, axis=1, keepdims=True)
            summed = jnp.dot(weights.astype(jnp.bfloat16), v_buf[:, lo:lo + 128],
                             preferred_element_type=jnp.float32)
            two = summed / total
            res = two[0:count_rows]
            for sub in range(1, per_pair):
                res = jnp.where(head_of_lane == sub, two[sub * count_rows:(sub + 1) * count_rows], res)
            parts.append(res.astype(jnp.bfloat16))
        attended = jnp.concatenate(parts, axis=1)
        wo_copy.wait()
        mixed = tok_ref[...].astype(jnp.float32) + jnp.dot(
            attended, wo_ref[...], preferred_element_type=jnp.float32
        )
        out_ref[...] = mixed.astype(out_ref.dtype)

    return kernel


def make_query_kernel(head_dim):
    quarter = head_dim // 4

    def kernel(x_ref, w_ref, cos_ref, sin_ref, out_ref):
        proj = jnp.dot(x_ref[...], w_ref[...], preferred_element_type=jnp.float32)
        lane = lax.broadcasted_iota(jnp.int32, (proj.shape[0], 128), 1)
        first = (lane % (2 * quarter)) < quarter
        cosine = cos_ref[...]
        signed = sin_ref[...]
        for p in range(proj.shape[1] // 128):
            lo = p * 128
            x = proj[:, lo:lo + 128]
            other = jnp.where(first, pltpu.roll(x, 128 - quarter, 1), pltpu.roll(x, quarter, 1))
            out_ref[:, lo:lo + 128] = (x * cosine + other * signed).astype(out_ref.dtype)

    return kernel


def make_prep_kernel(tile_count, tile_rows, count_rows):
    def kernel(order_ref, count_ref, tok_ref, gain_ref, normed_ref, out_ref):
        floated = tok_ref[...].astype(jnp.float32)
        normed_ref[...] = layer_norm(floated, gain_ref[...]).astype(normed_ref.dtype)
        row = lax.broadcasted_iota(jnp.int32, (tile_rows, 1), 0)
        for s in range(tile_count):
            src = order_ref[s]
            start = pl.multiple_of(src * tile_rows, tile_rows)
            rows = normed_ref[pl.ds(start, tile_rows), :]
            out_ref[s * tile_rows:(s + 1) * tile_rows, :] = jnp.where(
                row < count_ref[src], rows, jnp.asarray(jnp.inf, rows.dtype))

    return kernel


def across(shard, by):
    size = lax.axis_size("tok")
    epochs = lax.axis_size("ep")
    pairs = [
        ((i + by) * epochs + (epochs - 1 - e), i * epochs + e)
        for i in range(size)
        for e in range(epochs)
        if 0 <= i + by < size
    ]
    return lax.ppermute(shard, ("tok", "ep"), pairs)


def full_spec(shape):
    return pl.BlockSpec(shape, lambda i: (0,) * len(shape))


def on_device(
    tokens, norm_gain, query_weight, w_key, w_value, w_out, head_scale, matching, valid, stops
):
    count_rows, width = tokens.shape[1:]
    heads = head_scale.shape[0]
    head_dim = width // heads
    block_index = lax.axis_index("tok")
    smem = pl.BlockSpec(memory_space=pltpu.SMEM)
    vmem = pl.BlockSpec(memory_space=pltpu.VMEM)
    hbm = pl.BlockSpec(memory_space=pl.ANY)
    theirs = partner(matching[0], "ep", 0)
    tile_count = matching.shape[1]
    tile_rows = count_rows // tile_count
    normed, payload = pl.pallas_call(
        make_prep_kernel(tile_count, tile_rows, count_rows),
        out_shape=(
            jax.ShapeDtypeStruct((count_rows, width), jnp.bfloat16),
            jax.ShapeDtypeStruct((count_rows, width), jnp.bfloat16),
        ),
        in_specs=[smem, smem, vmem, vmem],
        out_specs=(vmem, vmem),
    )(theirs, valid[0], tokens[0], norm_gain.reshape(1, width))

    offsets = list(range(-BAND, BAND + 1))
    blocks = block_index + jnp.array(offsets, dtype=jnp.int32)
    needed = jnp.any(stops[0, 0][None, :] == blocks[:, None], axis=1)
    cosine, signed = angle_tables(blocks, count_rows, head_dim)
    scales = (head_scale / math.sqrt(head_dim)).astype(jnp.float32)
    own = offsets.index(0)
    table_spec = pl.BlockSpec((None, count_rows, 128), lambda i: (own, 0, 0))

    queries = pl.pallas_call(
        make_query_kernel(head_dim),
        out_shape=jax.ShapeDtypeStruct((count_rows, width), jnp.bfloat16),
        grid=(1,),
        in_specs=[full_spec((count_rows, width)), full_spec((width, width)), table_spec, table_spec],
        out_specs=full_spec((count_rows, width)),
    )(normed, query_weight, cosine, signed)

    slots = len(offsets)
    received = [partner(payload, "ep", 0) if d == 0 else across(payload, d) for d in offsets]
    reads = stops.shape[-1]
    flags = needed.astype(jnp.int32)
    place = jnp.minimum(jnp.cumsum(flags) - flags, reads - 1)
    out = pl.pallas_call(
        make_band_kernel(slots, reads, heads, head_dim, count_rows, width),
        out_shape=jax.ShapeDtypeStruct((count_rows, width), jnp.bfloat16),
        in_specs=[smem, smem, smem, vmem] + [hbm] * slots + [vmem] * 4 + [hbm, vmem],
        out_specs=vmem,
        scratch_shapes=[
            pltpu.VMEM((reads * count_rows, width), jnp.bfloat16),
            pltpu.VMEM((reads * count_rows, width), jnp.bfloat16),
            pltpu.VMEM((reads * count_rows, width), jnp.bfloat16),
            pltpu.VMEM((reads * count_rows, 128), jnp.float32),
            pltpu.VMEM((reads * count_rows, 128), jnp.float32),
            pltpu.VMEM((width, width), jnp.bfloat16),
            pltpu.SemaphoreType.DMA((slots + 1,)),
        ],
    )(flags, place, scales, queries, *received, cosine, signed, w_key, w_value, w_out, tokens[0])
    return out[None]


def solution(mesh):
    in_specs = (
        P("ep", ("grp", "tok"), None),
        P(),
        P(),
        P(),
        P(),
        P(),
        P(),
        P("ep", ("grp", "tok")),
        P("ep", ("grp", "tok")),
        P("ep", ("grp", "tok"), None),
    )
    out_specs = P("ep", ("grp", "tok"), None)
    return jax.shard_map(
        on_device, mesh=mesh, in_specs=in_specs, out_specs=out_specs, check_vma=False
    )
```

```python
import math

import jax
import jax.numpy as jnp
from jax import lax
from jax.experimental import pallas as pl
from jax.experimental.pallas import tpu as pltpu
from jax.sharding import PartitionSpec as P

BAND = 3
ROW_PATCHES = 1024
META_ROWS = 8
NEG = -1e30


def partner(block, axis, apart):
    count = lax.axis_size(axis)
    route = []
    for low in range(count):
        high = low | 1 << apart
        if high != low and high < count:
            route += [(low, high), (high, low)]
    return lax.ppermute(block, axis, route)


def layer_norm(floated, norm_gain):
    center = jnp.mean(floated, axis=-1, keepdims=True)
    spread = jnp.mean((floated - center) ** 2, axis=-1, keepdims=True)
    return (floated - center) * lax.rsqrt(spread + 1e-05) * norm_gain


def turn_pairs(part, angle):
    quarter = part.shape[-1] // 2
    first = part[..., :quarter]
    second = part[..., quarter:]
    cosine = jnp.cos(angle)[:, None, :]
    sine = jnp.sin(angle)[:, None, :]
    return jnp.concatenate(
        [first * cosine - second * sine, second * cosine + first * sine], axis=-1
    )


def frequencies(quarter):
    return 100.0 ** (-jnp.arange(quarter, dtype=jnp.float32) / quarter)


def rotate(values, patch_coordinates, heads):
    count_rows, width = values.shape
    head_dim = width // heads
    half = head_dim // 2
    quarter = head_dim // 4
    split = values.reshape(count_rows, heads, head_dim)
    row_coordinate = (patch_coordinates // ROW_PATCHES).astype(jnp.float32)
    column_coordinate = (patch_coordinates % ROW_PATCHES).astype(jnp.float32)
    freqs = frequencies(quarter)
    turned = jnp.concatenate(
        [
            turn_pairs(split[..., :half], row_coordinate[:, None] * freqs[None, :]),
            turn_pairs(split[..., half:], column_coordinate[:, None] * freqs[None, :]),
        ],
        axis=-1,
    )
    return turned.reshape(count_rows, width)


def angle_tables(blocks, count_rows, head_dim):
    half = head_dim // 2
    quarter = head_dim // 4
    lanes = jnp.arange(128, dtype=jnp.int32)
    spots = blocks[:, None] * count_rows + jnp.arange(count_rows, dtype=jnp.int32)[None, :]
    row_coordinate = (spots // ROW_PATCHES).astype(jnp.float32)
    column_coordinate = (spots % ROW_PATCHES).astype(jnp.float32)
    in_row_part = (lanes % head_dim) < half
    coordinate = jnp.where(
        in_row_part[None, None, :], row_coordinate[:, :, None], column_coordinate[:, :, None]
    )
    freq_lane = jnp.tile(frequencies(quarter), 128 // quarter)
    angle = coordinate * freq_lane[None, None, :]
    first = (lanes % half) < quarter
    cosine = jnp.cos(angle)
    sine = jnp.sin(angle)
    signed = jnp.where(first[None, None, :], -sine, sine)
    return cosine, signed


def make_band_kernel(slots, reads, heads, head_dim, count_rows, width):
    pairs = width // 128
    quarter = head_dim // 4
    per_pair = 128 // head_dim
    stacked = per_pair * count_rows

    def kernel(needed_ref, place_ref, scale_ref, q_ref, *rest):
        payload_refs = rest[:slots]
        (cos_ref, sin_ref, wk_ref, wv_ref, wo_ref, tok_ref, out_ref, k_buf, v_buf,
         r_buf, c_buf, s_buf) = rest[slots:]
        lane = lax.broadcasted_iota(jnp.int32, (count_rows, 128), 1)
        first = (lane % (2 * quarter)) < quarter
        head_of_lane = lane // head_dim
        row = lax.broadcasted_iota(jnp.int32, (stacked, 1), 0)

        for slot in range(slots):

            @pl.when(needed_ref[slot] != 0)
            def _():
                at = pl.ds(pl.multiple_of(place_ref[slot] * count_rows, count_rows), count_rows)
                r_buf[at, :] = payload_refs[slot][...]
                c_buf[at, :] = cos_ref[slot]
                s_buf[at, :] = sin_ref[slot]

        rows = r_buf[...]
        kp = jnp.dot(rows, wk_ref[...], preferred_element_type=jnp.float32)
        vp = jnp.dot(rows, wv_ref[...], preferred_element_type=jnp.float32)
        v_buf[...] = jnp.where(jnp.abs(vp) < jnp.inf, vp, jnp.float32(0)).astype(jnp.bfloat16)
        cosine = c_buf[...]
        signed = s_buf[...]
        lane_k = lax.broadcasted_iota(jnp.int32, (reads * count_rows, 128), 1)
        first_k = (lane_k % (2 * quarter)) < quarter
        for p in range(pairs):
            lo = p * 128
            x = kp[:, lo:lo + 128]
            other = jnp.where(first_k, pltpu.roll(x, 128 - quarter, 1), pltpu.roll(x, quarter, 1))
            k_buf[:, lo:lo + 128] = (x * cosine + other * signed).astype(jnp.bfloat16)

        parts = []
        for p in range(pairs):
            lo = p * 128
            q_pair = q_ref[:, lo:lo + 128]
            q_two = jnp.concatenate(
                [jnp.where(head_of_lane == sub, q_pair, jnp.zeros_like(q_pair))
                 for sub in range(per_pair)], axis=0)
            scale_col = jnp.zeros((stacked, 1), jnp.float32)
            for sub in range(per_pair):
                scale_col = jnp.where(row // count_rows == sub, scale_ref[p * per_pair + sub], scale_col)
            scores = lax.dot_general(
                q_two, k_buf[:, lo:lo + 128], (((1,), (1,)), ((), ())),
                preferred_element_type=jnp.float32,
            ) * scale_col
            scores = jnp.where(jnp.abs(scores) < jnp.inf, scores, jnp.float32(NEG))
            best = jnp.max(scores, axis=1, keepdims=True)
            weights = jnp.exp(scores - best)
            total = jnp.sum(weights, axis=1, keepdims=True)
            summed = jnp.dot(weights.astype(jnp.bfloat16), v_buf[:, lo:lo + 128],
                             preferred_element_type=jnp.float32)
            two = summed / total
            res = two[0:count_rows]
            for sub in range(1, per_pair):
                res = jnp.where(head_of_lane == sub, two[sub * count_rows:(sub + 1) * count_rows], res)
            parts.append(res.astype(jnp.bfloat16))
        attended = jnp.concatenate(parts, axis=1)
        mixed = tok_ref[...].astype(jnp.float32) + jnp.dot(
            attended, wo_ref[...], preferred_element_type=jnp.float32
        )
        out_ref[...] = mixed.astype(out_ref.dtype)

    return kernel


def make_query_kernel(head_dim):
    quarter = head_dim // 4

    def kernel(x_ref, w_ref, cos_ref, sin_ref, out_ref):
        proj = jnp.dot(x_ref[...], w_ref[...], preferred_element_type=jnp.float32)
        lane = lax.broadcasted_iota(jnp.int32, (proj.shape[0], 128), 1)
        first = (lane % (2 * quarter)) < quarter
        cosine = cos_ref[...]
        signed = sin_ref[...]
        for p in range(proj.shape[1] // 128):
            lo = p * 128
            x = proj[:, lo:lo + 128]
            other = jnp.where(first, pltpu.roll(x, 128 - quarter, 1), pltpu.roll(x, quarter, 1))
            out_ref[:, lo:lo + 128] = (x * cosine + other * signed).astype(out_ref.dtype)

    return kernel


def make_prep_kernel(tile_count, tile_rows, count_rows):
    def kernel(order_ref, count_ref, tok_ref, gain_ref, normed_ref, out_ref):
        floated = tok_ref[...].astype(jnp.float32)
        normed_ref[...] = layer_norm(floated, gain_ref[...]).astype(normed_ref.dtype)
        row = lax.broadcasted_iota(jnp.int32, (tile_rows, 1), 0)
        for s in range(tile_count):
            src = order_ref[s]
            start = pl.multiple_of(src * tile_rows, tile_rows)
            rows = normed_ref[pl.ds(start, tile_rows), :]
            out_ref[s * tile_rows:(s + 1) * tile_rows, :] = jnp.where(
                row < count_ref[src], rows, jnp.asarray(jnp.inf, rows.dtype))

    return kernel


def across(shard, by):
    size = lax.axis_size("tok")
    epochs = lax.axis_size("ep")
    pairs = [
        ((i + by) * epochs + (epochs - 1 - e), i * epochs + e)
        for i in range(size)
        for e in range(epochs)
        if 0 <= i + by < size
    ]
    return lax.ppermute(shard, ("tok", "ep"), pairs)


def full_spec(shape):
    return pl.BlockSpec(shape, lambda i: (0,) * len(shape))


def on_device(
    tokens, norm_gain, query_weight, w_key, w_value, w_out, head_scale, matching, valid, stops
):
    count_rows, width = tokens.shape[1:]
    heads = head_scale.shape[0]
    head_dim = width // heads
    block_index = lax.axis_index("tok")
    smem = pl.BlockSpec(memory_space=pltpu.SMEM)
    vmem = pl.BlockSpec(memory_space=pltpu.VMEM)
    theirs = partner(matching[0], "ep", 0)
    tile_count = matching.shape[1]
    tile_rows = count_rows // tile_count
    normed, payload = pl.pallas_call(
        make_prep_kernel(tile_count, tile_rows, count_rows),
        out_shape=(
            jax.ShapeDtypeStruct((count_rows, width), jnp.bfloat16),
            jax.ShapeDtypeStruct((count_rows, width), jnp.bfloat16),
        ),
        in_specs=[smem, smem, vmem, vmem],
        out_specs=(vmem, vmem),
    )(theirs, valid[0], tokens[0], norm_gain.reshape(1, width))

    _, block_index = lax.optimization_barrier((payload, block_index))
    offsets = list(range(-BAND, BAND + 1))
    blocks = block_index + jnp.array(offsets, dtype=jnp.int32)
    needed = jnp.any(stops[0, 0][None, :] == blocks[:, None], axis=1)
    cosine, signed = angle_tables(blocks, count_rows, head_dim)
    scales = (head_scale / math.sqrt(head_dim)).astype(jnp.float32)
    own = offsets.index(0)
    table_spec = pl.BlockSpec((None, count_rows, 128), lambda i: (own, 0, 0))

    queries = pl.pallas_call(
        make_query_kernel(head_dim),
        out_shape=jax.ShapeDtypeStruct((count_rows, width), jnp.bfloat16),
        grid=(1,),
        in_specs=[full_spec((count_rows, width)), full_spec((width, width)), table_spec, table_spec],
        out_specs=full_spec((count_rows, width)),
    )(normed, query_weight, cosine, signed)

    slots = len(offsets)
    received = [partner(payload, "ep", 0) if d == 0 else across(payload, d) for d in offsets]
    reads = stops.shape[-1]
    flags = needed.astype(jnp.int32)
    place = jnp.cumsum(flags) - flags
    out = pl.pallas_call(
        make_band_kernel(slots, reads, heads, head_dim, count_rows, width),
        out_shape=jax.ShapeDtypeStruct((count_rows, width), jnp.bfloat16),
        in_specs=[smem, smem, smem] + [vmem] * (1 + slots + 6),
        out_specs=vmem,
        scratch_shapes=[
            pltpu.VMEM((reads * count_rows, width), jnp.bfloat16),
            pltpu.VMEM((reads * count_rows, width), jnp.bfloat16),
            pltpu.VMEM((reads * count_rows, width), jnp.bfloat16),
            pltpu.VMEM((reads * count_rows, 128), jnp.float32),
            pltpu.VMEM((reads * count_rows, 128), jnp.float32),
        ],
    )(flags, place, scales, queries, *received, cosine, signed, w_key, w_value, w_out, tokens[0])
    return out[None]


def solution(mesh):
    in_specs = (
        P("ep", ("grp", "tok"), None),
        P(),
        P(),
        P(),
        P(),
        P(),
        P(),
        P("ep", ("grp", "tok")),
        P("ep", ("grp", "tok")),
        P("ep", ("grp", "tok"), None),
    )
    out_specs = P("ep", ("grp", "tok"), None)
    return jax.shard_map(
        on_device, mesh=mesh, in_specs=in_specs, out_specs=out_specs, check_vma=False
    )
```

```python
import math

import jax
import jax.numpy as jnp
from jax import lax
from jax.experimental import pallas as pl
from jax.experimental.pallas import tpu as pltpu
from jax.sharding import PartitionSpec as P

BAND = 3
ROW_PATCHES = 1024
META_ROWS = 8
NEG = -1e30


def partner(block, axis, apart):
    count = lax.axis_size(axis)
    route = []
    for low in range(count):
        high = low | 1 << apart
        if high != low and high < count:
            route += [(low, high), (high, low)]
    return lax.ppermute(block, axis, route)


def layer_norm(floated, norm_gain):
    center = jnp.mean(floated, axis=-1, keepdims=True)
    spread = jnp.mean((floated - center) ** 2, axis=-1, keepdims=True)
    return (floated - center) * lax.rsqrt(spread + 1e-05) * norm_gain


def turn_pairs(part, angle):
    quarter = part.shape[-1] // 2
    first = part[..., :quarter]
    second = part[..., quarter:]
    cosine = jnp.cos(angle)[:, None, :]
    sine = jnp.sin(angle)[:, None, :]
    return jnp.concatenate(
        [first * cosine - second * sine, second * cosine + first * sine], axis=-1
    )


def frequencies(quarter):
    return 100.0 ** (-jnp.arange(quarter, dtype=jnp.float32) / quarter)


def rotate(values, patch_coordinates, heads):
    count_rows, width = values.shape
    head_dim = width // heads
    half = head_dim // 2
    quarter = head_dim // 4
    split = values.reshape(count_rows, heads, head_dim)
    row_coordinate = (patch_coordinates // ROW_PATCHES).astype(jnp.float32)
    column_coordinate = (patch_coordinates % ROW_PATCHES).astype(jnp.float32)
    freqs = frequencies(quarter)
    turned = jnp.concatenate(
        [
            turn_pairs(split[..., :half], row_coordinate[:, None] * freqs[None, :]),
            turn_pairs(split[..., half:], column_coordinate[:, None] * freqs[None, :]),
        ],
        axis=-1,
    )
    return turned.reshape(count_rows, width)


def angle_tables(blocks, count_rows, head_dim):
    half = head_dim // 2
    quarter = head_dim // 4
    lanes = jnp.arange(128, dtype=jnp.int32)
    spots = blocks[:, None] * count_rows + jnp.arange(count_rows, dtype=jnp.int32)[None, :]
    row_coordinate = (spots // ROW_PATCHES).astype(jnp.float32)
    column_coordinate = (spots % ROW_PATCHES).astype(jnp.float32)
    in_row_part = (lanes % head_dim) < half
    coordinate = jnp.where(
        in_row_part[None, None, :], row_coordinate[:, :, None], column_coordinate[:, :, None]
    )
    freq_lane = jnp.tile(frequencies(quarter), 128 // quarter)
    angle = coordinate * freq_lane[None, None, :]
    first = (lanes % half) < quarter
    cosine = jnp.cos(angle)
    sine = jnp.sin(angle)
    signed = jnp.where(first[None, None, :], -sine, sine)
    return cosine, signed


def make_band_kernel(slots, reads, heads, head_dim, count_rows, width):
    pairs = width // 128
    quarter = head_dim // 4
    per_pair = 128 // head_dim
    stacked = per_pair * count_rows

    def kernel(needed_ref, place_ref, scale_ref, q_ref, *rest):
        payload_refs = rest[:slots]
        (cos_ref, sin_ref, wk_ref, wv_ref, wo_ref, tok_ref, out_ref, k_buf, v_buf,
         r_buf, c_buf, s_buf) = rest[slots:]
        lane = lax.broadcasted_iota(jnp.int32, (count_rows, 128), 1)
        first = (lane % (2 * quarter)) < quarter
        head_of_lane = lane // head_dim
        row = lax.broadcasted_iota(jnp.int32, (stacked, 1), 0)

        for slot in range(slots):

            @pl.when(needed_ref[slot] != 0)
            def _():
                at = pl.ds(pl.multiple_of(place_ref[slot] * count_rows, count_rows), count_rows)
                r_buf[at, :] = payload_refs[slot][...]
                c_buf[at, :] = cos_ref[slot]
                s_buf[at, :] = sin_ref[slot]

        rows = r_buf[...]
        kp = jnp.dot(rows, wk_ref[...], preferred_element_type=jnp.float32)
        vp = jnp.dot(rows, wv_ref[...], preferred_element_type=jnp.float32)
        v_buf[...] = jnp.where(jnp.abs(vp) < jnp.inf, vp, jnp.float32(0)).astype(jnp.bfloat16)
        cosine = c_buf[...]
        signed = s_buf[...]
        lane_k = lax.broadcasted_iota(jnp.int32, (reads * count_rows, 128), 1)
        first_k = (lane_k % (2 * quarter)) < quarter
        for p in range(pairs):
            lo = p * 128
            x = kp[:, lo:lo + 128]
            other = jnp.where(first_k, pltpu.roll(x, 128 - quarter, 1), pltpu.roll(x, quarter, 1))
            k_buf[:, lo:lo + 128] = (x * cosine + other * signed).astype(jnp.bfloat16)

        parts = []
        for p in range(pairs):
            lo = p * 128
            q_pair = q_ref[:, lo:lo + 128]
            q_two = jnp.concatenate(
                [jnp.where(head_of_lane == sub, q_pair, jnp.zeros_like(q_pair))
                 for sub in range(per_pair)], axis=0)
            scale_col = jnp.zeros((stacked, 1), jnp.float32)
            for sub in range(per_pair):
                scale_col = jnp.where(row // count_rows == sub, scale_ref[p * per_pair + sub], scale_col)
            scores = lax.dot_general(
                q_two, k_buf[:, lo:lo + 128], (((1,), (1,)), ((), ())),
                preferred_element_type=jnp.float32,
            ) * scale_col
            scores = jnp.where(jnp.abs(scores) < jnp.inf, scores, jnp.float32(NEG))
            best = jnp.max(scores, axis=1, keepdims=True)
            weights = jnp.exp(scores - best)
            total = jnp.sum(weights, axis=1, keepdims=True)
            summed = jnp.dot(weights.astype(jnp.bfloat16), v_buf[:, lo:lo + 128],
                             preferred_element_type=jnp.float32)
            two = summed / total
            res = two[0:count_rows]
            for sub in range(1, per_pair):
                res = jnp.where(head_of_lane == sub, two[sub * count_rows:(sub + 1) * count_rows], res)
            parts.append(res.astype(jnp.bfloat16))
        attended = jnp.concatenate(parts, axis=1)
        mixed = tok_ref[...].astype(jnp.float32) + jnp.dot(
            attended, wo_ref[...], preferred_element_type=jnp.float32
        )
        out_ref[...] = mixed.astype(out_ref.dtype)

    return kernel


def make_query_kernel(head_dim):
    quarter = head_dim // 4

    def kernel(x_ref, w_ref, cos_ref, sin_ref, out_ref):
        proj = jnp.dot(x_ref[...], w_ref[...], preferred_element_type=jnp.float32)
        lane = lax.broadcasted_iota(jnp.int32, (proj.shape[0], 128), 1)
        first = (lane % (2 * quarter)) < quarter
        cosine = cos_ref[...]
        signed = sin_ref[...]
        for p in range(proj.shape[1] // 128):
            lo = p * 128
            x = proj[:, lo:lo + 128]
            other = jnp.where(first, pltpu.roll(x, 128 - quarter, 1), pltpu.roll(x, quarter, 1))
            out_ref[:, lo:lo + 128] = (x * cosine + other * signed).astype(out_ref.dtype)

    return kernel


def make_prep_kernel(tile_count, tile_rows, count_rows):
    def kernel(order_ref, count_ref, tok_ref, gain_ref, normed_ref, out_ref):
        floated = tok_ref[...].astype(jnp.float32)
        normed_ref[...] = layer_norm(floated, gain_ref[...]).astype(normed_ref.dtype)
        row = lax.broadcasted_iota(jnp.int32, (tile_rows, 1), 0)
        for s in range(tile_count):
            src = order_ref[s]
            start = pl.multiple_of(src * tile_rows, tile_rows)
            rows = normed_ref[pl.ds(start, tile_rows), :]
            out_ref[s * tile_rows:(s + 1) * tile_rows, :] = jnp.where(
                row < count_ref[src], rows, jnp.asarray(jnp.inf, rows.dtype))

    return kernel


def across(shard, by):
    size = lax.axis_size("tok")
    epochs = lax.axis_size("ep")
    pairs = [
        ((i + by) * epochs + (epochs - 1 - e), i * epochs + e)
        for i in range(size)
        for e in range(epochs)
        if 0 <= i + by < size
    ]
    return lax.ppermute(shard, ("tok", "ep"), pairs)


def full_spec(shape):
    return pl.BlockSpec(shape, lambda i: (0,) * len(shape))


def on_device(
    tokens, norm_gain, query_weight, w_key, w_value, w_out, head_scale, matching, valid, stops
):
    count_rows, width = tokens.shape[1:]
    heads = head_scale.shape[0]
    head_dim = width // heads
    block_index = lax.axis_index("tok")
    smem = pl.BlockSpec(memory_space=pltpu.SMEM)
    vmem = pl.BlockSpec(memory_space=pltpu.VMEM)
    theirs = partner(matching[0], "ep", 0)
    tile_count = matching.shape[1]
    tile_rows = count_rows // tile_count
    normed, payload = pl.pallas_call(
        make_prep_kernel(tile_count, tile_rows, count_rows),
        out_shape=(
            jax.ShapeDtypeStruct((count_rows, width), jnp.bfloat16),
            jax.ShapeDtypeStruct((count_rows, width), jnp.bfloat16),
        ),
        in_specs=[smem, smem, vmem, vmem],
        out_specs=(vmem, vmem),
    )(theirs, valid[0], tokens[0], norm_gain.reshape(1, width))

    offsets = list(range(-BAND, BAND + 1))
    slots = len(offsets)
    received = [partner(payload, "ep", 0) if d == 0 else across(payload, d) for d in offsets]
    own_block = offsets.index(0)
    received[own_block], stops, head_scale, block_index = lax.optimization_barrier(
        (received[own_block], stops, head_scale, block_index))
    blocks = block_index + jnp.array(offsets, dtype=jnp.int32)
    needed = jnp.any(stops[0, 0][None, :] == blocks[:, None], axis=1)
    cosine, signed = angle_tables(blocks, count_rows, head_dim)
    scales = (head_scale / math.sqrt(head_dim)).astype(jnp.float32)
    own = offsets.index(0)
    table_spec = pl.BlockSpec((None, count_rows, 128), lambda i: (own, 0, 0))

    queries = pl.pallas_call(
        make_query_kernel(head_dim),
        out_shape=jax.ShapeDtypeStruct((count_rows, width), jnp.bfloat16),
        grid=(1,),
        in_specs=[full_spec((count_rows, width)), full_spec((width, width)), table_spec, table_spec],
        out_specs=full_spec((count_rows, width)),
    )(normed, query_weight, cosine, signed)

    reads = stops.shape[-1]
    flags = needed.astype(jnp.int32)
    place = jnp.cumsum(flags) - flags
    out = pl.pallas_call(
        make_band_kernel(slots, reads, heads, head_dim, count_rows, width),
        out_shape=jax.ShapeDtypeStruct((count_rows, width), jnp.bfloat16),
        in_specs=[smem, smem, smem] + [vmem] * (1 + slots + 6),
        out_specs=vmem,
        scratch_shapes=[
            pltpu.VMEM((reads * count_rows, width), jnp.bfloat16),
            pltpu.VMEM((reads * count_rows, width), jnp.bfloat16),
            pltpu.VMEM((reads * count_rows, width), jnp.bfloat16),
            pltpu.VMEM((reads * count_rows, 128), jnp.float32),
            pltpu.VMEM((reads * count_rows, 128), jnp.float32),
        ],
    )(flags, place, scales, queries, *received, cosine, signed, w_key, w_value, w_out, tokens[0])
    return out[None]


def solution(mesh):
    in_specs = (
        P("ep", ("grp", "tok"), None),
        P(),
        P(),
        P(),
        P(),
        P(),
        P(),
        P("ep", ("grp", "tok")),
        P("ep", ("grp", "tok")),
        P("ep", ("grp", "tok"), None),
    )
    out_specs = P("ep", ("grp", "tok"), None)
    return jax.shard_map(
        on_device, mesh=mesh, in_specs=in_specs, out_specs=out_specs, check_vma=False
    )
```

```python
import math

import jax
import jax.numpy as jnp
from jax import lax
from jax.experimental import pallas as pl
from jax.experimental.pallas import tpu as pltpu
from jax.sharding import PartitionSpec as P

BAND = 3
ROW_PATCHES = 1024
META_ROWS = 8
NEG = -1e30


def partner(block, axis, apart):
    count = lax.axis_size(axis)
    route = []
    for low in range(count):
        high = low | 1 << apart
        if high != low and high < count:
            route += [(low, high), (high, low)]
    return lax.ppermute(block, axis, route)


def layer_norm(floated, norm_gain):
    center = jnp.mean(floated, axis=-1, keepdims=True)
    spread = jnp.mean((floated - center) ** 2, axis=-1, keepdims=True)
    return (floated - center) * lax.rsqrt(spread + 1e-05) * norm_gain


def turn_pairs(part, angle):
    quarter = part.shape[-1] // 2
    first = part[..., :quarter]
    second = part[..., quarter:]
    cosine = jnp.cos(angle)[:, None, :]
    sine = jnp.sin(angle)[:, None, :]
    return jnp.concatenate(
        [first * cosine - second * sine, second * cosine + first * sine], axis=-1
    )


def frequencies(quarter):
    return 100.0 ** (-jnp.arange(quarter, dtype=jnp.float32) / quarter)


def rotate(values, patch_coordinates, heads):
    count_rows, width = values.shape
    head_dim = width // heads
    half = head_dim // 2
    quarter = head_dim // 4
    split = values.reshape(count_rows, heads, head_dim)
    row_coordinate = (patch_coordinates // ROW_PATCHES).astype(jnp.float32)
    column_coordinate = (patch_coordinates % ROW_PATCHES).astype(jnp.float32)
    freqs = frequencies(quarter)
    turned = jnp.concatenate(
        [
            turn_pairs(split[..., :half], row_coordinate[:, None] * freqs[None, :]),
            turn_pairs(split[..., half:], column_coordinate[:, None] * freqs[None, :]),
        ],
        axis=-1,
    )
    return turned.reshape(count_rows, width)


def angle_tables(blocks, count_rows, head_dim):
    quarter = head_dim // 4
    spots = blocks[:, None] * count_rows + jnp.arange(count_rows, dtype=jnp.int32)[None, :]
    row_coordinate = (spots // ROW_PATCHES).astype(jnp.float32)
    column_coordinate = (spots % ROW_PATCHES).astype(jnp.float32)
    freqs = frequencies(quarter)
    row_angle = row_coordinate[:, :, None] * freqs[None, None, :]
    column_angle = column_coordinate[:, :, None] * freqs[None, None, :]
    row_cos, row_sin = jnp.cos(row_angle), jnp.sin(row_angle)
    column_cos, column_sin = jnp.cos(column_angle), jnp.sin(column_angle)
    cosine = jnp.concatenate([row_cos, row_cos, column_cos, column_cos], axis=-1)
    signed = jnp.concatenate([-row_sin, row_sin, -column_sin, column_sin], axis=-1)
    copies = 128 // head_dim
    return jnp.tile(cosine, (1, 1, copies)), jnp.tile(signed, (1, 1, copies))


def make_band_kernel(slots, reads, heads, head_dim, count_rows, width):
    pairs = width // 128
    quarter = head_dim // 4
    per_pair = 128 // head_dim
    stacked = per_pair * count_rows

    def kernel(needed_ref, place_ref, scale_ref, q_ref, *rest):
        payload_refs = rest[:slots]
        (cos_ref, sin_ref, wk_ref, wv_ref, wo_ref, tok_ref, out_ref, k_buf, v_buf,
         r_buf, c_buf, s_buf) = rest[slots:]
        lane = lax.broadcasted_iota(jnp.int32, (count_rows, 128), 1)
        first = (lane % (2 * quarter)) < quarter
        head_of_lane = lane // head_dim
        row = lax.broadcasted_iota(jnp.int32, (stacked, 1), 0)

        for slot in range(slots):

            @pl.when(needed_ref[slot] != 0)
            def _():
                at = pl.ds(pl.multiple_of(place_ref[slot] * count_rows, count_rows), count_rows)
                r_buf[at, :] = payload_refs[slot][...]
                c_buf[at, :] = cos_ref[slot]
                s_buf[at, :] = sin_ref[slot]

        rows = r_buf[...]
        kp = jnp.dot(rows, wk_ref[...], preferred_element_type=jnp.float32)
        vp = jnp.dot(rows, wv_ref[...], preferred_element_type=jnp.float32)
        v_buf[...] = jnp.where(jnp.abs(vp) < jnp.inf, vp, jnp.float32(0)).astype(jnp.bfloat16)
        cosine = c_buf[...]
        signed = s_buf[...]
        lane_k = lax.broadcasted_iota(jnp.int32, (reads * count_rows, 128), 1)
        first_k = (lane_k % (2 * quarter)) < quarter
        for p in range(pairs):
            lo = p * 128
            x = kp[:, lo:lo + 128]
            other = jnp.where(first_k, pltpu.roll(x, 128 - quarter, 1), pltpu.roll(x, quarter, 1))
            k_buf[:, lo:lo + 128] = (x * cosine + other * signed).astype(jnp.bfloat16)

        parts = []
        for p in range(pairs):
            lo = p * 128
            q_pair = q_ref[:, lo:lo + 128]
            q_two = jnp.concatenate(
                [jnp.where(head_of_lane == sub, q_pair, jnp.zeros_like(q_pair))
                 for sub in range(per_pair)], axis=0)
            scale_col = jnp.zeros((stacked, 1), jnp.float32)
            for sub in range(per_pair):
                scale_col = jnp.where(row // count_rows == sub, scale_ref[p * per_pair + sub], scale_col)
            scores = lax.dot_general(
                q_two, k_buf[:, lo:lo + 128], (((1,), (1,)), ((), ())),
                preferred_element_type=jnp.float32,
            ) * scale_col
            scores = jnp.where(jnp.abs(scores) < jnp.inf, scores, jnp.float32(NEG))
            best = jnp.max(scores, axis=1, keepdims=True)
            weights = jnp.exp(scores - best)
            total = jnp.sum(weights, axis=1, keepdims=True)
            summed = jnp.dot(weights.astype(jnp.bfloat16), v_buf[:, lo:lo + 128],
                             preferred_element_type=jnp.float32)
            two = summed / total
            res = two[0:count_rows]
            for sub in range(1, per_pair):
                res = jnp.where(head_of_lane == sub, two[sub * count_rows:(sub + 1) * count_rows], res)
            parts.append(res.astype(jnp.bfloat16))
        attended = jnp.concatenate(parts, axis=1)
        mixed = tok_ref[...].astype(jnp.float32) + jnp.dot(
            attended, wo_ref[...], preferred_element_type=jnp.float32
        )
        out_ref[...] = mixed.astype(out_ref.dtype)

    return kernel


def make_query_kernel(head_dim):
    quarter = head_dim // 4

    def kernel(x_ref, w_ref, cos_ref, sin_ref, out_ref):
        proj = jnp.dot(x_ref[...], w_ref[...], preferred_element_type=jnp.float32)
        lane = lax.broadcasted_iota(jnp.int32, (proj.shape[0], 128), 1)
        first = (lane % (2 * quarter)) < quarter
        cosine = cos_ref[...]
        signed = sin_ref[...]
        for p in range(proj.shape[1] // 128):
            lo = p * 128
            x = proj[:, lo:lo + 128]
            other = jnp.where(first, pltpu.roll(x, 128 - quarter, 1), pltpu.roll(x, quarter, 1))
            out_ref[:, lo:lo + 128] = (x * cosine + other * signed).astype(out_ref.dtype)

    return kernel


def make_prep_kernel(tile_count, tile_rows, count_rows):
    def kernel(order_ref, count_ref, tok_ref, gain_ref, normed_ref, out_ref):
        floated = tok_ref[...].astype(jnp.float32)
        normed_ref[...] = layer_norm(floated, gain_ref[...]).astype(normed_ref.dtype)
        row = lax.broadcasted_iota(jnp.int32, (tile_rows, 1), 0)
        for s in range(tile_count):
            src = order_ref[s]
            start = pl.multiple_of(src * tile_rows, tile_rows)
            rows = normed_ref[pl.ds(start, tile_rows), :]
            out_ref[s * tile_rows:(s + 1) * tile_rows, :] = jnp.where(
                row < count_ref[src], rows, jnp.asarray(jnp.inf, rows.dtype))

    return kernel


def across(shard, by):
    size = lax.axis_size("tok")
    epochs = lax.axis_size("ep")
    pairs = [
        ((i + by) * epochs + (epochs - 1 - e), i * epochs + e)
        for i in range(size)
        for e in range(epochs)
        if 0 <= i + by < size
    ]
    return lax.ppermute(shard, ("tok", "ep"), pairs)


def full_spec(shape):
    return pl.BlockSpec(shape, lambda i: (0,) * len(shape))


def on_device(
    tokens, norm_gain, query_weight, w_key, w_value, w_out, head_scale, matching, valid, stops
):
    count_rows, width = tokens.shape[1:]
    heads = head_scale.shape[0]
    head_dim = width // heads
    block_index = lax.axis_index("tok")
    smem = pl.BlockSpec(memory_space=pltpu.SMEM)
    vmem = pl.BlockSpec(memory_space=pltpu.VMEM)
    theirs = partner(matching[0], "ep", 0)
    tile_count = matching.shape[1]
    tile_rows = count_rows // tile_count
    normed, payload = pl.pallas_call(
        make_prep_kernel(tile_count, tile_rows, count_rows),
        out_shape=(
            jax.ShapeDtypeStruct((count_rows, width), jnp.bfloat16),
            jax.ShapeDtypeStruct((count_rows, width), jnp.bfloat16),
        ),
        in_specs=[smem, smem, vmem, vmem],
        out_specs=(vmem, vmem),
    )(theirs, valid[0], tokens[0], norm_gain.reshape(1, width))

    offsets = list(range(-BAND, BAND + 1))
    slots = len(offsets)
    received = [partner(payload, "ep", 0) if d == 0 else across(payload, d) for d in offsets]
    own_block = offsets.index(0)
    received[own_block], stops, head_scale, block_index = lax.optimization_barrier(
        (received[own_block], stops, head_scale, block_index))
    blocks = block_index + jnp.array(offsets, dtype=jnp.int32)
    needed = jnp.any(stops[0, 0][None, :] == blocks[:, None], axis=1)
    cosine, signed = angle_tables(blocks, count_rows, head_dim)
    scales = (head_scale / math.sqrt(head_dim)).astype(jnp.float32)
    own = offsets.index(0)
    table_spec = pl.BlockSpec((None, count_rows, 128), lambda i: (own, 0, 0))

    queries = pl.pallas_call(
        make_query_kernel(head_dim),
        out_shape=jax.ShapeDtypeStruct((count_rows, width), jnp.bfloat16),
        grid=(1,),
        in_specs=[full_spec((count_rows, width)), full_spec((width, width)), table_spec, table_spec],
        out_specs=full_spec((count_rows, width)),
    )(normed, query_weight, cosine, signed)

    reads = stops.shape[-1]
    flags = needed.astype(jnp.int32)
    place = jnp.cumsum(flags) - flags
    out = pl.pallas_call(
        make_band_kernel(slots, reads, heads, head_dim, count_rows, width),
        out_shape=jax.ShapeDtypeStruct((count_rows, width), jnp.bfloat16),
        in_specs=[smem, smem, smem] + [vmem] * (1 + slots + 6),
        out_specs=vmem,
        scratch_shapes=[
            pltpu.VMEM((reads * count_rows, width), jnp.bfloat16),
            pltpu.VMEM((reads * count_rows, width), jnp.bfloat16),
            pltpu.VMEM((reads * count_rows, width), jnp.bfloat16),
            pltpu.VMEM((reads * count_rows, 128), jnp.float32),
            pltpu.VMEM((reads * count_rows, 128), jnp.float32),
        ],
    )(flags, place, scales, queries, *received, cosine, signed, w_key, w_value, w_out, tokens[0])
    return out[None]


def solution(mesh):
    in_specs = (
        P("ep", ("grp", "tok"), None),
        P(),
        P(),
        P(),
        P(),
        P(),
        P(),
        P("ep", ("grp", "tok")),
        P("ep", ("grp", "tok")),
        P("ep", ("grp", "tok"), None),
    )
    out_specs = P("ep", ("grp", "tok"), None)
    return jax.shard_map(
        on_device, mesh=mesh, in_specs=in_specs, out_specs=out_specs, check_vma=False
    )
```

```python
import math

import jax
import jax.numpy as jnp
from jax import lax
from jax.experimental import pallas as pl
from jax.experimental.pallas import tpu as pltpu
from jax.sharding import PartitionSpec as P

BAND = 3
ROW_PATCHES = 1024
META_ROWS = 8
NEG = -1e30


def partner(block, axis, apart):
    count = lax.axis_size(axis)
    route = []
    for low in range(count):
        high = low | 1 << apart
        if high != low and high < count:
            route += [(low, high), (high, low)]
    return lax.ppermute(block, axis, route)


def layer_norm(floated, norm_gain):
    center = jnp.mean(floated, axis=-1, keepdims=True)
    spread = jnp.mean((floated - center) ** 2, axis=-1, keepdims=True)
    return (floated - center) * lax.rsqrt(spread + 1e-05) * norm_gain


def turn_pairs(part, angle):
    quarter = part.shape[-1] // 2
    first = part[..., :quarter]
    second = part[..., quarter:]
    cosine = jnp.cos(angle)[:, None, :]
    sine = jnp.sin(angle)[:, None, :]
    return jnp.concatenate(
        [first * cosine - second * sine, second * cosine + first * sine], axis=-1
    )


def frequencies(quarter):
    return 100.0 ** (-jnp.arange(quarter, dtype=jnp.float32) / quarter)


def rotate(values, patch_coordinates, heads):
    count_rows, width = values.shape
    head_dim = width // heads
    half = head_dim // 2
    quarter = head_dim // 4
    split = values.reshape(count_rows, heads, head_dim)
    row_coordinate = (patch_coordinates // ROW_PATCHES).astype(jnp.float32)
    column_coordinate = (patch_coordinates % ROW_PATCHES).astype(jnp.float32)
    freqs = frequencies(quarter)
    turned = jnp.concatenate(
        [
            turn_pairs(split[..., :half], row_coordinate[:, None] * freqs[None, :]),
            turn_pairs(split[..., half:], column_coordinate[:, None] * freqs[None, :]),
        ],
        axis=-1,
    )
    return turned.reshape(count_rows, width)


def angle_tables(blocks, count_rows, head_dim):
    half = head_dim // 2
    quarter = head_dim // 4
    lanes = jnp.arange(128, dtype=jnp.int32)
    spots = blocks[:, None] * count_rows + jnp.arange(count_rows, dtype=jnp.int32)[None, :]
    row_coordinate = (spots // ROW_PATCHES).astype(jnp.float32)
    column_coordinate = (spots % ROW_PATCHES).astype(jnp.float32)
    in_row_part = (lanes % head_dim) < half
    coordinate = jnp.where(
        in_row_part[None, None, :], row_coordinate[:, :, None], column_coordinate[:, :, None]
    )
    freq_lane = jnp.tile(frequencies(quarter), 128 // quarter)
    angle = coordinate * freq_lane[None, None, :]
    first = (lanes % half) < quarter
    cosine = jnp.cos(angle)
    sine = jnp.sin(angle)
    signed = jnp.where(first[None, None, :], -sine, sine)
    return cosine, signed


def table_rows(block, freq_lane, count_rows, head_dim):
    half = head_dim // 2
    quarter = head_dim // 4
    lane = lax.broadcasted_iota(jnp.int32, (count_rows, 128), 1)
    spots = block * count_rows + lax.broadcasted_iota(jnp.int32, (count_rows, 128), 0)
    coordinate = jnp.where((lane % head_dim) < half, spots // ROW_PATCHES, spots % ROW_PATCHES)
    angle = coordinate.astype(jnp.float32) * freq_lane
    sine = jnp.sin(angle)
    return jnp.cos(angle), jnp.where((lane % half) < quarter, -sine, sine)


def make_band_kernel(slots, reads, heads, head_dim, count_rows, width):
    pairs = width // 128
    quarter = head_dim // 4
    per_pair = 128 // head_dim
    stacked = per_pair * count_rows

    def kernel(needed_ref, place_ref, scale_ref, q_ref, *rest):
        payload_refs = rest[:slots]
        (block_ref, freq_ref, wk_ref, wv_ref, wo_ref, tok_ref, out_ref, k_buf, v_buf,
         r_buf, c_buf, s_buf) = rest[slots:]
        lane = lax.broadcasted_iota(jnp.int32, (count_rows, 128), 1)
        first = (lane % (2 * quarter)) < quarter
        head_of_lane = lane // head_dim
        row = lax.broadcasted_iota(jnp.int32, (stacked, 1), 0)

        for slot in range(slots):

            @pl.when(needed_ref[slot] != 0)
            def _():
                at = pl.ds(pl.multiple_of(place_ref[slot] * count_rows, count_rows), count_rows)
                r_buf[at, :] = payload_refs[slot][...]
                cosine, signed = table_rows(block_ref[slot], freq_ref[...], count_rows, head_dim)
                c_buf[at, :] = cosine
                s_buf[at, :] = signed

        rows = r_buf[...]
        kp = jnp.dot(rows, wk_ref[...], preferred_element_type=jnp.float32)
        vp = jnp.dot(rows, wv_ref[...], preferred_element_type=jnp.float32)
        v_buf[...] = jnp.where(jnp.abs(vp) < jnp.inf, vp, jnp.float32(0)).astype(jnp.bfloat16)
        cosine = c_buf[...]
        signed = s_buf[...]
        lane_k = lax.broadcasted_iota(jnp.int32, (reads * count_rows, 128), 1)
        first_k = (lane_k % (2 * quarter)) < quarter
        for p in range(pairs):
            lo = p * 128
            x = kp[:, lo:lo + 128]
            other = jnp.where(first_k, pltpu.roll(x, 128 - quarter, 1), pltpu.roll(x, quarter, 1))
            k_buf[:, lo:lo + 128] = (x * cosine + other * signed).astype(jnp.bfloat16)

        parts = []
        for p in range(pairs):
            lo = p * 128
            q_pair = q_ref[:, lo:lo + 128]
            q_two = jnp.concatenate(
                [jnp.where(head_of_lane == sub, q_pair, jnp.zeros_like(q_pair))
                 for sub in range(per_pair)], axis=0)
            scale_col = jnp.zeros((stacked, 1), jnp.float32)
            for sub in range(per_pair):
                scale_col = jnp.where(row // count_rows == sub, scale_ref[p * per_pair + sub], scale_col)
            scores = lax.dot_general(
                q_two, k_buf[:, lo:lo + 128], (((1,), (1,)), ((), ())),
                preferred_element_type=jnp.float32,
            ) * scale_col
            scores = jnp.where(jnp.abs(scores) < jnp.inf, scores, jnp.float32(NEG))
            best = jnp.max(scores, axis=1, keepdims=True)
            weights = jnp.exp(scores - best)
            total = jnp.sum(weights, axis=1, keepdims=True)
            summed = jnp.dot(weights.astype(jnp.bfloat16), v_buf[:, lo:lo + 128],
                             preferred_element_type=jnp.float32)
            two = summed / total
            res = two[0:count_rows]
            for sub in range(1, per_pair):
                res = jnp.where(head_of_lane == sub, two[sub * count_rows:(sub + 1) * count_rows], res)
            parts.append(res.astype(jnp.bfloat16))
        attended = jnp.concatenate(parts, axis=1)
        mixed = tok_ref[...].astype(jnp.float32) + jnp.dot(
            attended, wo_ref[...], preferred_element_type=jnp.float32
        )
        out_ref[...] = mixed.astype(out_ref.dtype)

    return kernel


def make_query_kernel(head_dim):
    quarter = head_dim // 4

    def kernel(block_ref, x_ref, w_ref, freq_ref, out_ref):
        proj = jnp.dot(x_ref[...], w_ref[...], preferred_element_type=jnp.float32)
        lane = lax.broadcasted_iota(jnp.int32, (proj.shape[0], 128), 1)
        first = (lane % (2 * quarter)) < quarter
        cosine, signed = table_rows(block_ref[0], freq_ref[...], proj.shape[0], head_dim)
        for p in range(proj.shape[1] // 128):
            lo = p * 128
            x = proj[:, lo:lo + 128]
            other = jnp.where(first, pltpu.roll(x, 128 - quarter, 1), pltpu.roll(x, quarter, 1))
            out_ref[:, lo:lo + 128] = (x * cosine + other * signed).astype(out_ref.dtype)

    return kernel


def make_prep_kernel(tile_count, tile_rows, count_rows):
    def kernel(order_ref, count_ref, tok_ref, gain_ref, normed_ref, out_ref):
        floated = tok_ref[...].astype(jnp.float32)
        normed_ref[...] = layer_norm(floated, gain_ref[...]).astype(normed_ref.dtype)
        row = lax.broadcasted_iota(jnp.int32, (tile_rows, 1), 0)
        for s in range(tile_count):
            src = order_ref[s]
            start = pl.multiple_of(src * tile_rows, tile_rows)
            rows = normed_ref[pl.ds(start, tile_rows), :]
            out_ref[s * tile_rows:(s + 1) * tile_rows, :] = jnp.where(
                row < count_ref[src], rows, jnp.asarray(jnp.inf, rows.dtype))

    return kernel


def across(shard, by):
    size = lax.axis_size("tok")
    epochs = lax.axis_size("ep")
    pairs = [
        ((i + by) * epochs + (epochs - 1 - e), i * epochs + e)
        for i in range(size)
        for e in range(epochs)
        if 0 <= i + by < size
    ]
    return lax.ppermute(shard, ("tok", "ep"), pairs)


def full_spec(shape):
    return pl.BlockSpec(shape, lambda i: (0,) * len(shape))


def on_device(
    tokens, norm_gain, query_weight, w_key, w_value, w_out, head_scale, matching, valid, stops
):
    count_rows, width = tokens.shape[1:]
    heads = head_scale.shape[0]
    head_dim = width // heads
    block_index = lax.axis_index("tok")
    smem = pl.BlockSpec(memory_space=pltpu.SMEM)
    vmem = pl.BlockSpec(memory_space=pltpu.VMEM)
    theirs = partner(matching[0], "ep", 0)
    tile_count = matching.shape[1]
    tile_rows = count_rows // tile_count
    normed, payload = pl.pallas_call(
        make_prep_kernel(tile_count, tile_rows, count_rows),
        out_shape=(
            jax.ShapeDtypeStruct((count_rows, width), jnp.bfloat16),
            jax.ShapeDtypeStruct((count_rows, width), jnp.bfloat16),
        ),
        in_specs=[smem, smem, vmem, vmem],
        out_specs=(vmem, vmem),
    )(theirs, valid[0], tokens[0], norm_gain.reshape(1, width))

    offsets = list(range(-BAND, BAND + 1))
    slots = len(offsets)
    received = [partner(payload, "ep", 0) if d == 0 else across(payload, d) for d in offsets]
    own_block = offsets.index(0)
    received[own_block], stops, head_scale, block_index = lax.optimization_barrier(
        (received[own_block], stops, head_scale, block_index))
    blocks = block_index + jnp.array(offsets, dtype=jnp.int32)
    needed = jnp.any(stops[0, 0][None, :] == blocks[:, None], axis=1)
    freq_lane = jnp.tile(frequencies(head_dim // 4), 128 // (head_dim // 4)).reshape(1, 128)
    scales = (head_scale / math.sqrt(head_dim)).astype(jnp.float32)
    own = offsets.index(0)
    table_spec = pl.BlockSpec((None, count_rows, 128), lambda i: (own, 0, 0))

    queries = pl.pallas_call(
        make_query_kernel(head_dim),
        out_shape=jax.ShapeDtypeStruct((count_rows, width), jnp.bfloat16),
        grid=(1,),
        in_specs=[smem, full_spec((count_rows, width)), full_spec((width, width)), full_spec((1, 128))],
        out_specs=full_spec((count_rows, width)),
    )(block_index.reshape(1), normed, query_weight, freq_lane)

    reads = stops.shape[-1]
    flags = needed.astype(jnp.int32)
    place = jnp.cumsum(flags) - flags
    out = pl.pallas_call(
        make_band_kernel(slots, reads, heads, head_dim, count_rows, width),
        out_shape=jax.ShapeDtypeStruct((count_rows, width), jnp.bfloat16),
        in_specs=[smem, smem, smem, vmem] + [vmem] * slots + [smem] + [vmem] * 5,
        out_specs=vmem,
        scratch_shapes=[
            pltpu.VMEM((reads * count_rows, width), jnp.bfloat16),
            pltpu.VMEM((reads * count_rows, width), jnp.bfloat16),
            pltpu.VMEM((reads * count_rows, width), jnp.bfloat16),
            pltpu.VMEM((reads * count_rows, 128), jnp.float32),
            pltpu.VMEM((reads * count_rows, 128), jnp.float32),
        ],
    )(flags, place, scales, queries, *received, blocks, freq_lane, w_key, w_value, w_out, tokens[0])
    return out[None]


def solution(mesh):
    in_specs = (
        P("ep", ("grp", "tok"), None),
        P(),
        P(),
        P(),
        P(),
        P(),
        P(),
        P("ep", ("grp", "tok")),
        P("ep", ("grp", "tok")),
        P("ep", ("grp", "tok"), None),
    )
    out_specs = P("ep", ("grp", "tok"), None)
    return jax.shard_map(
        on_device, mesh=mesh, in_specs=in_specs, out_specs=out_specs, check_vma=False
    )
```

```python
import math

import jax
import jax.numpy as jnp
from jax import lax
from jax.experimental import pallas as pl
from jax.experimental.pallas import tpu as pltpu
from jax.sharding import PartitionSpec as P

BAND = 3
ROW_PATCHES = 1024
META_ROWS = 8
NEG = -1e30


def partner(block, axis, apart):
    count = lax.axis_size(axis)
    route = []
    for low in range(count):
        high = low | 1 << apart
        if high != low and high < count:
            route += [(low, high), (high, low)]
    return lax.ppermute(block, axis, route)


def layer_norm(floated, norm_gain):
    center = jnp.mean(floated, axis=-1, keepdims=True)
    spread = jnp.mean((floated - center) ** 2, axis=-1, keepdims=True)
    return (floated - center) * lax.rsqrt(spread + 1e-05) * norm_gain


def turn_pairs(part, angle):
    quarter = part.shape[-1] // 2
    first = part[..., :quarter]
    second = part[..., quarter:]
    cosine = jnp.cos(angle)[:, None, :]
    sine = jnp.sin(angle)[:, None, :]
    return jnp.concatenate(
        [first * cosine - second * sine, second * cosine + first * sine], axis=-1
    )


def frequencies(quarter):
    return 100.0 ** (-jnp.arange(quarter, dtype=jnp.float32) / quarter)


def rotate(values, patch_coordinates, heads):
    count_rows, width = values.shape
    head_dim = width // heads
    half = head_dim // 2
    quarter = head_dim // 4
    split = values.reshape(count_rows, heads, head_dim)
    row_coordinate = (patch_coordinates // ROW_PATCHES).astype(jnp.float32)
    column_coordinate = (patch_coordinates % ROW_PATCHES).astype(jnp.float32)
    freqs = frequencies(quarter)
    turned = jnp.concatenate(
        [
            turn_pairs(split[..., :half], row_coordinate[:, None] * freqs[None, :]),
            turn_pairs(split[..., half:], column_coordinate[:, None] * freqs[None, :]),
        ],
        axis=-1,
    )
    return turned.reshape(count_rows, width)


def angle_tables(blocks, count_rows, head_dim):
    half = head_dim // 2
    quarter = head_dim // 4
    lanes = jnp.arange(128, dtype=jnp.int32)
    spots = blocks[:, None] * count_rows + jnp.arange(count_rows, dtype=jnp.int32)[None, :]
    row_coordinate = (spots // ROW_PATCHES).astype(jnp.float32)
    column_coordinate = (spots % ROW_PATCHES).astype(jnp.float32)
    in_row_part = (lanes % head_dim) < half
    coordinate = jnp.where(
        in_row_part[None, None, :], row_coordinate[:, :, None], column_coordinate[:, :, None]
    )
    freq_lane = jnp.tile(frequencies(quarter), 128 // quarter)
    angle = coordinate * freq_lane[None, None, :]
    first = (lanes % half) < quarter
    cosine = jnp.cos(angle)
    sine = jnp.sin(angle)
    signed = jnp.where(first[None, None, :], -sine, sine)
    return cosine, signed


def make_band_kernel(slots, reads, heads, head_dim, count_rows, width):
    pairs = width // 128
    quarter = head_dim // 4
    per_pair = 128 // head_dim
    stacked = per_pair * count_rows

    def kernel(stops_ref, base_ref, scale_ref, q_ref, *rest):
        payload_refs = rest[:slots]
        (cos_ref, sin_ref, wk_ref, wv_ref, wo_ref, tok_ref, out_ref, k_buf, v_buf,
         r_buf, c_buf, s_buf) = rest[slots:]
        lane = lax.broadcasted_iota(jnp.int32, (count_rows, 128), 1)
        first = (lane % (2 * quarter)) < quarter
        head_of_lane = lane // head_dim
        row = lax.broadcasted_iota(jnp.int32, (stacked, 1), 0)

        place = jnp.int32(0)
        for slot in range(slots):
            block = base_ref[0] + (slot - slots // 2)
            hit = stops_ref[0] == block
            for r in range(1, reads):
                hit = hit | (stops_ref[r] == block)
            spot = place

            @pl.when(hit)
            def _():
                at = pl.ds(pl.multiple_of(spot * count_rows, count_rows), count_rows)
                r_buf[at, :] = payload_refs[slot][...]
                c_buf[at, :] = cos_ref[slot]
                s_buf[at, :] = sin_ref[slot]

            place = place + jnp.where(hit, jnp.int32(1), jnp.int32(0))

        rows = r_buf[...]
        kp = jnp.dot(rows, wk_ref[...], preferred_element_type=jnp.float32)
        vp = jnp.dot(rows, wv_ref[...], preferred_element_type=jnp.float32)
        v_buf[...] = jnp.where(jnp.abs(vp) < jnp.inf, vp, jnp.float32(0)).astype(jnp.bfloat16)
        cosine = c_buf[...]
        signed = s_buf[...]
        lane_k = lax.broadcasted_iota(jnp.int32, (reads * count_rows, 128), 1)
        first_k = (lane_k % (2 * quarter)) < quarter
        for p in range(pairs):
            lo = p * 128
            x = kp[:, lo:lo + 128]
            other = jnp.where(first_k, pltpu.roll(x, 128 - quarter, 1), pltpu.roll(x, quarter, 1))
            k_buf[:, lo:lo + 128] = (x * cosine + other * signed).astype(jnp.bfloat16)

        parts = []
        for p in range(pairs):
            lo = p * 128
            q_pair = q_ref[:, lo:lo + 128]
            q_two = jnp.concatenate(
                [jnp.where(head_of_lane == sub, q_pair, jnp.zeros_like(q_pair))
                 for sub in range(per_pair)], axis=0)
            scale_col = jnp.zeros((stacked, 1), jnp.float32)
            for sub in range(per_pair):
                scale_col = jnp.where(row // count_rows == sub, scale_ref[p * per_pair + sub] / jnp.float32(math.sqrt(head_dim)), scale_col)
            scores = lax.dot_general(
                q_two, k_buf[:, lo:lo + 128], (((1,), (1,)), ((), ())),
                preferred_element_type=jnp.float32,
            ) * scale_col
            scores = jnp.where(jnp.abs(scores) < jnp.inf, scores, jnp.float32(NEG))
            best = jnp.max(scores, axis=1, keepdims=True)
            weights = jnp.exp(scores - best)
            total = jnp.sum(weights, axis=1, keepdims=True)
            summed = jnp.dot(weights.astype(jnp.bfloat16), v_buf[:, lo:lo + 128],
                             preferred_element_type=jnp.float32)
            two = summed / total
            res = two[0:count_rows]
            for sub in range(1, per_pair):
                res = jnp.where(head_of_lane == sub, two[sub * count_rows:(sub + 1) * count_rows], res)
            parts.append(res.astype(jnp.bfloat16))
        attended = jnp.concatenate(parts, axis=1)
        mixed = tok_ref[...].astype(jnp.float32) + jnp.dot(
            attended, wo_ref[...], preferred_element_type=jnp.float32
        )
        out_ref[...] = mixed.astype(out_ref.dtype)

    return kernel


def make_query_kernel(head_dim):
    quarter = head_dim // 4

    def kernel(x_ref, w_ref, cos_ref, sin_ref, out_ref):
        proj = jnp.dot(x_ref[...], w_ref[...], preferred_element_type=jnp.float32)
        lane = lax.broadcasted_iota(jnp.int32, (proj.shape[0], 128), 1)
        first = (lane % (2 * quarter)) < quarter
        cosine = cos_ref[...]
        signed = sin_ref[...]
        for p in range(proj.shape[1] // 128):
            lo = p * 128
            x = proj[:, lo:lo + 128]
            other = jnp.where(first, pltpu.roll(x, 128 - quarter, 1), pltpu.roll(x, quarter, 1))
            out_ref[:, lo:lo + 128] = (x * cosine + other * signed).astype(out_ref.dtype)

    return kernel


def make_prep_kernel(tile_count, tile_rows, count_rows):
    def kernel(order_ref, count_ref, tok_ref, gain_ref, normed_ref, out_ref):
        floated = tok_ref[...].astype(jnp.float32)
        normed_ref[...] = layer_norm(floated, gain_ref[...]).astype(normed_ref.dtype)
        row = lax.broadcasted_iota(jnp.int32, (tile_rows, 1), 0)
        for s in range(tile_count):
            src = order_ref[s]
            start = pl.multiple_of(src * tile_rows, tile_rows)
            rows = normed_ref[pl.ds(start, tile_rows), :]
            out_ref[s * tile_rows:(s + 1) * tile_rows, :] = jnp.where(
                row < count_ref[src], rows, jnp.asarray(jnp.inf, rows.dtype))

    return kernel


def across(shard, by):
    size = lax.axis_size("tok")
    epochs = lax.axis_size("ep")
    pairs = [
        ((i + by) * epochs + (epochs - 1 - e), i * epochs + e)
        for i in range(size)
        for e in range(epochs)
        if 0 <= i + by < size
    ]
    return lax.ppermute(shard, ("tok", "ep"), pairs)


def full_spec(shape):
    return pl.BlockSpec(shape, lambda i: (0,) * len(shape))


def on_device(
    tokens, norm_gain, query_weight, w_key, w_value, w_out, head_scale, matching, valid, stops
):
    count_rows, width = tokens.shape[1:]
    heads = head_scale.shape[0]
    head_dim = width // heads
    block_index = lax.axis_index("tok")
    smem = pl.BlockSpec(memory_space=pltpu.SMEM)
    vmem = pl.BlockSpec(memory_space=pltpu.VMEM)
    theirs = partner(matching[0], "ep", 0)
    tile_count = matching.shape[1]
    tile_rows = count_rows // tile_count
    normed, payload = pl.pallas_call(
        make_prep_kernel(tile_count, tile_rows, count_rows),
        out_shape=(
            jax.ShapeDtypeStruct((count_rows, width), jnp.bfloat16),
            jax.ShapeDtypeStruct((count_rows, width), jnp.bfloat16),
        ),
        in_specs=[smem, smem, vmem, vmem],
        out_specs=(vmem, vmem),
    )(theirs, valid[0], tokens[0], norm_gain.reshape(1, width))

    offsets = list(range(-BAND, BAND + 1))
    slots = len(offsets)
    received = [partner(payload, "ep", 0) if d == 0 else across(payload, d) for d in offsets]
    own_block = offsets.index(0)
    received[own_block], stops, head_scale, block_index = lax.optimization_barrier(
        (received[own_block], stops, head_scale, block_index))
    blocks = block_index + jnp.array(offsets, dtype=jnp.int32)
    cosine, signed = angle_tables(blocks, count_rows, head_dim)
    own = offsets.index(0)
    table_spec = pl.BlockSpec((None, count_rows, 128), lambda i: (own, 0, 0))

    queries = pl.pallas_call(
        make_query_kernel(head_dim),
        out_shape=jax.ShapeDtypeStruct((count_rows, width), jnp.bfloat16),
        grid=(1,),
        in_specs=[full_spec((count_rows, width)), full_spec((width, width)), table_spec, table_spec],
        out_specs=full_spec((count_rows, width)),
    )(normed, query_weight, cosine, signed)

    reads = stops.shape[-1]
    out = pl.pallas_call(
        make_band_kernel(slots, reads, heads, head_dim, count_rows, width),
        out_shape=jax.ShapeDtypeStruct((count_rows, width), jnp.bfloat16),
        in_specs=[smem, smem, smem] + [vmem] * (1 + slots + 6),
        out_specs=vmem,
        scratch_shapes=[
            pltpu.VMEM((reads * count_rows, width), jnp.bfloat16),
            pltpu.VMEM((reads * count_rows, width), jnp.bfloat16),
            pltpu.VMEM((reads * count_rows, width), jnp.bfloat16),
            pltpu.VMEM((reads * count_rows, 128), jnp.float32),
            pltpu.VMEM((reads * count_rows, 128), jnp.float32),
        ],
    )(stops[0, 0], block_index.reshape(1), head_scale, queries, *received, cosine, signed, w_key,
      w_value, w_out, tokens[0])
    return out[None]


def solution(mesh):
    in_specs = (
        P("ep", ("grp", "tok"), None),
        P(),
        P(),
        P(),
        P(),
        P(),
        P(),
        P("ep", ("grp", "tok")),
        P("ep", ("grp", "tok")),
        P("ep", ("grp", "tok"), None),
    )
    out_specs = P("ep", ("grp", "tok"), None)
    return jax.shard_map(
        on_device, mesh=mesh, in_specs=in_specs, out_specs=out_specs, check_vma=False
    )
```

```python
import math

import jax
import jax.numpy as jnp
from jax import lax
from jax.experimental import pallas as pl
from jax.experimental.pallas import tpu as pltpu
from jax.sharding import PartitionSpec as P

BAND = 3
ROW_PATCHES = 1024
META_ROWS = 8
NEG = -1e30


def partner(block, axis, apart):
    count = lax.axis_size(axis)
    route = []
    for low in range(count):
        high = low | 1 << apart
        if high != low and high < count:
            route += [(low, high), (high, low)]
    return lax.ppermute(block, axis, route)


def layer_norm(floated, norm_gain):
    center = jnp.mean(floated, axis=-1, keepdims=True)
    spread = jnp.mean((floated - center) ** 2, axis=-1, keepdims=True)
    return (floated - center) * lax.rsqrt(spread + 1e-05) * norm_gain


def turn_pairs(part, angle):
    quarter = part.shape[-1] // 2
    first = part[..., :quarter]
    second = part[..., quarter:]
    cosine = jnp.cos(angle)[:, None, :]
    sine = jnp.sin(angle)[:, None, :]
    return jnp.concatenate(
        [first * cosine - second * sine, second * cosine + first * sine], axis=-1
    )


def frequencies(quarter):
    return 100.0 ** (-jnp.arange(quarter, dtype=jnp.float32) / quarter)


def rotate(values, patch_coordinates, heads):
    count_rows, width = values.shape
    head_dim = width // heads
    half = head_dim // 2
    quarter = head_dim // 4
    split = values.reshape(count_rows, heads, head_dim)
    row_coordinate = (patch_coordinates // ROW_PATCHES).astype(jnp.float32)
    column_coordinate = (patch_coordinates % ROW_PATCHES).astype(jnp.float32)
    freqs = frequencies(quarter)
    turned = jnp.concatenate(
        [
            turn_pairs(split[..., :half], row_coordinate[:, None] * freqs[None, :]),
            turn_pairs(split[..., half:], column_coordinate[:, None] * freqs[None, :]),
        ],
        axis=-1,
    )
    return turned.reshape(count_rows, width)


def angle_tables(blocks, count_rows, head_dim):
    half = head_dim // 2
    quarter = head_dim // 4
    lanes = jnp.arange(128, dtype=jnp.int32)
    spots = blocks[:, None] * count_rows + jnp.arange(count_rows, dtype=jnp.int32)[None, :]
    row_coordinate = (spots // ROW_PATCHES).astype(jnp.float32)
    column_coordinate = (spots % ROW_PATCHES).astype(jnp.float32)
    in_row_part = (lanes % head_dim) < half
    coordinate = jnp.where(
        in_row_part[None, None, :], row_coordinate[:, :, None], column_coordinate[:, :, None]
    )
    freq_lane = jnp.tile(frequencies(quarter), 128 // quarter)
    angle = coordinate * freq_lane[None, None, :]
    first = (lanes % half) < quarter
    cosine = jnp.cos(angle)
    sine = jnp.sin(angle)
    signed = jnp.where(first[None, None, :], -sine, sine)
    return cosine, signed


def make_band_kernel(slots, reads, heads, head_dim, count_rows, width):
    pairs = width // 128
    quarter = head_dim // 4
    per_pair = 128 // head_dim
    stacked = per_pair * count_rows

    def kernel(stops_ref, base_ref, scale_ref, q_ref, *rest):
        payload_refs = rest[:slots]
        (cos_ref, sin_ref, wk_ref, wv_ref, wo_ref, tok_ref, out_ref, k_buf, v_buf,
         r_buf, c_buf, s_buf) = rest[slots:]
        lane = lax.broadcasted_iota(jnp.int32, (count_rows, 128), 1)
        first = (lane % (2 * quarter)) < quarter
        head_of_lane = lane // head_dim
        row = lax.broadcasted_iota(jnp.int32, (stacked, 1), 0)

        place = jnp.int32(0)
        for slot in range(slots):
            block = base_ref[0] + (slot - slots // 2)
            hit = stops_ref[0] == block
            for r in range(1, reads):
                hit = hit | (stops_ref[r] == block)
            spot = place

            @pl.when(hit)
            def _():
                at = pl.ds(pl.multiple_of(spot * count_rows, count_rows), count_rows)
                r_buf[at, :] = payload_refs[slot][...]
                c_buf[at, :] = cos_ref[slot]
                s_buf[at, :] = sin_ref[slot]

            place = place + jnp.where(hit, jnp.int32(1), jnp.int32(0))

        rows = r_buf[...]
        kp = jnp.dot(rows, wk_ref[...], preferred_element_type=jnp.float32)
        vp = jnp.dot(rows, wv_ref[...], preferred_element_type=jnp.float32)
        v_buf[...] = jnp.where(jnp.abs(vp) < jnp.inf, vp, jnp.float32(0)).astype(jnp.bfloat16)
        cosine = c_buf[...]
        signed = s_buf[...]
        lane_k = lax.broadcasted_iota(jnp.int32, (reads * count_rows, 128), 1)
        first_k = (lane_k % (2 * quarter)) < quarter
        for p in range(pairs):
            lo = p * 128
            x = kp[:, lo:lo + 128]
            other = jnp.where(first_k, pltpu.roll(x, 128 - quarter, 1), pltpu.roll(x, quarter, 1))
            k_buf[:, lo:lo + 128] = (x * cosine + other * signed).astype(jnp.bfloat16)

        parts = []
        for p in range(pairs):
            lo = p * 128
            q_pair = q_ref[:, lo:lo + 128]
            q_two = jnp.concatenate(
                [jnp.where(head_of_lane == sub, q_pair, jnp.zeros_like(q_pair))
                 for sub in range(per_pair)], axis=0)
            scale_col = jnp.zeros((stacked, 1), jnp.float32)
            for sub in range(per_pair):
                scale_col = jnp.where(row // count_rows == sub, scale_ref[p * per_pair + sub] / jnp.float32(math.sqrt(head_dim)), scale_col)
            scores = lax.dot_general(
                q_two, k_buf[:, lo:lo + 128], (((1,), (1,)), ((), ())),
                preferred_element_type=jnp.float32,
            ) * scale_col
            scores = jnp.where(jnp.abs(scores) < jnp.inf, scores, jnp.float32(NEG))
            best = jnp.max(scores, axis=1, keepdims=True)
            weights = jnp.exp(scores - best)
            total = jnp.sum(weights, axis=1, keepdims=True)
            summed = jnp.dot(weights.astype(jnp.bfloat16), v_buf[:, lo:lo + 128],
                             preferred_element_type=jnp.float32)
            two = summed / total
            res = two[0:count_rows]
            for sub in range(1, per_pair):
                res = jnp.where(head_of_lane == sub, two[sub * count_rows:(sub + 1) * count_rows], res)
            parts.append(res.astype(jnp.bfloat16))
        attended = jnp.concatenate(parts, axis=1)
        mixed = tok_ref[...].astype(jnp.float32) + jnp.dot(
            attended, wo_ref[...], preferred_element_type=jnp.float32
        )
        out_ref[...] = mixed.astype(out_ref.dtype)

    return kernel


def make_query_kernel(head_dim):
    quarter = head_dim // 4

    def kernel(x_ref, w_ref, cos_ref, sin_ref, out_ref):
        proj = jnp.dot(x_ref[...], w_ref[...], preferred_element_type=jnp.float32)
        lane = lax.broadcasted_iota(jnp.int32, (proj.shape[0], 128), 1)
        first = (lane % (2 * quarter)) < quarter
        cosine = cos_ref[...]
        signed = sin_ref[...]
        for p in range(proj.shape[1] // 128):
            lo = p * 128
            x = proj[:, lo:lo + 128]
            other = jnp.where(first, pltpu.roll(x, 128 - quarter, 1), pltpu.roll(x, quarter, 1))
            out_ref[:, lo:lo + 128] = (x * cosine + other * signed).astype(out_ref.dtype)

    return kernel


def make_prep_kernel(tile_count, tile_rows, count_rows):
    def kernel(order_ref, count_ref, tok_ref, gain_ref, normed_ref, out_ref):
        floated = tok_ref[...].astype(jnp.float32)
        gain = gain_ref[...].reshape(1, floated.shape[1])
        normed_ref[...] = layer_norm(floated, gain).astype(normed_ref.dtype)
        row = lax.broadcasted_iota(jnp.int32, (tile_rows, 1), 0)
        for s in range(tile_count):
            src = order_ref[s]
            start = pl.multiple_of(src * tile_rows, tile_rows)
            rows = normed_ref[pl.ds(start, tile_rows), :]
            out_ref[s * tile_rows:(s + 1) * tile_rows, :] = jnp.where(
                row < count_ref[src], rows, jnp.asarray(jnp.inf, rows.dtype))

    return kernel


def across(shard, by):
    size = lax.axis_size("tok")
    epochs = lax.axis_size("ep")
    pairs = [
        ((i + by) * epochs + (epochs - 1 - e), i * epochs + e)
        for i in range(size)
        for e in range(epochs)
        if 0 <= i + by < size
    ]
    return lax.ppermute(shard, ("tok", "ep"), pairs)


def full_spec(shape):
    return pl.BlockSpec(shape, lambda i: (0,) * len(shape))


def on_device(
    tokens, norm_gain, query_weight, w_key, w_value, w_out, head_scale, matching, valid, stops
):
    count_rows, width = tokens.shape[1:]
    heads = head_scale.shape[0]
    head_dim = width // heads
    block_index = lax.axis_index("tok")
    smem = pl.BlockSpec(memory_space=pltpu.SMEM)
    vmem = pl.BlockSpec(memory_space=pltpu.VMEM)
    theirs = partner(matching[0], "ep", 0)
    tile_count = matching.shape[1]
    tile_rows = count_rows // tile_count
    normed, payload = pl.pallas_call(
        make_prep_kernel(tile_count, tile_rows, count_rows),
        out_shape=(
            jax.ShapeDtypeStruct((count_rows, width), jnp.bfloat16),
            jax.ShapeDtypeStruct((count_rows, width), jnp.bfloat16),
        ),
        in_specs=[smem, smem, vmem, vmem],
        out_specs=(vmem, vmem),
    )(theirs, valid[0], tokens[0], norm_gain)

    offsets = list(range(-BAND, BAND + 1))
    slots = len(offsets)
    received = [partner(payload, "ep", 0) if d == 0 else across(payload, d) for d in offsets]
    own_block = offsets.index(0)
    received[own_block], stops, head_scale, block_index = lax.optimization_barrier(
        (received[own_block], stops, head_scale, block_index))
    blocks = block_index + jnp.array(offsets, dtype=jnp.int32)
    cosine, signed = angle_tables(blocks, count_rows, head_dim)
    own = offsets.index(0)
    table_spec = pl.BlockSpec((None, count_rows, 128), lambda i: (own, 0, 0))

    queries = pl.pallas_call(
        make_query_kernel(head_dim),
        out_shape=jax.ShapeDtypeStruct((count_rows, width), jnp.bfloat16),
        grid=(1,),
        in_specs=[full_spec((count_rows, width)), full_spec((width, width)), table_spec, table_spec],
        out_specs=full_spec((count_rows, width)),
    )(normed, query_weight, cosine, signed)

    reads = stops.shape[-1]
    out = pl.pallas_call(
        make_band_kernel(slots, reads, heads, head_dim, count_rows, width),
        out_shape=jax.ShapeDtypeStruct((count_rows, width), jnp.bfloat16),
        in_specs=[smem, smem, smem] + [vmem] * (1 + slots + 6),
        out_specs=vmem,
        scratch_shapes=[
            pltpu.VMEM((reads * count_rows, width), jnp.bfloat16),
            pltpu.VMEM((reads * count_rows, width), jnp.bfloat16),
            pltpu.VMEM((reads * count_rows, width), jnp.bfloat16),
            pltpu.VMEM((reads * count_rows, 128), jnp.float32),
            pltpu.VMEM((reads * count_rows, 128), jnp.float32),
        ],
    )(stops[0, 0], block_index.reshape(1), head_scale, queries, *received, cosine, signed, w_key,
      w_value, w_out, tokens[0])
    return out[None]


def solution(mesh):
    in_specs = (
        P("ep", ("grp", "tok"), None),
        P(),
        P(),
        P(),
        P(),
        P(),
        P(),
        P("ep", ("grp", "tok")),
        P("ep", ("grp", "tok")),
        P("ep", ("grp", "tok"), None),
    )
    out_specs = P("ep", ("grp", "tok"), None)
    return jax.shard_map(
        on_device, mesh=mesh, in_specs=in_specs, out_specs=out_specs, check_vma=False
    )
```

```python
import math

import jax
import jax.numpy as jnp
from jax import lax
from jax.experimental import pallas as pl
from jax.experimental.pallas import tpu as pltpu
from jax.sharding import PartitionSpec as P

BAND = 3
ROW_PATCHES = 1024
META_ROWS = 8
NEG = -1e30


def partner(block, axis, apart):
    count = lax.axis_size(axis)
    route = []
    for low in range(count):
        high = low | 1 << apart
        if high != low and high < count:
            route += [(low, high), (high, low)]
    return lax.ppermute(block, axis, route)


def layer_norm(floated, norm_gain):
    center = jnp.mean(floated, axis=-1, keepdims=True)
    spread = jnp.mean((floated - center) ** 2, axis=-1, keepdims=True)
    return (floated - center) * lax.rsqrt(spread + 1e-05) * norm_gain


def turn_pairs(part, angle):
    quarter = part.shape[-1] // 2
    first = part[..., :quarter]
    second = part[..., quarter:]
    cosine = jnp.cos(angle)[:, None, :]
    sine = jnp.sin(angle)[:, None, :]
    return jnp.concatenate(
        [first * cosine - second * sine, second * cosine + first * sine], axis=-1
    )


def frequencies(quarter):
    return 100.0 ** (-jnp.arange(quarter, dtype=jnp.float32) / quarter)


def rotate(values, patch_coordinates, heads):
    count_rows, width = values.shape
    head_dim = width // heads
    half = head_dim // 2
    quarter = head_dim // 4
    split = values.reshape(count_rows, heads, head_dim)
    row_coordinate = (patch_coordinates // ROW_PATCHES).astype(jnp.float32)
    column_coordinate = (patch_coordinates % ROW_PATCHES).astype(jnp.float32)
    freqs = frequencies(quarter)
    turned = jnp.concatenate(
        [
            turn_pairs(split[..., :half], row_coordinate[:, None] * freqs[None, :]),
            turn_pairs(split[..., half:], column_coordinate[:, None] * freqs[None, :]),
        ],
        axis=-1,
    )
    return turned.reshape(count_rows, width)


def angle_tables(blocks, count_rows, head_dim):
    half = head_dim // 2
    quarter = head_dim // 4
    lanes = jnp.arange(128, dtype=jnp.int32)
    spots = blocks[:, None] * count_rows + jnp.arange(count_rows, dtype=jnp.int32)[None, :]
    row_coordinate = (spots // ROW_PATCHES).astype(jnp.float32)
    column_coordinate = (spots % ROW_PATCHES).astype(jnp.float32)
    in_row_part = (lanes % head_dim) < half
    coordinate = jnp.where(
        in_row_part[None, None, :], row_coordinate[:, :, None], column_coordinate[:, :, None]
    )
    freq_lane = jnp.tile(frequencies(quarter), 128 // quarter)
    angle = coordinate * freq_lane[None, None, :]
    first = (lanes % half) < quarter
    cosine = jnp.cos(angle)
    sine = jnp.sin(angle)
    signed = jnp.where(first[None, None, :], -sine, sine)
    return cosine, signed


def make_band_kernel(slots, reads, heads, head_dim, count_rows, width):
    pairs = width // 128
    quarter = head_dim // 4
    per_pair = 128 // head_dim
    stacked = per_pair * count_rows

    def kernel(stops_ref, base_ref, scale_ref, x_ref, *rest):
        payload_refs = rest[:slots]
        (cos_ref, sin_ref, wq_ref, wk_ref, wv_ref, wo_ref, tok_ref, out_ref, k_buf, v_buf,
         r_buf, c_buf, s_buf, q_ref) = rest[slots:]
        lane = lax.broadcasted_iota(jnp.int32, (count_rows, 128), 1)
        first = (lane % (2 * quarter)) < quarter
        proj = jnp.dot(x_ref[...], wq_ref[...], preferred_element_type=jnp.float32)
        own_cos = cos_ref[slots // 2]
        own_sin = sin_ref[slots // 2]
        for p in range(pairs):
            lo = p * 128
            x = proj[:, lo:lo + 128]
            other = jnp.where(first, pltpu.roll(x, 128 - quarter, 1), pltpu.roll(x, quarter, 1))
            q_ref[:, lo:lo + 128] = (x * own_cos + other * own_sin).astype(q_ref.dtype)
        head_of_lane = lane // head_dim
        row = lax.broadcasted_iota(jnp.int32, (stacked, 1), 0)

        place = jnp.int32(0)
        for slot in range(slots):
            block = base_ref[0] + (slot - slots // 2)
            hit = stops_ref[0] == block
            for r in range(1, reads):
                hit = hit | (stops_ref[r] == block)
            spot = place

            @pl.when(hit)
            def _():
                at = pl.ds(pl.multiple_of(spot * count_rows, count_rows), count_rows)
                r_buf[at, :] = payload_refs[slot][...]
                c_buf[at, :] = cos_ref[slot]
                s_buf[at, :] = sin_ref[slot]

            place = place + jnp.where(hit, jnp.int32(1), jnp.int32(0))

        rows = r_buf[...]
        kp = jnp.dot(rows, wk_ref[...], preferred_element_type=jnp.float32)
        vp = jnp.dot(rows, wv_ref[...], preferred_element_type=jnp.float32)
        v_buf[...] = jnp.where(jnp.abs(vp) < jnp.inf, vp, jnp.float32(0)).astype(jnp.bfloat16)
        cosine = c_buf[...]
        signed = s_buf[...]
        lane_k = lax.broadcasted_iota(jnp.int32, (reads * count_rows, 128), 1)
        first_k = (lane_k % (2 * quarter)) < quarter
        for p in range(pairs):
            lo = p * 128
            x = kp[:, lo:lo + 128]
            other = jnp.where(first_k, pltpu.roll(x, 128 - quarter, 1), pltpu.roll(x, quarter, 1))
            k_buf[:, lo:lo + 128] = (x * cosine + other * signed).astype(jnp.bfloat16)

        parts = []
        for p in range(pairs):
            lo = p * 128
            q_pair = q_ref[:, lo:lo + 128]
            q_two = jnp.concatenate(
                [jnp.where(head_of_lane == sub, q_pair, jnp.zeros_like(q_pair))
                 for sub in range(per_pair)], axis=0)
            scale_col = jnp.zeros((stacked, 1), jnp.float32)
            for sub in range(per_pair):
                scale_col = jnp.where(row // count_rows == sub, scale_ref[p * per_pair + sub] / jnp.float32(math.sqrt(head_dim)), scale_col)
            scores = lax.dot_general(
                q_two, k_buf[:, lo:lo + 128], (((1,), (1,)), ((), ())),
                preferred_element_type=jnp.float32,
            ) * scale_col
            scores = jnp.where(jnp.abs(scores) < jnp.inf, scores, jnp.float32(NEG))
            best = jnp.max(scores, axis=1, keepdims=True)
            weights = jnp.exp(scores - best)
            total = jnp.sum(weights, axis=1, keepdims=True)
            summed = jnp.dot(weights.astype(jnp.bfloat16), v_buf[:, lo:lo + 128],
                             preferred_element_type=jnp.float32)
            two = summed / total
            res = two[0:count_rows]
            for sub in range(1, per_pair):
                res = jnp.where(head_of_lane == sub, two[sub * count_rows:(sub + 1) * count_rows], res)
            parts.append(res.astype(jnp.bfloat16))
        attended = jnp.concatenate(parts, axis=1)
        mixed = tok_ref[...].astype(jnp.float32) + jnp.dot(
            attended, wo_ref[...], preferred_element_type=jnp.float32
        )
        out_ref[...] = mixed.astype(out_ref.dtype)

    return kernel


def make_query_kernel(head_dim):
    quarter = head_dim // 4

    def kernel(x_ref, w_ref, cos_ref, sin_ref, out_ref):
        proj = jnp.dot(x_ref[...], w_ref[...], preferred_element_type=jnp.float32)
        lane = lax.broadcasted_iota(jnp.int32, (proj.shape[0], 128), 1)
        first = (lane % (2 * quarter)) < quarter
        cosine = cos_ref[...]
        signed = sin_ref[...]
        for p in range(proj.shape[1] // 128):
            lo = p * 128
            x = proj[:, lo:lo + 128]
            other = jnp.where(first, pltpu.roll(x, 128 - quarter, 1), pltpu.roll(x, quarter, 1))
            out_ref[:, lo:lo + 128] = (x * cosine + other * signed).astype(out_ref.dtype)

    return kernel


def make_prep_kernel(tile_count, tile_rows, count_rows):
    def kernel(order_ref, count_ref, tok_ref, gain_ref, normed_ref, out_ref):
        floated = tok_ref[...].astype(jnp.float32)
        gain = gain_ref[...].reshape(1, floated.shape[1])
        normed_ref[...] = layer_norm(floated, gain).astype(normed_ref.dtype)
        row = lax.broadcasted_iota(jnp.int32, (tile_rows, 1), 0)
        for s in range(tile_count):
            src = order_ref[s]
            start = pl.multiple_of(src * tile_rows, tile_rows)
            rows = normed_ref[pl.ds(start, tile_rows), :]
            out_ref[s * tile_rows:(s + 1) * tile_rows, :] = jnp.where(
                row < count_ref[src], rows, jnp.asarray(jnp.inf, rows.dtype))

    return kernel


def across(shard, by):
    size = lax.axis_size("tok")
    epochs = lax.axis_size("ep")
    pairs = [
        ((i + by) * epochs + (epochs - 1 - e), i * epochs + e)
        for i in range(size)
        for e in range(epochs)
        if 0 <= i + by < size
    ]
    return lax.ppermute(shard, ("tok", "ep"), pairs)


def full_spec(shape):
    return pl.BlockSpec(shape, lambda i: (0,) * len(shape))


def on_device(
    tokens, norm_gain, query_weight, w_key, w_value, w_out, head_scale, matching, valid, stops
):
    count_rows, width = tokens.shape[1:]
    heads = head_scale.shape[0]
    head_dim = width // heads
    block_index = lax.axis_index("tok")
    smem = pl.BlockSpec(memory_space=pltpu.SMEM)
    vmem = pl.BlockSpec(memory_space=pltpu.VMEM)
    theirs = partner(matching[0], "ep", 0)
    tile_count = matching.shape[1]
    tile_rows = count_rows // tile_count
    normed, payload = pl.pallas_call(
        make_prep_kernel(tile_count, tile_rows, count_rows),
        out_shape=(
            jax.ShapeDtypeStruct((count_rows, width), jnp.bfloat16),
            jax.ShapeDtypeStruct((count_rows, width), jnp.bfloat16),
        ),
        in_specs=[smem, smem, vmem, vmem],
        out_specs=(vmem, vmem),
    )(theirs, valid[0], tokens[0], norm_gain)

    offsets = list(range(-BAND, BAND + 1))
    slots = len(offsets)
    received = [partner(payload, "ep", 0) if d == 0 else across(payload, d) for d in offsets]
    own_block = offsets.index(0)
    received[own_block], stops, head_scale, block_index = lax.optimization_barrier(
        (received[own_block], stops, head_scale, block_index))
    blocks = block_index + jnp.array(offsets, dtype=jnp.int32)
    cosine, signed = angle_tables(blocks, count_rows, head_dim)
    reads = stops.shape[-1]
    out = pl.pallas_call(
        make_band_kernel(slots, reads, heads, head_dim, count_rows, width),
        out_shape=jax.ShapeDtypeStruct((count_rows, width), jnp.bfloat16),
        in_specs=[smem, smem, smem] + [vmem] * (1 + slots + 7),
        out_specs=vmem,
        scratch_shapes=[
            pltpu.VMEM((reads * count_rows, width), jnp.bfloat16),
            pltpu.VMEM((reads * count_rows, width), jnp.bfloat16),
            pltpu.VMEM((reads * count_rows, width), jnp.bfloat16),
            pltpu.VMEM((reads * count_rows, 128), jnp.float32),
            pltpu.VMEM((reads * count_rows, 128), jnp.float32),
            pltpu.VMEM((count_rows, width), jnp.bfloat16),
        ],
    )(stops[0, 0], block_index.reshape(1), head_scale, normed, *received, cosine, signed, query_weight, w_key,
      w_value, w_out, tokens[0])
    return out[None]


def solution(mesh):
    in_specs = (
        P("ep", ("grp", "tok"), None),
        P(),
        P(),
        P(),
        P(),
        P(),
        P(),
        P("ep", ("grp", "tok")),
        P("ep", ("grp", "tok")),
        P("ep", ("grp", "tok"), None),
    )
    out_specs = P("ep", ("grp", "tok"), None)
    return jax.shard_map(
        on_device, mesh=mesh, in_specs=in_specs, out_specs=out_specs, check_vma=False
    )
```
